32 devices in a mesh: seg: 4 (over y, x), fibre: 8 (over z, core).
Axes of the slice: x: 2, y: 2, z: 4, core: 2. Of those that a mesh axis runs over, the one named last changes fastest.
Arguments:
- record: bfloat16 [4, 128, 27648], P('seg', 'fibre'), may hold values from -6 to 6
- offsets: int32 [4, 16], P('seg'), may hold values from 0 to 24576
- live_mask: int32 [128], P('fibre'), may hold values 0 or 1
Outputs:
- stacked: float32 [256, 128, 128], P('seg', 'fibre')
The draws below stay inside these ranges and needn't reach their ends.
All inputs are finite; a program needn't handle non-finite values. No bound on the sum of `live_mask` on one device may be relied on, other than what follows from the above.
Results may differ from the reference program's by a relative error of at most 0.0036.
Values may be sent and summed in bfloat16 or wider, within the bound.
No kernel may reach another device: no remote copies, remote signals or barrier semaphores. Data moves between devices by JAX's collectives and lax.ppermute only.
A program may use at most 64 MiB of HBM per device.

```python
import math
import jax
import jax.numpy as jnp
from jax import lax

NF = 64
NT = 3072
BIN0 = 32
BAND = 256
WIN = 16
SEGS = 4
CHANNELS = 128
REC = 27648


def set_ends(array, own_key, smallest, largest):
    longest = array.shape.index(max(array.shape))
    spots = []
    for shift in (0, 1):
        where = [jax.random.randint(jax.random.fold_in(own_key, axis), (), 0, length) for axis, length in enumerate(array.shape)]
        where[longest] = (where[longest] + shift) % array.shape[longest]
        spots.append(tuple(where))
    return array.at[spots[0]].set(smallest).at[spots[1]].set(largest)


def block_scale(key, extent, shards, least, top_value):
    level, own = 1.0, jax.random.fold_in(key, 6)
    for position, shards_of in shards:
        steps = jnp.exp(jax.random.uniform(jax.random.fold_in(own, position), (shards_of,), jnp.float32, least / len(shards), top_value / len(shards)))
        level = level * jnp.repeat(steps, extent[position] // shards_of).reshape([-1 if axis == position else 1 for axis in range(len(extent))])
    return level


def centred(key, shape, spread, limit, split=(), kind=jnp.bfloat16):
    array = spread * jax.random.normal(key, shape, jnp.float32)
    if split:
        array = array * block_scale(key, shape, split, -0.22, 0.18)
    return jnp.clip(array, -limit, limit).astype(kind)


def setup_inputs(seed: int = 0) -> dict:
    arg_keys = jax.random.split(jax.random.key(seed), 4)
    return {
        "record": centred(arg_keys[0], (SEGS, CHANNELS, REC), 1.0, 6.0, ((0, 4), (1, 8))),
        "offsets": set_ends(jax.random.randint(arg_keys[1], (SEGS, WIN), 0, REC - NT + 1), jax.random.fold_in(arg_keys[1], 1), 0, REC - NT).astype(jnp.int32),
        "live_mask": set_ends((jax.random.randint(arg_keys[2], (CHANNELS,), 0, 16) < 15).astype(jnp.int32), jax.random.fold_in(arg_keys[2], 1), 0, 1),
    }


def spectral_table():
    sample_idx = jnp.arange(NT, dtype=jnp.int32)
    bin_idx = BIN0 + jnp.arange(NF, dtype=jnp.int32)
    phase_int = sample_idx[:, None] * bin_idx[None, :] % NT
    angle_rad = 2.0 * math.pi / NT * phase_int.astype(jnp.float32)
    return jnp.concatenate([jnp.cos(angle_rad), -jnp.sin(angle_rad)], axis=1).astype(jnp.bfloat16)

def whiten(record_rows, starts, live_mask):
    windows = jax.vmap(lambda first_sample: lax.dynamic_slice_in_dim(record_rows, first_sample, NT, axis=1))(starts)
    spectra = jnp.dot(windows, spectral_table(), preferred_element_type=jnp.float32)
    real_part = spectra[..., :NF]
    imag_part = spectra[..., NF:]
    power_bins = real_part * real_part + imag_part * imag_part
    bin_index = jnp.arange(NF, dtype=jnp.int32)
    nearby = (jnp.abs(bin_index[:, None] - bin_index[None, :]) <= 4).astype(jnp.float32)
    smooth = jnp.dot(power_bins, nearby, precision=lax.Precision.HIGHEST) / lax.optimization_barrier(jnp.sum(nearby, axis=0))
    water_level = lax.optimization_barrier(jnp.mean(power_bins, axis=-1, keepdims=True))
    gain_of = live_mask.astype(jnp.float32)[None, :, None] / jnp.sqrt(smooth + 0.1 * water_level + 1e-06)
    return jnp.concatenate([real_part * gain_of, imag_part * gain_of], axis=-1).astype(jnp.bfloat16)

def reference(record, offsets, live_mask):
    whitened = lax.map(lambda packed: whiten(packed[0], packed[1], live_mask), (record, offsets))
    own_part = whitened.astype(jnp.float32)
    own_re = own_part[..., :NF]
    own_im = own_part[..., NF:]
    padded = jnp.concatenate([whitened, jnp.zeros((SEGS, WIN, BAND, 2 * NF), jnp.bfloat16)], axis=2)

    def offset_term(distance):
        other = lax.dynamic_slice_in_dim(padded, distance, CHANNELS, axis=2).astype(jnp.float32)
        far_re = other[..., :NF]
        far_im = other[..., NF:]
        real_sum = lax.optimization_barrier(jnp.sum(own_re * far_re + own_im * far_im, axis=(0, 1)))
        imag_sum = lax.optimization_barrier(jnp.sum(own_im * far_re - own_re * far_im, axis=(0, 1)))
        return jnp.concatenate([real_sum, imag_sum], axis=-1)
    stacked = lax.map(offset_term, jnp.arange(1, BAND + 1, dtype=jnp.int32))
    return stacked * (1.0 / math.sqrt(SEGS * WIN))
```

```python
import math

import jax
import jax.numpy as jnp
import ml_dtypes
import numpy as np
from jax import lax
from jax.sharding import PartitionSpec as P

NF = 64
NT = 3072
BIN0 = 32
BAND = 256
LANES = 128


def spectral_table():
    sample_idx = np.arange(NT, dtype=np.int64)
    bin_idx = BIN0 + np.arange(NF, dtype=np.int64)
    phase_int = sample_idx[:, None] * bin_idx[None, :] % NT
    angle_rad = np.float32(2.0 * math.pi / NT) * phase_int.astype(np.float32)
    angle = angle_rad.astype(np.float64)
    table = np.concatenate([np.cos(angle), -np.sin(angle)], axis=1)
    return table.astype(ml_dtypes.bfloat16)


def window_spectra(record_rows, starts):
    channels, length = record_rows.shape
    blocks = length // LANES
    per_window = NT // LANES
    by_block = record_rows.reshape(channels, blocks, LANES).transpose(1, 0, 2)
    by_block = jnp.concatenate([by_block, jnp.zeros((1, channels, LANES), by_block.dtype)], axis=0)
    first_block = starts // LANES
    shift = starts % LANES
    chunks = jax.vmap(lambda q: lax.dynamic_slice_in_dim(by_block, q, per_window + 1, axis=0))(first_block)
    pairs = jnp.concatenate([chunks[:, :per_window], chunks[:, 1:]], axis=-1)
    src = lax.broadcasted_iota(jnp.int32, (2 * LANES, LANES), 0)
    dst = lax.broadcasted_iota(jnp.int32, (2 * LANES, LANES), 1)
    pick = (src[None] == dst[None] + shift[:, None, None]).astype(jnp.bfloat16)
    windows = jnp.einsum(
        "wbcm,wmi->wcbi", pairs, pick, preferred_element_type=jnp.float32
    ).astype(jnp.bfloat16)
    table = jnp.asarray(spectral_table()).reshape(per_window, LANES, 2 * NF)
    return jnp.einsum("wcbi,bif->wcf", windows, table, preferred_element_type=jnp.float32)


def whiten(record_rows, starts, live_mask):
    spectra = window_spectra(record_rows, starts)
    real_part = spectra[..., :NF]
    imag_part = spectra[..., NF:]
    power_bins = real_part * real_part + imag_part * imag_part
    bin_index = jnp.arange(NF, dtype=jnp.int32)
    nearby = (jnp.abs(bin_index[:, None] - bin_index[None, :]) <= 4).astype(jnp.float32)
    smooth = jnp.dot(power_bins, nearby, precision=lax.Precision.HIGHEST) / jnp.sum(nearby, axis=0)
    water_level = jnp.mean(power_bins, axis=-1, keepdims=True)
    gain_of = live_mask.astype(jnp.float32)[None, :, None] / jnp.sqrt(
        smooth + 0.1 * water_level + 1e-06
    )
    return jnp.concatenate([real_part * gain_of, imag_part * gain_of], axis=-1).astype(jnp.bfloat16)


def shards(record, offsets, live_mask):
    seg_count = lax.axis_size("seg")
    fibre_count = lax.axis_size("fibre")
    own_block = whiten(record[0], offsets[0], live_mask)
    windows_count, block, _ = own_block.shape
    channels = block * fibre_count
    per_owner = BAND // seg_count
    bins_each = NF // seg_count
    live_offsets = min(BAND, channels - 1)
    live_owners = -(-live_offsets // per_owner)
    kept = live_owners * per_owner
    span = block + kept
    hops = min(-(-span // block) - 1, fibre_count - 1)
    me = lax.axis_index("seg")

    split = own_block.reshape(windows_count, block, 2, seg_count, bins_each).transpose(3, 0, 1, 2, 4)
    gathered = [lax.dynamic_index_in_dim(split, me, 0, keepdims=False)]
    for step in range(1, seg_count):
        sent = lax.dynamic_index_in_dim(split, (me + step) % seg_count, 0, keepdims=False)
        pairs = [(i, (i + step) % seg_count) for i in range(seg_count)]
        gathered.append(lax.ppermute(sent, "seg", pairs))
    mine = jnp.stack(gathered)

    columns = [mine]
    for step in range(1, hops + 1):
        pairs = [(i, i - step) for i in range(step, fibre_count)]
        columns.append(lax.ppermute(mine, "fibre", pairs))
    columns = jnp.concatenate(columns, axis=2)
    if columns.shape[2] < span:
        pad = jnp.zeros(columns.shape[:2] + (span - columns.shape[2],) + columns.shape[3:], columns.dtype)
        columns = jnp.concatenate([columns, pad], axis=2)
    columns = columns.reshape((seg_count * windows_count,) + columns.shape[2:])
    re_all = columns[:, :, 0]
    im_all = columns[:, :, 1]
    re_own = re_all[:, :block]
    im_own = im_all[:, :block]
    right = jnp.stack([re_all, im_all])
    left = jnp.stack([jnp.stack([re_own, im_own]), jnp.stack([im_own, -re_own])])
    cross = jnp.einsum("opscn,psjn->nocj", left, right, preferred_element_type=jnp.float32)
    band = jnp.stack([cross[:, :, c, c + 1 : c + 1 + kept] for c in range(block)])
    band = band.transpose(3, 0, 2, 1) * (1.0 / math.sqrt(seg_count * windows_count))
    if kept < BAND:
        band = jnp.concatenate([band, jnp.zeros((BAND - kept,) + band.shape[1:], band.dtype)], axis=0)
    band = band.reshape((seg_count, per_owner) + band.shape[1:])

    collected = [lax.dynamic_index_in_dim(band, me, 0, keepdims=False)]
    for step in range(1, seg_count):
        sent = lax.dynamic_index_in_dim(band, (me + step) % seg_count, 0, keepdims=False)
        pairs = [(i, (i + step) % seg_count) for i in range(seg_count) if (i + step) % seg_count < live_owners]
        if pairs:
            collected.append(lax.ppermute(sent, "seg", pairs))
        else:
            collected.append(jnp.zeros_like(sent))
    collected = jnp.stack(collected)
    holder = (me - jnp.arange(seg_count, dtype=jnp.int32)) % seg_count
    by_bins = jnp.take(collected, holder, axis=0)
    return by_bins.transpose(1, 2, 3, 0, 4).reshape(per_owner, block, 2 * NF)


def solution(mesh):
    placed = (P("seg", "fibre", None), P("seg", None), P("fibre"))
    return jax.shard_map(
        shards, mesh=mesh, in_specs=placed, out_specs=P("seg", "fibre", None), check_vma=False
    )
```

```python
import math

import jax
import jax.numpy as jnp
import ml_dtypes
import numpy as np
from jax import lax
from jax.sharding import PartitionSpec as P

NF = 64
NT = 3072
BIN0 = 32
BAND = 256
LANES = 128


def spectral_table():
    sample_idx = np.arange(NT, dtype=np.int64)
    bin_idx = BIN0 + np.arange(NF, dtype=np.int64)
    phase_int = sample_idx[:, None] * bin_idx[None, :] % NT
    angle_rad = np.float32(2.0 * math.pi / NT) * phase_int.astype(np.float32)
    angle = angle_rad.astype(np.float64)
    table = np.concatenate([np.cos(angle), -np.sin(angle)], axis=1)
    return table.astype(ml_dtypes.bfloat16)


def window_spectra(record_rows, starts):
    channels, length = record_rows.shape
    blocks = length // LANES
    per_window = NT // LANES
    by_block = record_rows.reshape(channels, blocks, LANES).transpose(1, 0, 2)
    by_block = jnp.concatenate([by_block, jnp.zeros((1, channels, LANES), by_block.dtype)], axis=0)
    first_block = starts // LANES
    shift = starts % LANES
    chunks = jax.vmap(lambda q: lax.dynamic_slice_in_dim(by_block, q, per_window + 1, axis=0))(first_block)
    pairs = jnp.concatenate([chunks[:, :per_window], chunks[:, 1:]], axis=-1)
    src = lax.broadcasted_iota(jnp.int32, (2 * LANES, LANES), 0)
    dst = lax.broadcasted_iota(jnp.int32, (2 * LANES, LANES), 1)
    pick = (src[None] == dst[None] + shift[:, None, None]).astype(jnp.bfloat16)
    windows = jnp.einsum(
        "wbcm,wmi->wcbi", pairs, pick, preferred_element_type=jnp.float32
    ).astype(jnp.bfloat16)
    table = jnp.asarray(spectral_table()).reshape(per_window, LANES, 2 * NF)
    return jnp.einsum("wcbi,bif->wcf", windows, table, preferred_element_type=jnp.float32)


def whiten(record_rows, starts, live_mask):
    spectra = window_spectra(record_rows, starts)
    real_part = spectra[..., :NF]
    imag_part = spectra[..., NF:]
    power_bins = real_part * real_part + imag_part * imag_part
    bin_index = jnp.arange(NF, dtype=jnp.int32)
    nearby = (jnp.abs(bin_index[:, None] - bin_index[None, :]) <= 4).astype(jnp.float32)
    smooth = jnp.dot(power_bins, nearby, precision=lax.Precision.HIGHEST) / jnp.sum(nearby, axis=0)
    water_level = jnp.mean(power_bins, axis=-1, keepdims=True)
    gain_of = live_mask.astype(jnp.float32)[None, :, None] / jnp.sqrt(
        smooth + 0.1 * water_level + 1e-06
    )
    return jnp.concatenate([real_part * gain_of, imag_part * gain_of], axis=-1).astype(jnp.bfloat16)


def shards(record, offsets, live_mask):
    seg_count = lax.axis_size("seg")
    fibre_count = lax.axis_size("fibre")
    own_block = whiten(record[0], offsets[0], live_mask)
    windows_count, block, _ = own_block.shape
    channels = block * fibre_count
    per_owner = BAND // seg_count
    bins_each = NF // seg_count
    live_offsets = min(BAND, channels - 1)
    live_owners = -(-live_offsets // per_owner)
    kept = live_owners * per_owner
    span = block + kept
    hops = min(-(-span // block) - 1, fibre_count - 1)
    me = lax.axis_index("seg")
    rows = seg_count * windows_count

    split = own_block.reshape(windows_count, block, 2, seg_count, bins_each).transpose(3, 1, 0, 2, 4)
    split = split.reshape(seg_count, block, windows_count * 2 * bins_each)
    gathered = [lax.dynamic_index_in_dim(split, me, 0, keepdims=False)]
    for step in range(1, seg_count):
        sent = lax.dynamic_index_in_dim(split, (me + step) % seg_count, 0, keepdims=False)
        pairs = [(i, (i + step) % seg_count) for i in range(seg_count)]
        gathered.append(lax.ppermute(sent, "seg", pairs))
    mine = jnp.concatenate(gathered, axis=1)

    columns = [mine]
    for step in range(1, hops + 1):
        pairs = [(i, i - step) for i in range(step, fibre_count)]
        columns.append(lax.ppermute(mine, "fibre", pairs))
    columns = jnp.concatenate(columns, axis=0)
    if columns.shape[0] < span:
        columns = jnp.concatenate(
            [columns, jnp.zeros((span - columns.shape[0], columns.shape[1]), columns.dtype)], axis=0
        )
    right = columns.reshape(span, rows, 2, bins_each)
    re_own = right[:block, :, 0]
    im_own = right[:block, :, 1]
    left = jnp.stack([jnp.stack([re_own, im_own], axis=2), jnp.stack([im_own, -re_own], axis=2)])
    cross = jnp.einsum("ocspn,jspn->nocj", left, right, preferred_element_type=jnp.float32)
    band = jnp.stack([cross[:, :, c, c + 1 : c + 1 + kept] for c in range(block)])
    band = band.transpose(3, 0, 2, 1) * (1.0 / math.sqrt(seg_count * windows_count))
    band = band.reshape(kept, block * 2 * bins_each)
    if kept < BAND:
        band = jnp.concatenate([band, jnp.zeros((BAND - kept, band.shape[1]), band.dtype)], axis=0)
    band = band.reshape(seg_count, per_owner, band.shape[1])

    collected = [lax.dynamic_index_in_dim(band, me, 0, keepdims=False)]
    for step in range(1, seg_count):
        sent = lax.dynamic_index_in_dim(band, (me + step) % seg_count, 0, keepdims=False)
        pairs = [(i, (i + step) % seg_count) for i in range(seg_count) if (i + step) % seg_count < live_owners]
        if pairs:
            collected.append(lax.ppermute(sent, "seg", pairs))
        else:
            collected.append(jnp.zeros_like(sent))
    collected = jnp.stack(collected)
    holder = (me - jnp.arange(seg_count, dtype=jnp.int32)) % seg_count
    by_bins = jnp.take(collected, holder, axis=0).reshape(seg_count, per_owner, block, 2, bins_each)
    return by_bins.transpose(1, 2, 3, 0, 4).reshape(per_owner, block, 2 * NF)


def solution(mesh):
    placed = (P("seg", "fibre", None), P("seg", None), P("fibre"))
    return jax.shard_map(
        shards, mesh=mesh, in_specs=placed, out_specs=P("seg", "fibre", None), check_vma=False
    )
```

```python
import math

import jax
import jax.numpy as jnp
import ml_dtypes
import numpy as np
from jax import lax
from jax.sharding import PartitionSpec as P

NF = 64
NT = 3072
BIN0 = 32
BAND = 256
LANES = 128


def spectral_table():
    sample_idx = np.arange(NT, dtype=np.int64)
    bin_idx = BIN0 + np.arange(NF, dtype=np.int64)
    phase_int = sample_idx[:, None] * bin_idx[None, :] % NT
    angle_rad = np.float32(2.0 * math.pi / NT) * phase_int.astype(np.float32)
    angle = angle_rad.astype(np.float64)
    table = np.concatenate([np.cos(angle), -np.sin(angle)], axis=1)
    return table.astype(ml_dtypes.bfloat16)


def window_spectra(record_rows, starts):
    channels, length = record_rows.shape
    blocks = length // LANES
    per_window = NT // LANES
    by_block = record_rows.reshape(channels, blocks, LANES).transpose(1, 0, 2)
    by_block = jnp.concatenate([by_block, jnp.zeros((1, channels, LANES), by_block.dtype)], axis=0)
    first_block = starts // LANES
    shift = starts % LANES
    chunks = jax.vmap(lambda q: lax.dynamic_slice_in_dim(by_block, q, per_window + 1, axis=0))(first_block)
    pairs = jnp.concatenate([chunks[:, :per_window], chunks[:, 1:]], axis=-1)
    src = lax.broadcasted_iota(jnp.int32, (2 * LANES, LANES), 0)
    dst = lax.broadcasted_iota(jnp.int32, (2 * LANES, LANES), 1)
    pick = (src[None] == dst[None] + shift[:, None, None]).astype(jnp.bfloat16)
    windows = jnp.einsum(
        "wbcm,wmi->wcbi", pairs, pick, preferred_element_type=jnp.float32
    ).astype(jnp.bfloat16)
    table = jnp.asarray(spectral_table()).reshape(per_window, LANES, 2 * NF)
    return jnp.einsum("wcbi,bif->wcf", windows, table, preferred_element_type=jnp.float32)


def whiten(record_rows, starts, live_mask):
    spectra = window_spectra(record_rows, starts)
    real_part = spectra[..., :NF]
    imag_part = spectra[..., NF:]
    power_bins = real_part * real_part + imag_part * imag_part
    bin_index = jnp.arange(NF, dtype=jnp.int32)
    nearby = (jnp.abs(bin_index[:, None] - bin_index[None, :]) <= 4).astype(jnp.float32)
    smooth = jnp.dot(power_bins, nearby, precision=lax.Precision.HIGHEST) / jnp.sum(nearby, axis=0)
    water_level = jnp.mean(power_bins, axis=-1, keepdims=True)
    gain_of = live_mask.astype(jnp.float32)[None, :, None] / jnp.sqrt(
        smooth + 0.1 * water_level + 1e-06
    )
    return jnp.concatenate([real_part * gain_of, imag_part * gain_of], axis=-1).astype(jnp.bfloat16)


def halo(mine, hops, fibre_count):
    if fibre_count % 2:
        columns = [mine]
        for step in range(1, hops + 1):
            pairs = [(i, i - step) for i in range(step, fibre_count)]
            columns.append(lax.ppermute(mine, "fibre", pairs))
        return jnp.concatenate(columns, axis=0)
    strides = min(-(-hops // 2), (fibre_count - 1) // 2)
    own = [mine]
    for step in range(1, strides + 1):
        pairs = [(i, i - 2 * step) for i in range(2 * step, fibre_count)]
        own.append(lax.ppermute(mine, "fibre", pairs))
    swapped = lax.ppermute(jnp.concatenate(own, axis=0), "fibre", [(i, i ^ 1) for i in range(fibre_count)])
    swapped = jnp.split(swapped, strides + 1, axis=0)
    even = [part for pair in zip(own, swapped) for part in pair]
    odd = [part for pair in zip(own, swapped[1:] + [jnp.zeros_like(mine)]) for part in pair]
    odd_side = lax.axis_index("fibre") % 2 == 1
    return jnp.where(odd_side, jnp.concatenate(odd, axis=0), jnp.concatenate(even, axis=0))


def shards(record, offsets, live_mask):
    seg_count = lax.axis_size("seg")
    fibre_count = lax.axis_size("fibre")
    own_block = whiten(record[0], offsets[0], live_mask)
    windows_count, block, _ = own_block.shape
    channels = block * fibre_count
    per_owner = BAND // seg_count
    bins_each = NF // seg_count
    live_offsets = min(BAND, channels - 1)
    live_owners = -(-live_offsets // per_owner)
    kept = live_owners * per_owner
    span = block + kept
    hops = min(-(-span // block) - 1, fibre_count - 1)
    me = lax.axis_index("seg")
    rows = seg_count * windows_count

    split = own_block.reshape(windows_count, block, 2, seg_count, bins_each).transpose(3, 1, 0, 2, 4)
    split = split.reshape(seg_count, block, windows_count * 2 * bins_each)
    gathered = [lax.dynamic_index_in_dim(split, me, 0, keepdims=False)]
    for step in range(1, seg_count):
        sent = lax.dynamic_index_in_dim(split, (me + step) % seg_count, 0, keepdims=False)
        pairs = [(i, (i + step) % seg_count) for i in range(seg_count)]
        gathered.append(lax.ppermute(sent, "seg", pairs))
    mine = jnp.concatenate(gathered, axis=1)

    columns = halo(mine, hops, fibre_count)[:span]
    if columns.shape[0] < span:
        columns = jnp.concatenate(
            [columns, jnp.zeros((span - columns.shape[0], columns.shape[1]), columns.dtype)], axis=0
        )
    right = columns.reshape(span, rows, 2, bins_each)
    re_own = right[:block, :, 0]
    im_own = right[:block, :, 1]
    left = jnp.stack([jnp.stack([re_own, im_own], axis=2), jnp.stack([im_own, -re_own], axis=2)])
    cross = jnp.einsum("ocspn,jspn->nocj", left, right, preferred_element_type=jnp.float32)
    band = jnp.stack([cross[:, :, c, c + 1 : c + 1 + kept] for c in range(block)])
    band = band.transpose(3, 0, 2, 1) * (1.0 / math.sqrt(seg_count * windows_count))
    band = band.reshape(kept, block * 2 * bins_each)
    if kept < BAND:
        band = jnp.concatenate([band, jnp.zeros((BAND - kept, band.shape[1]), band.dtype)], axis=0)
    band = band.reshape(seg_count, per_owner, band.shape[1])

    collected = [lax.dynamic_index_in_dim(band, me, 0, keepdims=False)]
    for step in range(1, seg_count):
        sent = lax.dynamic_index_in_dim(band, (me + step) % seg_count, 0, keepdims=False)
        pairs = [(i, (i + step) % seg_count) for i in range(seg_count) if (i + step) % seg_count < live_owners]
        if pairs:
            collected.append(lax.ppermute(sent, "seg", pairs))
        else:
            collected.append(jnp.zeros_like(sent))
    collected = jnp.stack(collected)
    holder = (me - jnp.arange(seg_count, dtype=jnp.int32)) % seg_count
    by_bins = jnp.take(collected, holder, axis=0).reshape(seg_count, per_owner, block, 2, bins_each)
    return by_bins.transpose(1, 2, 3, 0, 4).reshape(per_owner, block, 2 * NF)


def solution(mesh):
    placed = (P("seg", "fibre", None), P("seg", None), P("fibre"))
    return jax.shard_map(
        shards, mesh=mesh, in_specs=placed, out_specs=P("seg", "fibre", None), check_vma=False
    )
```

```python
import math

import jax
import jax.numpy as jnp
import ml_dtypes
import numpy as np
from jax import lax
from jax.experimental import pallas as pl
from jax.experimental.pallas import tpu as pltpu
from jax.sharding import PartitionSpec as P

NF = 64
NT = 3072
BIN0 = 32
BAND = 256
LANES = 128


def spectral_table():
    sample_idx = np.arange(NT, dtype=np.int64)
    bin_idx = BIN0 + np.arange(NF, dtype=np.int64)
    phase_int = sample_idx[:, None] * bin_idx[None, :] % NT
    angle_rad = np.float32(2.0 * math.pi / NT) * phase_int.astype(np.float32)
    angle = angle_rad.astype(np.float64)
    table = np.concatenate([np.cos(angle), -np.sin(angle)], axis=1)
    return table.astype(ml_dtypes.bfloat16)


def whiten_kernel(starts_ref, record_hbm, table_ref, near_ref, count_ref, live_ref, out_ref, chunks, moved_rows, sems):
    windows, channels, span = chunks.shape
    blocks = NT // LANES
    last = record_hbm.shape[1] - span
    shifts = []
    for w in range(windows):
        first = starts_ref[w]
        base = pl.multiple_of(jnp.minimum(first - first % LANES, last), LANES)
        pltpu.make_async_copy(record_hbm.at[:, pl.ds(base, span)], chunks.at[w], sems.at[w]).start()
        shifts.append(first - base)
    src = lax.broadcasted_iota(jnp.int32, (2 * LANES, LANES), 0)
    dst = lax.broadcasted_iota(jnp.int32, (2 * LANES, LANES), 1)
    for w in range(windows):
        pltpu.make_async_copy(record_hbm.at[:, pl.ds(0, span)], chunks.at[w], sems.at[w]).wait()
        pick = (src == dst + shifts[w]).astype(jnp.bfloat16)
        pairs = jnp.concatenate([chunks[w, :, pl.ds(b * LANES, 2 * LANES)] for b in range(blocks)], axis=0)
        moved = jnp.dot(pairs, pick, preferred_element_type=jnp.float32).astype(jnp.bfloat16)
        for b in range(blocks):
            moved_rows[b, pl.ds(w * channels, channels), :] = moved[b * channels : (b + 1) * channels]
    spectra = jnp.zeros(out_ref.shape, jnp.float32)
    for b in range(blocks):
        spectra = spectra + jnp.dot(moved_rows[b], table_ref[b], preferred_element_type=jnp.float32)
    power = spectra * spectra
    smooth = jnp.dot(
        power, near_ref[...], precision=lax.Precision.HIGHEST, preferred_element_type=jnp.float32
    ) / count_ref[...]
    water_level = jnp.sum(power, axis=-1, keepdims=True) / NF
    gain_of = live_ref[...] / jnp.sqrt(smooth + 0.1 * water_level + 1e-06)
    out_ref[...] = (spectra * gain_of).astype(out_ref.dtype)


def whiten(record_rows, starts, live_mask):
    channels, _ = record_rows.shape
    windows = starts.shape[0]
    blocks = NT // LANES
    table = jnp.asarray(spectral_table()).reshape(blocks, LANES, 2 * NF)
    lane_bin = np.arange(2 * NF) % NF
    near = (np.abs(lane_bin[:, None] - lane_bin[None, :]) <= 4).astype(np.float32)
    count = near[:NF].sum(axis=0, keepdims=True)
    live_rows = jnp.tile(live_mask.astype(jnp.float32), windows)[:, None]
    vmem = pl.BlockSpec(memory_space=pltpu.VMEM)
    out = pl.pallas_call(
        whiten_kernel,
        out_shape=jax.ShapeDtypeStruct((windows * channels, 2 * NF), jnp.bfloat16),
        in_specs=[pl.BlockSpec(memory_space=pltpu.SMEM), pl.BlockSpec(memory_space=pl.ANY), vmem, vmem, vmem, vmem],
        out_specs=vmem,
        scratch_shapes=[
            pltpu.VMEM((windows, channels, NT + LANES), jnp.bfloat16),
            pltpu.VMEM((blocks, windows * channels, LANES), jnp.bfloat16),
            pltpu.SemaphoreType.DMA((windows,)),
        ],
    )(starts, record_rows, table, jnp.asarray(near), jnp.asarray(count), live_rows)
    return out.reshape(windows, channels, 2 * NF)


def halo(mine, hops, fibre_count):
    if fibre_count % 2:
        columns = [mine]
        for step in range(1, hops + 1):
            pairs = [(i, i - step) for i in range(step, fibre_count)]
            columns.append(lax.ppermute(mine, "fibre", pairs))
        return jnp.concatenate(columns, axis=0)
    strides = min(-(-hops // 2), (fibre_count - 1) // 2)
    own = [mine]
    for step in range(1, strides + 1):
        pairs = [(i, i - 2 * step) for i in range(2 * step, fibre_count)]
        own.append(lax.ppermute(mine, "fibre", pairs))
    swapped = lax.ppermute(jnp.concatenate(own, axis=0), "fibre", [(i, i ^ 1) for i in range(fibre_count)])
    swapped = jnp.split(swapped, strides + 1, axis=0)
    even = [part for pair in zip(own, swapped) for part in pair]
    odd = [part for pair in zip(own, swapped[1:] + [jnp.zeros_like(mine)]) for part in pair]
    odd_side = lax.axis_index("fibre") % 2 == 1
    return jnp.where(odd_side, jnp.concatenate(odd, axis=0), jnp.concatenate(even, axis=0))


def shards(record, offsets, live_mask):
    seg_count = lax.axis_size("seg")
    fibre_count = lax.axis_size("fibre")
    own_block = whiten(record[0], offsets[0], live_mask)
    windows_count, block, _ = own_block.shape
    channels = block * fibre_count
    per_owner = BAND // seg_count
    bins_each = NF // seg_count
    live_offsets = min(BAND, channels - 1)
    live_owners = -(-live_offsets // per_owner)
    kept = live_owners * per_owner
    span = block + kept
    hops = min(-(-span // block) - 1, fibre_count - 1)
    me = lax.axis_index("seg")
    rows = seg_count * windows_count

    split = own_block.reshape(windows_count, block, 2, seg_count, bins_each).transpose(3, 1, 0, 2, 4)
    split = split.reshape(seg_count, block, windows_count * 2 * bins_each)
    gathered = [lax.dynamic_index_in_dim(split, me, 0, keepdims=False)]
    for step in range(1, seg_count):
        sent = lax.dynamic_index_in_dim(split, (me + step) % seg_count, 0, keepdims=False)
        pairs = [(i, (i + step) % seg_count) for i in range(seg_count)]
        gathered.append(lax.ppermute(sent, "seg", pairs))
    mine = jnp.concatenate(gathered, axis=1)

    columns = halo(mine, hops, fibre_count)[:span]
    if columns.shape[0] < span:
        columns = jnp.concatenate(
            [columns, jnp.zeros((span - columns.shape[0], columns.shape[1]), columns.dtype)], axis=0
        )
    right = columns.reshape(span, rows, 2, bins_each)
    re_own = right[:block, :, 0]
    im_own = right[:block, :, 1]
    left = jnp.stack([jnp.stack([re_own, im_own], axis=2), jnp.stack([im_own, -re_own], axis=2)])
    cross = jnp.einsum("ocspn,jspn->nocj", left, right, preferred_element_type=jnp.float32)
    band = jnp.stack([cross[:, :, c, c + 1 : c + 1 + kept] for c in range(block)])
    band = band.transpose(3, 0, 2, 1) * (1.0 / math.sqrt(seg_count * windows_count))
    band = band.reshape(kept, block * 2 * bins_each)
    if kept < BAND:
        band = jnp.concatenate([band, jnp.zeros((BAND - kept, band.shape[1]), band.dtype)], axis=0)
    band = band.reshape(seg_count, per_owner, band.shape[1])

    collected = [lax.dynamic_index_in_dim(band, me, 0, keepdims=False)]
    for step in range(1, seg_count):
        sent = lax.dynamic_index_in_dim(band, (me + step) % seg_count, 0, keepdims=False)
        pairs = [(i, (i + step) % seg_count) for i in range(seg_count) if (i + step) % seg_count < live_owners]
        if pairs:
            collected.append(lax.ppermute(sent, "seg", pairs))
        else:
            collected.append(jnp.zeros_like(sent))
    collected = jnp.stack(collected)
    holder = (me - jnp.arange(seg_count, dtype=jnp.int32)) % seg_count
    by_bins = jnp.take(collected, holder, axis=0).reshape(seg_count, per_owner, block, 2, bins_each)
    return by_bins.transpose(1, 2, 3, 0, 4).reshape(per_owner, block, 2 * NF)


def solution(mesh):
    placed = (P("seg", "fibre", None), P("seg", None), P("fibre"))
    return jax.shard_map(
        shards, mesh=mesh, in_specs=placed, out_specs=P("seg", "fibre", None), check_vma=False
    )
```

```python
import math

import jax
import jax.numpy as jnp
import ml_dtypes
import numpy as np
from jax import lax
from jax.experimental import pallas as pl
from jax.experimental.pallas import tpu as pltpu
from jax.sharding import PartitionSpec as P

NF = 64
NT = 3072
BIN0 = 32
BAND = 256
LANES = 128


def spectral_table():
    sample_idx = np.arange(NT, dtype=np.int64)
    bin_idx = BIN0 + np.arange(NF, dtype=np.int64)
    phase_int = sample_idx[:, None] * bin_idx[None, :] % NT
    angle_rad = np.float32(2.0 * math.pi / NT) * phase_int.astype(np.float32)
    angle = angle_rad.astype(np.float64)
    table = np.concatenate([np.cos(angle), -np.sin(angle)], axis=1)
    return table.astype(ml_dtypes.bfloat16)


def whiten_kernel(starts_ref, record_hbm, table_ref, near_ref, count_ref, live_ref, out_ref, chunks, moved_rows, sems):
    windows, channels, span = chunks.shape
    blocks = NT // LANES
    last = record_hbm.shape[1] - span
    shifts = []
    for w in range(windows):
        first = starts_ref[w]
        base = pl.multiple_of(jnp.minimum(first - first % LANES, last), LANES)
        pltpu.make_async_copy(record_hbm.at[:, pl.ds(base, span)], chunks.at[w], sems.at[w]).start()
        shifts.append(first - base)
    lane = lax.broadcasted_iota(jnp.int32, (channels, LANES), 1)
    for w in range(windows):
        pltpu.make_async_copy(record_hbm.at[:, pl.ds(0, span)], chunks.at[w], sems.at[w]).wait()
        shift = shifts[w]
        low = lane < LANES - shift
        rolled = [
            pltpu.roll(chunks[w, :, pl.ds(b * LANES, LANES)].astype(jnp.float32), (LANES - shift) % LANES, 1)
            for b in range(blocks + 1)
        ]
        for b in range(blocks):
            moved_rows[pl.ds(w * channels, channels), pl.ds(b * LANES, LANES)] = jnp.where(
                low, rolled[b], rolled[b + 1]
            ).astype(jnp.bfloat16)
    spectra = jnp.dot(moved_rows[...], table_ref[...], preferred_element_type=jnp.float32)
    power = spectra * spectra
    smooth = jnp.dot(
        power, near_ref[...], precision=lax.Precision.HIGHEST, preferred_element_type=jnp.float32
    ) / count_ref[...]
    water_level = jnp.sum(power, axis=-1, keepdims=True) / NF
    gain_of = live_ref[...] / jnp.sqrt(smooth + 0.1 * water_level + 1e-06)
    out_ref[...] = (spectra * gain_of).astype(out_ref.dtype)


def whiten(record_rows, starts, live_mask):
    channels, _ = record_rows.shape
    windows = starts.shape[0]
    blocks = NT // LANES
    table = jnp.asarray(spectral_table())
    lane_bin = np.arange(2 * NF) % NF
    near = (np.abs(lane_bin[:, None] - lane_bin[None, :]) <= 4).astype(np.float32)
    count = near[:NF].sum(axis=0, keepdims=True)
    live_rows = jnp.tile(live_mask.astype(jnp.float32), windows)[:, None]
    vmem = pl.BlockSpec(memory_space=pltpu.VMEM)
    out = pl.pallas_call(
        whiten_kernel,
        out_shape=jax.ShapeDtypeStruct((windows * channels, 2 * NF), jnp.bfloat16),
        in_specs=[pl.BlockSpec(memory_space=pltpu.SMEM), pl.BlockSpec(memory_space=pl.ANY), vmem, vmem, vmem, vmem],
        out_specs=vmem,
        scratch_shapes=[
            pltpu.VMEM((windows, channels, NT + LANES), jnp.bfloat16),
            pltpu.VMEM((windows * channels, NT), jnp.bfloat16),
            pltpu.SemaphoreType.DMA((windows,)),
        ],
    )(starts, record_rows, table, jnp.asarray(near), jnp.asarray(count), live_rows)
    return out.reshape(windows, channels, 2 * NF)


def halo(mine, hops, fibre_count):
    if fibre_count % 2:
        columns = [mine]
        for step in range(1, hops + 1):
            pairs = [(i, i - step) for i in range(step, fibre_count)]
            columns.append(lax.ppermute(mine, "fibre", pairs))
        return jnp.concatenate(columns, axis=0)
    strides = min(-(-hops // 2), (fibre_count - 1) // 2)
    own = [mine]
    for step in range(1, strides + 1):
        pairs = [(i, i - 2 * step) for i in range(2 * step, fibre_count)]
        own.append(lax.ppermute(mine, "fibre", pairs))
    swapped = lax.ppermute(jnp.concatenate(own, axis=0), "fibre", [(i, i ^ 1) for i in range(fibre_count)])
    swapped = jnp.split(swapped, strides + 1, axis=0)
    even = [part for pair in zip(own, swapped) for part in pair]
    odd = [part for pair in zip(own, swapped[1:] + [jnp.zeros_like(mine)]) for part in pair]
    odd_side = lax.axis_index("fibre") % 2 == 1
    return jnp.where(odd_side, jnp.concatenate(odd, axis=0), jnp.concatenate(even, axis=0))


def shards(record, offsets, live_mask):
    seg_count = lax.axis_size("seg")
    fibre_count = lax.axis_size("fibre")
    own_block = whiten(record[0], offsets[0], live_mask)
    windows_count, block, _ = own_block.shape
    channels = block * fibre_count
    per_owner = BAND // seg_count
    bins_each = NF // seg_count
    live_offsets = min(BAND, channels - 1)
    live_owners = -(-live_offsets // per_owner)
    kept = live_owners * per_owner
    span = block + kept
    hops = min(-(-span // block) - 1, fibre_count - 1)
    me = lax.axis_index("seg")
    rows = seg_count * windows_count

    split = own_block.reshape(windows_count, block, 2, seg_count, bins_each).transpose(3, 1, 0, 2, 4)
    split = split.reshape(seg_count, block, windows_count * 2 * bins_each)
    gathered = [lax.dynamic_index_in_dim(split, me, 0, keepdims=False)]
    for step in range(1, seg_count):
        sent = lax.dynamic_index_in_dim(split, (me + step) % seg_count, 0, keepdims=False)
        pairs = [(i, (i + step) % seg_count) for i in range(seg_count)]
        gathered.append(lax.ppermute(sent, "seg", pairs))
    mine = jnp.concatenate(gathered, axis=1)

    columns = halo(mine, hops, fibre_count)[:span]
    if columns.shape[0] < span:
        columns = jnp.concatenate(
            [columns, jnp.zeros((span - columns.shape[0], columns.shape[1]), columns.dtype)], axis=0
        )
    right = columns.reshape(span, rows, 2, bins_each)
    re_own = right[:block, :, 0]
    im_own = right[:block, :, 1]
    left = jnp.stack([jnp.stack([re_own, im_own], axis=2), jnp.stack([im_own, -re_own], axis=2)])
    cross = jnp.einsum("ocspn,jspn->nocj", left, right, preferred_element_type=jnp.float32)
    band = jnp.stack([cross[:, :, c, c + 1 : c + 1 + kept] for c in range(block)])
    band = band.transpose(3, 0, 2, 1) * (1.0 / math.sqrt(seg_count * windows_count))
    band = band.reshape(kept, block * 2 * bins_each)
    if kept < BAND:
        band = jnp.concatenate([band, jnp.zeros((BAND - kept, band.shape[1]), band.dtype)], axis=0)
    band = band.reshape(seg_count, per_owner, band.shape[1])

    collected = [lax.dynamic_index_in_dim(band, me, 0, keepdims=False)]
    for step in range(1, seg_count):
        sent = lax.dynamic_index_in_dim(band, (me + step) % seg_count, 0, keepdims=False)
        pairs = [(i, (i + step) % seg_count) for i in range(seg_count) if (i + step) % seg_count < live_owners]
        if pairs:
            collected.append(lax.ppermute(sent, "seg", pairs))
        else:
            collected.append(jnp.zeros_like(sent))
    collected = jnp.stack(collected)
    holder = (me - jnp.arange(seg_count, dtype=jnp.int32)) % seg_count
    by_bins = jnp.take(collected, holder, axis=0).reshape(seg_count, per_owner, block, 2, bins_each)
    return by_bins.transpose(1, 2, 3, 0, 4).reshape(per_owner, block, 2 * NF)


def solution(mesh):
    placed = (P("seg", "fibre", None), P("seg", None), P("fibre"))
    return jax.shard_map(
        shards, mesh=mesh, in_specs=placed, out_specs=P("seg", "fibre", None), check_vma=False
    )
```

```python
import math

import jax
import jax.numpy as jnp
import ml_dtypes
import numpy as np
from jax import lax
from jax.experimental import pallas as pl
from jax.experimental.pallas import tpu as pltpu
from jax.sharding import PartitionSpec as P

NF = 64
NT = 3072
BIN0 = 32
BAND = 256
LANES = 128


def spectral_table():
    sample_idx = np.arange(NT, dtype=np.int64)
    bin_idx = BIN0 + np.arange(NF, dtype=np.int64)
    phase_int = sample_idx[:, None] * bin_idx[None, :] % NT
    angle_rad = np.float32(2.0 * math.pi / NT) * phase_int.astype(np.float32)
    angle = angle_rad.astype(np.float64)
    table = np.concatenate([np.cos(angle), -np.sin(angle)], axis=1)
    return table.astype(ml_dtypes.bfloat16)


def whiten_kernel(starts_ref, record_hbm, table_ref, near_ref, count_ref, live_ref, out_ref, chunks, moved_rows, sems):
    windows, channels, span = chunks.shape
    blocks = NT // LANES
    last = record_hbm.shape[1] - span
    shifts = []
    for w in range(windows):
        first = starts_ref[w]
        base = pl.multiple_of(jnp.minimum(first - first % LANES, last), LANES)
        pltpu.make_async_copy(record_hbm.at[:, pl.ds(base, span)], chunks.at[w], sems.at[w]).start()
        shifts.append(first - base)
    lane = lax.broadcasted_iota(jnp.int32, (channels, LANES), 1)
    for w in range(windows):
        pltpu.make_async_copy(record_hbm.at[:, pl.ds(0, span)], chunks.at[w], sems.at[w]).wait()
        shift = shifts[w]
        low = lane < LANES - shift
        rolled = [
            pltpu.roll(chunks[w, :, pl.ds(b * LANES, LANES)].astype(jnp.float32), (LANES - shift) % LANES, 1)
            for b in range(blocks + 1)
        ]
        for b in range(blocks):
            moved_rows[pl.ds(w * channels, channels), pl.ds(b * LANES, LANES)] = jnp.where(
                low, rolled[b], rolled[b + 1]
            ).astype(jnp.bfloat16)
    spectra = jnp.dot(moved_rows[...], table_ref[...], preferred_element_type=jnp.float32)
    power = spectra * spectra
    smooth = jnp.dot(
        power, near_ref[...], precision=lax.Precision.HIGHEST, preferred_element_type=jnp.float32
    ) / count_ref[...]
    water_level = jnp.sum(power, axis=-1, keepdims=True) / NF
    gain_of = live_ref[...] / jnp.sqrt(smooth + 0.1 * water_level + 1e-06)
    out_ref[...] = (spectra * gain_of).T.astype(out_ref.dtype)


def whiten(record_rows, starts, live_mask, groups):
    channels, _ = record_rows.shape
    windows = starts.shape[0]
    per_group = NF // groups
    lane_group, lane_part, lane_bin = np.unravel_index(np.arange(2 * NF), (groups, 2, per_group))
    lane_bin = lane_group * per_group + lane_bin
    table = jnp.asarray(spectral_table()[:, lane_part * NF + lane_bin])
    near = (np.abs(lane_bin[:, None] - lane_bin[None, :]) <= 4).astype(np.float32)
    count = (np.abs(np.arange(NF)[:, None] - lane_bin[None, :]) <= 4).sum(axis=0, keepdims=True).astype(np.float32)
    live_rows = jnp.tile(live_mask.astype(jnp.float32), windows)[:, None]
    vmem = pl.BlockSpec(memory_space=pltpu.VMEM)
    return pl.pallas_call(
        whiten_kernel,
        out_shape=jax.ShapeDtypeStruct((2 * NF, windows * channels), jnp.bfloat16),
        in_specs=[pl.BlockSpec(memory_space=pltpu.SMEM), pl.BlockSpec(memory_space=pl.ANY), vmem, vmem, vmem, vmem],
        out_specs=vmem,
        scratch_shapes=[
            pltpu.VMEM((windows, channels, NT + LANES), jnp.bfloat16),
            pltpu.VMEM((windows * channels, NT), jnp.bfloat16),
            pltpu.SemaphoreType.DMA((windows,)),
        ],
    )(starts, record_rows, table, jnp.asarray(near), jnp.asarray(count), live_rows)


def halo(mine, hops, fibre_count):
    if fibre_count % 2:
        columns = [mine]
        for step in range(1, hops + 1):
            pairs = [(i, i - step) for i in range(step, fibre_count)]
            columns.append(lax.ppermute(mine, "fibre", pairs))
        return jnp.concatenate(columns, axis=0)
    strides = min(-(-hops // 2), (fibre_count - 1) // 2)
    own = [mine]
    for step in range(1, strides + 1):
        pairs = [(i, i - 2 * step) for i in range(2 * step, fibre_count)]
        own.append(lax.ppermute(mine, "fibre", pairs))
    swapped = lax.ppermute(jnp.concatenate(own, axis=0), "fibre", [(i, i ^ 1) for i in range(fibre_count)])
    swapped = jnp.split(swapped, strides + 1, axis=0)
    even = [part for pair in zip(own, swapped) for part in pair]
    odd = [part for pair in zip(own, swapped[1:] + [jnp.zeros_like(mine)]) for part in pair]
    odd_side = lax.axis_index("fibre") % 2 == 1
    return jnp.where(odd_side, jnp.concatenate(odd, axis=0), jnp.concatenate(even, axis=0))


def shards(record, offsets, live_mask):
    seg_count = lax.axis_size("seg")
    fibre_count = lax.axis_size("fibre")
    windows_count = offsets.shape[1]
    block = record.shape[1]
    own_block = whiten(record[0], offsets[0], live_mask, seg_count)
    channels = block * fibre_count
    per_owner = BAND // seg_count
    bins_each = NF // seg_count
    live_offsets = min(BAND, channels - 1)
    live_owners = -(-live_offsets // per_owner)
    kept = live_owners * per_owner
    span = block + kept
    hops = min(-(-span // block) - 1, fibre_count - 1)
    needed = -(-span // block)
    me = lax.axis_index("seg")

    split = own_block.reshape(seg_count, 2 * bins_each, windows_count * block)
    gathered = [lax.dynamic_index_in_dim(split, me, 0, keepdims=False)]
    for step in range(1, seg_count):
        sent = lax.dynamic_index_in_dim(split, (me + step) % seg_count, 0, keepdims=False)
        pairs = [(i, (i + step) % seg_count) for i in range(seg_count)]
        gathered.append(lax.ppermute(sent, "seg", pairs))
    mine = jnp.concatenate(gathered, axis=0)

    columns = halo(mine, hops, fibre_count).reshape((-1,) + mine.shape)[:needed]
    if columns.shape[0] < needed:
        columns = jnp.concatenate(
            [columns, jnp.zeros((needed - columns.shape[0],) + mine.shape, columns.dtype)], axis=0
        )
    right = columns.reshape(needed, seg_count, 2, bins_each, windows_count, block)
    re_own = right[0, :, 0]
    im_own = right[0, :, 1]
    left = jnp.stack([jnp.stack([re_own, im_own], axis=1), jnp.stack([im_own, -re_own], axis=1)])
    depth = seg_count * 2 * windows_count
    right = right.transpose(3, 1, 2, 4, 0, 5).reshape(bins_each, depth, needed * block)
    left = left.transpose(3, 0, 5, 1, 2, 4).reshape(bins_each, 2 * block, depth)
    cross = jnp.einsum("nik,nkj->nij", left, right, preferred_element_type=jnp.float32)
    cross = cross.reshape(bins_each, 2, block, needed * block)
    band = jnp.stack([cross[:, :, c, c + 1 : c + 1 + kept] for c in range(block)])
    band = band.transpose(3, 0, 2, 1) * (1.0 / math.sqrt(seg_count * windows_count))
    band = band.reshape(kept, block * 2 * bins_each)
    if kept < BAND:
        band = jnp.concatenate([band, jnp.zeros((BAND - kept, band.shape[1]), band.dtype)], axis=0)
    band = band.reshape(seg_count, per_owner, band.shape[1])

    collected = [lax.dynamic_index_in_dim(band, me, 0, keepdims=False)]
    for step in range(1, seg_count):
        sent = lax.dynamic_index_in_dim(band, (me + step) % seg_count, 0, keepdims=False)
        pairs = [(i, (i + step) % seg_count) for i in range(seg_count) if (i + step) % seg_count < live_owners]
        if pairs:
            collected.append(lax.ppermute(sent, "seg", pairs))
        else:
            collected.append(jnp.zeros_like(sent))
    collected = jnp.stack(collected)
    holder = (me - jnp.arange(seg_count, dtype=jnp.int32)) % seg_count
    by_bins = jnp.take(collected, holder, axis=0).reshape(seg_count, per_owner, block, 2, bins_each)
    return by_bins.transpose(1, 2, 3, 0, 4).reshape(per_owner, block, 2 * NF)


def solution(mesh):
    placed = (P("seg", "fibre", None), P("seg", None), P("fibre"))
    return jax.shard_map(
        shards, mesh=mesh, in_specs=placed, out_specs=P("seg", "fibre", None), check_vma=False
    )
```

```python
import math

import jax
import jax.numpy as jnp
import ml_dtypes
import numpy as np
from jax import lax
from jax.experimental import pallas as pl
from jax.experimental.pallas import tpu as pltpu
from jax.sharding import PartitionSpec as P

NF = 64
NT = 3072
BIN0 = 32
BAND = 256
LANES = 128


def spectral_table():
    sample_idx = np.arange(NT, dtype=np.int64)
    bin_idx = BIN0 + np.arange(NF, dtype=np.int64)
    phase_int = sample_idx[:, None] * bin_idx[None, :] % NT
    angle_rad = np.float32(2.0 * math.pi / NT) * phase_int.astype(np.float32)
    angle = angle_rad.astype(np.float64)
    table = np.concatenate([np.cos(angle), -np.sin(angle)], axis=1)
    return table.astype(ml_dtypes.bfloat16)


def whiten_kernel(starts_ref, record_hbm, table_ref, near_ref, count_ref, live_ref, out_ref, chunks, moved_rows, sems):
    windows, channels, span = chunks.shape
    blocks = NT // LANES
    last = record_hbm.shape[1] - span
    shifts = []
    for w in range(windows):
        first = starts_ref[w]
        base = pl.multiple_of(jnp.minimum(first - first % LANES, last), LANES)
        pltpu.make_async_copy(record_hbm.at[:, pl.ds(base, span)], chunks.at[w], sems.at[w]).start()
        shifts.append(first - base)
    lane = lax.broadcasted_iota(jnp.int32, (channels, LANES), 1)
    for w in range(windows):
        pltpu.make_async_copy(record_hbm.at[:, pl.ds(0, span)], chunks.at[w], sems.at[w]).wait()
        shift = shifts[w]
        low = lane < LANES - shift
        rolled = [
            pltpu.roll(chunks[w, :, pl.ds(b * LANES, LANES)].astype(jnp.float32), (LANES - shift) % LANES, 1)
            for b in range(blocks + 1)
        ]
        for b in range(blocks):
            moved_rows[pl.ds(w * channels, channels), pl.ds(b * LANES, LANES)] = jnp.where(
                low, rolled[b], rolled[b + 1]
            ).astype(jnp.bfloat16)
    spectra = jnp.dot(moved_rows[...], table_ref[...], preferred_element_type=jnp.float32)
    power = spectra * spectra
    smooth = jnp.dot(
        power, near_ref[...], precision=lax.Precision.HIGHEST, preferred_element_type=jnp.float32
    ) / count_ref[...]
    water_level = jnp.sum(power, axis=-1, keepdims=True) / NF
    gain_of = live_ref[...] / jnp.sqrt(smooth + 0.1 * water_level + 1e-06)
    whitened = spectra * gain_of
    groups, _, lanes_out = out_ref.shape
    width = 2 * LANES // (2 * groups)
    per_vreg = LANES // width
    lane = lax.broadcasted_iota(jnp.int32, (channels, LANES), 1)
    for g in range(groups):
        for v in range(lanes_out // LANES):
            gathered = jnp.zeros((channels, LANES), jnp.float32)
            for slot in range(per_vreg):
                w = v * per_vreg + slot
                piece = whitened[w * channels : (w + 1) * channels]
                piece = pltpu.roll(piece, (slot - g) * width % LANES, 1)
                inside = (lane >= slot * width) & (lane < (slot + 1) * width)
                gathered = jnp.where(inside, piece, gathered)
            out_ref[g, :, pl.ds(v * LANES, LANES)] = gathered.astype(out_ref.dtype)


def whiten(record_rows, starts, live_mask, groups):
    channels, _ = record_rows.shape
    windows = starts.shape[0]
    per_group = NF // groups
    lane_group, lane_part, lane_bin = np.unravel_index(np.arange(2 * NF), (groups, 2, per_group))
    lane_bin = lane_group * per_group + lane_bin
    table = jnp.asarray(spectral_table()[:, lane_part * NF + lane_bin])
    near = (np.abs(lane_bin[:, None] - lane_bin[None, :]) <= 4).astype(np.float32)
    count = (np.abs(np.arange(NF)[:, None] - lane_bin[None, :]) <= 4).sum(axis=0, keepdims=True).astype(np.float32)
    live_rows = jnp.tile(live_mask.astype(jnp.float32), windows)[:, None]
    vmem = pl.BlockSpec(memory_space=pltpu.VMEM)
    return pl.pallas_call(
        whiten_kernel,
        out_shape=jax.ShapeDtypeStruct((groups, channels, windows * 2 * per_group), jnp.bfloat16),
        in_specs=[pl.BlockSpec(memory_space=pltpu.SMEM), pl.BlockSpec(memory_space=pl.ANY), vmem, vmem, vmem, vmem],
        out_specs=vmem,
        scratch_shapes=[
            pltpu.VMEM((windows, channels, NT + LANES), jnp.bfloat16),
            pltpu.VMEM((windows * channels, NT), jnp.bfloat16),
            pltpu.SemaphoreType.DMA((windows,)),
        ],
    )(starts, record_rows, table, jnp.asarray(near), jnp.asarray(count), live_rows)


def halo(mine, hops, fibre_count):
    if fibre_count % 2:
        columns = [mine]
        for step in range(1, hops + 1):
            pairs = [(i, i - step) for i in range(step, fibre_count)]
            columns.append(lax.ppermute(mine, "fibre", pairs))
        return jnp.concatenate(columns, axis=0)
    strides = min(-(-hops // 2), (fibre_count - 1) // 2)
    own = [mine]
    for step in range(1, strides + 1):
        pairs = [(i, i - 2 * step) for i in range(2 * step, fibre_count)]
        own.append(lax.ppermute(mine, "fibre", pairs))
    swapped = lax.ppermute(jnp.concatenate(own, axis=0), "fibre", [(i, i ^ 1) for i in range(fibre_count)])
    swapped = jnp.split(swapped, strides + 1, axis=0)
    even = [part for pair in zip(own, swapped) for part in pair]
    odd = [part for pair in zip(own, swapped[1:] + [jnp.zeros_like(mine)]) for part in pair]
    odd_side = lax.axis_index("fibre") % 2 == 1
    return jnp.where(odd_side, jnp.concatenate(odd, axis=0), jnp.concatenate(even, axis=0))


def shards(record, offsets, live_mask):
    seg_count = lax.axis_size("seg")
    fibre_count = lax.axis_size("fibre")
    windows_count = offsets.shape[1]
    block = record.shape[1]
    split = whiten(record[0], offsets[0], live_mask, seg_count)
    channels = block * fibre_count
    per_owner = BAND // seg_count
    bins_each = NF // seg_count
    live_offsets = min(BAND, channels - 1)
    live_owners = -(-live_offsets // per_owner)
    kept = live_owners * per_owner
    span = block + kept
    hops = min(-(-span // block) - 1, fibre_count - 1)
    me = lax.axis_index("seg")
    rows = seg_count * windows_count

    gathered = [lax.dynamic_index_in_dim(split, me, 0, keepdims=False)]
    for step in range(1, seg_count):
        sent = lax.dynamic_index_in_dim(split, (me + step) % seg_count, 0, keepdims=False)
        pairs = [(i, (i + step) % seg_count) for i in range(seg_count)]
        gathered.append(lax.ppermute(sent, "seg", pairs))
    mine = jnp.concatenate(gathered, axis=1)

    columns = halo(mine, hops, fibre_count)[:span]
    if columns.shape[0] < span:
        columns = jnp.concatenate(
            [columns, jnp.zeros((span - columns.shape[0], columns.shape[1]), columns.dtype)], axis=0
        )
    right = columns.reshape(span, rows, 2, bins_each)
    re_own = right[:block, :, 0]
    im_own = right[:block, :, 1]
    left = jnp.stack([jnp.stack([re_own, im_own], axis=2), jnp.stack([im_own, -re_own], axis=2)])
    cross = jnp.einsum("ocspn,jspn->nocj", left, right, preferred_element_type=jnp.float32)
    band = jnp.stack([cross[:, :, c, c + 1 : c + 1 + kept] for c in range(block)])
    band = band.transpose(3, 0, 2, 1) * (1.0 / math.sqrt(seg_count * windows_count))
    band = band.reshape(kept, block * 2 * bins_each)
    if kept < BAND:
        band = jnp.concatenate([band, jnp.zeros((BAND - kept, band.shape[1]), band.dtype)], axis=0)
    band = band.reshape(seg_count, per_owner, band.shape[1])

    collected = [lax.dynamic_index_in_dim(band, me, 0, keepdims=False)]
    for step in range(1, seg_count):
        sent = lax.dynamic_index_in_dim(band, (me + step) % seg_count, 0, keepdims=False)
        pairs = [(i, (i + step) % seg_count) for i in range(seg_count) if (i + step) % seg_count < live_owners]
        if pairs:
            collected.append(lax.ppermute(sent, "seg", pairs))
        else:
            collected.append(jnp.zeros_like(sent))
    collected = jnp.stack(collected)
    holder = (me - jnp.arange(seg_count, dtype=jnp.int32)) % seg_count
    by_bins = jnp.take(collected, holder, axis=0).reshape(seg_count, per_owner, block, 2, bins_each)
    return by_bins.transpose(1, 2, 3, 0, 4).reshape(per_owner, block, 2 * NF)


def solution(mesh):
    placed = (P("seg", "fibre", None), P("seg", None), P("fibre"))
    return jax.shard_map(
        shards, mesh=mesh, in_specs=placed, out_specs=P("seg", "fibre", None), check_vma=False
    )
```

```python
import math

import jax
import jax.numpy as jnp
import ml_dtypes
import numpy as np
from jax import lax
from jax.experimental import pallas as pl
from jax.experimental.pallas import tpu as pltpu
from jax.sharding import PartitionSpec as P

NF = 64
NT = 3072
BIN0 = 32
BAND = 256
LANES = 128


def spectral_table():
    sample_idx = np.arange(NT, dtype=np.int64)
    bin_idx = BIN0 + np.arange(NF, dtype=np.int64)
    phase_int = sample_idx[:, None] * bin_idx[None, :] % NT
    angle_rad = np.float32(2.0 * math.pi / NT) * phase_int.astype(np.float32)
    angle = angle_rad.astype(np.float64)
    table = np.concatenate([np.cos(angle), -np.sin(angle)], axis=1)
    return table.astype(ml_dtypes.bfloat16)


def whiten_kernel(starts_ref, record_hbm, table_ref, near_ref, count_ref, live_ref, out_ref, chunks, moved_rows, sems):
    windows, channels, span = chunks.shape
    blocks = NT // LANES
    last = record_hbm.shape[1] - span
    shifts = []
    for w in range(windows):
        first = starts_ref[w]
        base = pl.multiple_of(jnp.minimum(first - first % LANES, last), LANES)
        pltpu.make_async_copy(record_hbm.at[:, pl.ds(base, span)], chunks.at[w], sems.at[w]).start()
        shifts.append(first - base)
    lane = lax.broadcasted_iota(jnp.int32, (channels, LANES), 1)
    for w in range(windows):
        pltpu.make_async_copy(record_hbm.at[:, pl.ds(0, span)], chunks.at[w], sems.at[w]).wait()
        shift = shifts[w]
        low = lane < LANES - shift
        rolled = [
            pltpu.roll(chunks[w, :, pl.ds(b * LANES, LANES)].astype(jnp.float32), (LANES - shift) % LANES, 1)
            for b in range(blocks + 1)
        ]
        for b in range(blocks):
            moved_rows[pl.ds(w * channels, channels), pl.ds(b * LANES, LANES)] = jnp.where(
                low, rolled[b], rolled[b + 1]
            ).astype(jnp.bfloat16)
    spectra = jnp.dot(moved_rows[...], table_ref[...], preferred_element_type=jnp.float32)
    power = spectra * spectra
    smooth = jnp.dot(
        power, near_ref[...], precision=lax.Precision.HIGHEST, preferred_element_type=jnp.float32
    ) / count_ref[...]
    water_level = jnp.sum(power, axis=-1, keepdims=True) / NF
    gain_of = live_ref[...] / jnp.sqrt(smooth + 0.1 * water_level + 1e-06)
    whitened = spectra * gain_of
    groups, _, lanes_out = out_ref.shape
    width = 2 * LANES // (2 * groups)
    per_vreg = LANES // width
    lane = lax.broadcasted_iota(jnp.int32, (channels, LANES), 1)
    for g in range(groups):
        for v in range(lanes_out // LANES):
            gathered = jnp.zeros((channels, LANES), jnp.float32)
            for slot in range(per_vreg):
                w = v * per_vreg + slot
                piece = whitened[w * channels : (w + 1) * channels]
                piece = pltpu.roll(piece, (slot - g) * width % LANES, 1)
                inside = (lane >= slot * width) & (lane < (slot + 1) * width)
                gathered = jnp.where(inside, piece, gathered)
            out_ref[g, :, pl.ds(v * LANES, LANES)] = gathered.astype(out_ref.dtype)


def whiten(record_rows, starts, live_mask, groups):
    channels, _ = record_rows.shape
    windows = starts.shape[0]
    per_group = NF // groups
    lane_group, lane_part, lane_bin = np.unravel_index(np.arange(2 * NF), (groups, 2, per_group))
    lane_bin = lane_group * per_group + lane_bin
    table = jnp.asarray(spectral_table()[:, lane_part * NF + lane_bin])
    near = (np.abs(lane_bin[:, None] - lane_bin[None, :]) <= 4).astype(np.float32)
    count = (np.abs(np.arange(NF)[:, None] - lane_bin[None, :]) <= 4).sum(axis=0, keepdims=True).astype(np.float32)
    live_rows = jnp.tile(live_mask.astype(jnp.float32), windows)[:, None]
    vmem = pl.BlockSpec(memory_space=pltpu.VMEM)
    return pl.pallas_call(
        whiten_kernel,
        out_shape=jax.ShapeDtypeStruct((groups, channels, windows * 2 * per_group), jnp.bfloat16),
        in_specs=[pl.BlockSpec(memory_space=pltpu.SMEM), pl.BlockSpec(memory_space=pl.ANY), vmem, vmem, vmem, vmem],
        out_specs=vmem,
        scratch_shapes=[
            pltpu.VMEM((windows, channels, NT + LANES), jnp.bfloat16),
            pltpu.VMEM((windows * channels, NT), jnp.bfloat16),
            pltpu.SemaphoreType.DMA((windows,)),
        ],
    )(starts, record_rows, table, jnp.asarray(near), jnp.asarray(count), live_rows)


def window_plan(owners, fibre_count, block, per_owner, width):
    strides, lowest = [], []
    for owner in range(owners):
        low = (owner * per_owner + 1) // block
        offsets = range(low, low + width)
        wanted = {q // 2 for q in offsets} | {(q + 1) // 2 for q in offsets}
        strides.append(sorted(k for k in wanted if 0 < 2 * k < fibre_count))
        lowest.append(low)
    rounds = max(len(s) for s in strides)
    zero = 2 * rounds + 2
    plan = np.full((owners * 2, width), zero, np.int32)
    for owner in range(owners):
        for parity in range(2):
            for i in range(width):
                q = lowest[owner] + i
                k, odd = divmod(q + parity, 2)
                if q == 0:
                    plan[owner * 2 + parity, i] = 0
                elif k == 0:
                    plan[owner * 2 + parity, i] = 1
                elif k in strides[owner]:
                    plan[owner * 2 + parity, i] = 2 + 2 * strides[owner].index(k) + (odd if parity == 0 else 1 - odd)
    return strides, lowest, rounds, plan


def shards(record, offsets, live_mask):
    seg_count = lax.axis_size("seg")
    fibre_count = lax.axis_size("fibre")
    windows_count = offsets.shape[1]
    block = record.shape[1]
    channels = block * fibre_count
    per_owner = BAND // seg_count
    live_offsets = min(BAND, channels - 1)
    owners = -(-live_offsets // per_owner)
    helpers = seg_count // owners if seg_count % owners == 0 else 1
    owners = seg_count // helpers
    bins_each = NF // helpers
    width = max((o * per_owner + per_owner + block - 1) // block - (o * per_owner + 1) // block + 1 for o in range(owners))
    me = lax.axis_index("seg")
    fibre_me = lax.axis_index("fibre")
    my_owner = me % owners
    split = whiten(record[0], offsets[0], live_mask, helpers)

    gathered = [lax.dynamic_index_in_dim(split, me // owners, 0, keepdims=False)]
    for step in range(1, seg_count):
        target = (me + step) % seg_count
        sent = lax.dynamic_index_in_dim(split, target // owners, 0, keepdims=False)
        pairs = [(i, (i + step) % seg_count) for i in range(seg_count)]
        gathered.append(lax.ppermute(sent, "seg", pairs))
    mine = jnp.concatenate(gathered, axis=1)

    strides, lowest, rounds, plan = window_plan(owners, fibre_count, block, per_owner, width)
    fetched = []
    for r in range(rounds):
        pairs = []
        for s in range(seg_count):
            if r < len(strides[s % owners]):
                step = 2 * strides[s % owners][r]
                pairs += [(s * fibre_count + f, s * fibre_count + f - step) for f in range(step, fibre_count)]
        fetched.append(lax.ppermute(mine, ("seg", "fibre"), pairs) if pairs else jnp.zeros_like(mine))
    held = jnp.stack([mine] + fetched)
    if fibre_count % 2 == 0:
        swapped = lax.ppermute(held, "fibre", [(i, i ^ 1) for i in range(fibre_count)])
    else:
        swapped = jnp.zeros_like(held)
    pool = jnp.stack([held, swapped], axis=1).reshape((-1,) + mine.shape)
    pool = jnp.concatenate([pool, jnp.zeros((1,) + mine.shape, mine.dtype)], axis=0)
    pick = jnp.asarray(plan)[my_owner * 2 + fibre_me % 2]
    right = jnp.take(pool, pick, axis=0).reshape(width * block, seg_count * windows_count, 2, bins_each)
    re_own = mine.reshape(block, seg_count * windows_count, 2, bins_each)[:, :, 0]
    im_own = mine.reshape(block, seg_count * windows_count, 2, bins_each)[:, :, 1]
    left = jnp.stack([jnp.stack([re_own, im_own], axis=2), jnp.stack([im_own, -re_own], axis=2)])
    cross = jnp.einsum("ocspn,jspn->nocj", left, right, preferred_element_type=jnp.float32)
    shifts = [o * per_owner - lowest[o] * block for o in range(owners)]
    if len(set(shifts)) > 1:
        cross = lax.dynamic_slice_in_dim(cross, jnp.asarray(shifts, jnp.int32)[my_owner], cross.shape[3] - max(shifts), 3)
    else:
        cross = cross[..., shifts[0]:]
    band = jnp.stack([cross[:, :, c, c + 1 : c + 1 + per_owner] for c in range(block)])
    band = band.transpose(3, 0, 2, 1) * (1.0 / math.sqrt(seg_count * windows_count))

    band = band.reshape(per_owner, block * 2 * bins_each)
    parts = [band]
    for helper in range(1, helpers):
        pairs = [(o + owners * helper, o) for o in range(owners)]
        parts.append(lax.ppermute(band, "seg", pairs))
    parts = jnp.stack(parts).reshape(helpers, per_owner, block, 2, bins_each)
    stacked = parts.transpose(1, 2, 3, 0, 4).reshape(per_owner, block, 2 * NF)
    return jnp.where(me < owners, stacked, jnp.zeros_like(stacked))


def solution(mesh):
    placed = (P("seg", "fibre", None), P("seg", None), P("fibre"))
    return jax.shard_map(
        shards, mesh=mesh, in_specs=placed, out_specs=P("seg", "fibre", None), check_vma=False
    )
```

```python
import math

import jax
import jax.numpy as jnp
import ml_dtypes
import numpy as np
from jax import lax
from jax.experimental import pallas as pl
from jax.experimental.pallas import tpu as pltpu
from jax.sharding import PartitionSpec as P

NF = 64
NT = 3072
BIN0 = 32
BAND = 256
LANES = 128


def spectral_table():
    sample_idx = np.arange(NT, dtype=np.int64)
    bin_idx = BIN0 + np.arange(NF, dtype=np.int64)
    phase_int = sample_idx[:, None] * bin_idx[None, :] % NT
    angle_rad = np.float32(2.0 * math.pi / NT) * phase_int.astype(np.float32)
    angle = angle_rad.astype(np.float64)
    table = np.concatenate([np.cos(angle), -np.sin(angle)], axis=1)
    return table.astype(ml_dtypes.bfloat16)


def whiten_kernel(starts_ref, place_ref, live_ref, record_hbm, table_ref, near_ref, count_ref, out_ref, chunks, moved_rows, sems):
    windows, channels, span = chunks.shape
    blocks = NT // LANES
    last = record_hbm.shape[1] - span
    shifts = []
    for w in range(windows):
        first = starts_ref[w]
        base = pl.multiple_of(jnp.minimum(first - first % LANES, last), LANES)
        pltpu.make_async_copy(record_hbm.at[:, pl.ds(base, span)], chunks.at[w], sems.at[w]).start()
        shifts.append(first - base)
    lane = lax.broadcasted_iota(jnp.int32, (channels, LANES), 1)
    for w in range(windows):
        pltpu.make_async_copy(record_hbm.at[:, pl.ds(0, span)], chunks.at[w], sems.at[w]).wait()
        shift = shifts[w]
        low = lane < LANES - shift
        rolled = [
            pltpu.roll(chunks[w, :, pl.ds(b * LANES, LANES)].astype(jnp.float32), (LANES - shift) % LANES, 1)
            for b in range(blocks + 1)
        ]
        for b in range(blocks):
            moved_rows[pl.ds(w * channels, channels), pl.ds(b * LANES, LANES)] = jnp.where(
                low, rolled[b], rolled[b + 1]
            ).astype(jnp.bfloat16)
    spectra = jnp.dot(moved_rows[...], table_ref[...], preferred_element_type=jnp.float32)
    power = spectra * spectra
    smooth = jnp.dot(
        power, near_ref[...], precision=lax.Precision.HIGHEST, preferred_element_type=jnp.float32
    ) / count_ref[...]
    water_level = jnp.sum(power, axis=-1, keepdims=True) / NF
    rows_of = lax.broadcasted_iota(jnp.int32, spectra.shape, 0) % channels
    live = jnp.zeros(spectra.shape, jnp.float32)
    for c in range(channels):
        live = jnp.where(rows_of == c, live_ref[c].astype(jnp.float32), live)
    gain_of = live / jnp.sqrt(smooth + 0.1 * water_level + 1e-06)
    whitened = spectra * gain_of
    groups, _, lanes_out = out_ref.shape
    width = 2 * LANES // (2 * groups)
    per_vreg = LANES // width
    lane = lax.broadcasted_iota(jnp.int32, (channels, LANES), 1)
    for d in range(groups):
        g = (place_ref[0] + d) % groups
        for v in range(lanes_out // LANES):
            gathered = jnp.zeros((channels, LANES), jnp.float32)
            for slot in range(per_vreg):
                w = v * per_vreg + slot
                piece = whitened[w * channels : (w + 1) * channels]
                piece = pltpu.roll(piece, (slot - g) * width % LANES, 1)
                inside = (lane >= slot * width) & (lane < (slot + 1) * width)
                gathered = jnp.where(inside, piece, gathered)
            out_ref[d, :, pl.ds(v * LANES, LANES)] = gathered.astype(out_ref.dtype)


def whiten(record_rows, starts, live_mask, groups, place):
    channels, _ = record_rows.shape
    windows = starts.shape[0]
    per_group = NF // groups
    lane_group, lane_part, lane_bin = np.unravel_index(np.arange(2 * NF), (groups, 2, per_group))
    lane_bin = lane_group * per_group + lane_bin
    table = jnp.asarray(spectral_table()[:, lane_part * NF + lane_bin])
    near = (np.abs(lane_bin[:, None] - lane_bin[None, :]) <= 4).astype(np.float32)
    count = (np.abs(np.arange(NF)[:, None] - lane_bin[None, :]) <= 4).sum(axis=0, keepdims=True).astype(np.float32)
    vmem = pl.BlockSpec(memory_space=pltpu.VMEM)
    smem = pl.BlockSpec(memory_space=pltpu.SMEM)
    return pl.pallas_call(
        whiten_kernel,
        out_shape=jax.ShapeDtypeStruct((groups, channels, windows * 2 * per_group), jnp.bfloat16),
        in_specs=[smem, smem, smem, pl.BlockSpec(memory_space=pl.ANY), vmem, vmem, vmem],
        out_specs=vmem,
        scratch_shapes=[
            pltpu.VMEM((windows, channels, NT + LANES), jnp.bfloat16),
            pltpu.VMEM((windows * channels, NT), jnp.bfloat16),
            pltpu.SemaphoreType.DMA((windows,)),
        ],
    )(starts, place.reshape(1), live_mask, record_rows, table, jnp.asarray(near), jnp.asarray(count))


def halo(mine, hops, fibre_count):
    if fibre_count % 2:
        columns = [mine]
        for step in range(1, hops + 1):
            pairs = [(i, i - step) for i in range(step, fibre_count)]
            columns.append(lax.ppermute(mine, "fibre", pairs))
        return jnp.concatenate(columns, axis=0)
    strides = min(-(-hops // 2), (fibre_count - 1) // 2)
    own = [mine]
    for step in range(1, strides + 1):
        pairs = [(i, i - 2 * step) for i in range(2 * step, fibre_count)]
        own.append(lax.ppermute(mine, "fibre", pairs))
    swapped = lax.ppermute(jnp.concatenate(own, axis=0), "fibre", [(i, i ^ 1) for i in range(fibre_count)])
    swapped = jnp.split(swapped, strides + 1, axis=0)
    even = [part for pair in zip(own, swapped) for part in pair]
    odd = [part for pair in zip(own, swapped[1:] + [jnp.zeros_like(mine)]) for part in pair]
    odd_side = lax.axis_index("fibre") % 2 == 1
    return jnp.where(odd_side, jnp.concatenate(odd, axis=0), jnp.concatenate(even, axis=0))


def shards(record, offsets, live_mask):
    seg_count = lax.axis_size("seg")
    fibre_count = lax.axis_size("fibre")
    windows_count = offsets.shape[1]
    block = record.shape[1]
    channels = block * fibre_count
    per_owner = BAND // seg_count
    bins_each = NF // seg_count
    live_offsets = min(BAND, channels - 1)
    live_owners = -(-live_offsets // per_owner)
    kept = live_owners * per_owner
    span = block + kept
    hops = min(-(-span // block) - 1, fibre_count - 1)
    me = lax.axis_index("seg")
    rows = seg_count * windows_count
    split = whiten(record[0], offsets[0], live_mask, seg_count, me.astype(jnp.int32))

    gathered = [split[0]]
    for step in range(1, seg_count):
        pairs = [(i, (i + step) % seg_count) for i in range(seg_count)]
        gathered.append(lax.ppermute(split[step], "seg", pairs))
    mine = jnp.concatenate(gathered, axis=1)

    columns = halo(mine, hops, fibre_count)[:span]
    if columns.shape[0] < span:
        columns = jnp.concatenate(
            [columns, jnp.zeros((span - columns.shape[0], columns.shape[1]), columns.dtype)], axis=0
        )
    right = columns.reshape(span, rows, 2, bins_each)
    re_own = right[:block, :, 0]
    im_own = right[:block, :, 1]
    left = jnp.stack([jnp.stack([re_own, im_own], axis=2), jnp.stack([im_own, -re_own], axis=2)])
    cross = jnp.einsum("ocspn,jspn->nocj", left, right, preferred_element_type=jnp.float32)
    band = jnp.stack([cross[:, :, c, c + 1 : c + 1 + kept] for c in range(block)])
    band = band.transpose(3, 0, 2, 1) * (1.0 / math.sqrt(seg_count * windows_count))
    band = band.reshape(kept, block * 2 * bins_each)
    if kept < BAND:
        band = jnp.concatenate([band, jnp.zeros((BAND - kept, band.shape[1]), band.dtype)], axis=0)
    band = band.reshape(seg_count, per_owner, band.shape[1])

    collected = [lax.dynamic_index_in_dim(band, me, 0, keepdims=False)]
    for step in range(1, seg_count):
        sent = lax.dynamic_index_in_dim(band, (me + step) % seg_count, 0, keepdims=False)
        pairs = [(i, (i + step) % seg_count) for i in range(seg_count) if (i + step) % seg_count < live_owners]
        if pairs:
            collected.append(lax.ppermute(sent, "seg", pairs))
        else:
            collected.append(jnp.zeros_like(sent))
    collected = jnp.stack(collected)
    holder = (me - jnp.arange(seg_count, dtype=jnp.int32)) % seg_count
    by_bins = jnp.take(collected, holder, axis=0).reshape(seg_count, per_owner, block, 2, bins_each)
    return by_bins.transpose(1, 2, 3, 0, 4).reshape(per_owner, block, 2 * NF)


def solution(mesh):
    placed = (P("seg", "fibre", None), P("seg", None), P("fibre"))
    return jax.shard_map(
        shards, mesh=mesh, in_specs=placed, out_specs=P("seg", "fibre", None), check_vma=False
    )
```

```python
import math

import jax
import jax.numpy as jnp
import ml_dtypes
import numpy as np
from jax import lax
from jax.experimental import pallas as pl
from jax.experimental.pallas import tpu as pltpu
from jax.sharding import PartitionSpec as P

NF = 64
NT = 3072
BIN0 = 32
BAND = 256
LANES = 128


def spectral_table():
    sample_idx = np.arange(NT, dtype=np.int64)
    bin_idx = BIN0 + np.arange(NF, dtype=np.int64)
    phase_int = sample_idx[:, None] * bin_idx[None, :] % NT
    angle_rad = np.float32(2.0 * math.pi / NT) * phase_int.astype(np.float32)
    angle = angle_rad.astype(np.float64)
    table = np.concatenate([np.cos(angle), -np.sin(angle)], axis=1)
    return table.astype(ml_dtypes.bfloat16)


def whiten_kernel(starts_ref, place_ref, live_ref, record_hbm, table_ref, near_ref, count_ref, *refs):
    *out_refs, chunks, moved_rows, sems = refs
    windows, channels, span = chunks.shape
    blocks = NT // LANES
    last = record_hbm.shape[1] - span
    shifts = []
    for w in range(windows):
        first = starts_ref[w]
        base = pl.multiple_of(jnp.minimum(first - first % LANES, last), LANES)
        pltpu.make_async_copy(record_hbm.at[:, pl.ds(base, span)], chunks.at[w], sems.at[w]).start()
        shifts.append(first - base)
    lane = lax.broadcasted_iota(jnp.int32, (channels, LANES), 1)
    for w in range(windows):
        pltpu.make_async_copy(record_hbm.at[:, pl.ds(0, span)], chunks.at[w], sems.at[w]).wait()
        shift = shifts[w]
        low = lane < LANES - shift
        rolled = [
            pltpu.roll(chunks[w, :, pl.ds(b * LANES, LANES)].astype(jnp.float32), (LANES - shift) % LANES, 1)
            for b in range(blocks + 1)
        ]
        for b in range(blocks):
            moved_rows[pl.ds(w * channels, channels), pl.ds(b * LANES, LANES)] = jnp.where(
                low, rolled[b], rolled[b + 1]
            ).astype(jnp.bfloat16)
    spectra = jnp.dot(moved_rows[...], table_ref[...], preferred_element_type=jnp.float32)
    power = spectra * spectra
    smooth = jnp.dot(
        power, near_ref[...], precision=lax.Precision.HIGHEST, preferred_element_type=jnp.float32
    ) / count_ref[...]
    water_level = jnp.sum(power, axis=-1, keepdims=True) / NF
    rows_of = lax.broadcasted_iota(jnp.int32, spectra.shape, 0) % channels
    live = jnp.zeros(spectra.shape, jnp.float32)
    for c in range(channels):
        live = jnp.where(rows_of == c, live_ref[c].astype(jnp.float32), live)
    gain_of = live / jnp.sqrt(smooth + 0.1 * water_level + 1e-06)
    whitened = spectra * gain_of
    groups = len(out_refs)
    _, lanes_out = out_refs[0].shape
    width = 2 * LANES // (2 * groups)
    per_vreg = LANES // width
    lane = lax.broadcasted_iota(jnp.int32, (channels, LANES), 1)
    for d in range(groups):
        g = (place_ref[0] + d) % groups
        for v in range(lanes_out // LANES):
            gathered = jnp.zeros((channels, LANES), jnp.float32)
            for slot in range(per_vreg):
                w = v * per_vreg + slot
                piece = whitened[w * channels : (w + 1) * channels]
                piece = pltpu.roll(piece, (slot - g) * width % LANES, 1)
                inside = (lane >= slot * width) & (lane < (slot + 1) * width)
                gathered = jnp.where(inside, piece, gathered)
            out_refs[d][:, pl.ds(v * LANES, LANES)] = gathered.astype(out_refs[d].dtype)


def whiten(record_rows, starts, live_mask, groups, place):
    channels, _ = record_rows.shape
    windows = starts.shape[0]
    per_group = NF // groups
    lane_group, lane_part, lane_bin = np.unravel_index(np.arange(2 * NF), (groups, 2, per_group))
    lane_bin = lane_group * per_group + lane_bin
    table = jnp.asarray(spectral_table()[:, lane_part * NF + lane_bin])
    near = (np.abs(lane_bin[:, None] - lane_bin[None, :]) <= 4).astype(np.float32)
    count = (np.abs(np.arange(NF)[:, None] - lane_bin[None, :]) <= 4).sum(axis=0, keepdims=True).astype(np.float32)
    vmem = pl.BlockSpec(memory_space=pltpu.VMEM)
    smem = pl.BlockSpec(memory_space=pltpu.SMEM)
    return pl.pallas_call(
        whiten_kernel,
        out_shape=[jax.ShapeDtypeStruct((channels, windows * 2 * per_group), jnp.bfloat16)] * groups,
        in_specs=[smem, smem, smem, pl.BlockSpec(memory_space=pl.ANY), vmem, vmem, vmem],
        out_specs=[vmem] * groups,
        scratch_shapes=[
            pltpu.VMEM((windows, channels, NT + LANES), jnp.bfloat16),
            pltpu.VMEM((windows * channels, NT), jnp.bfloat16),
            pltpu.SemaphoreType.DMA((windows,)),
        ],
    )(starts, place.reshape(1), live_mask, record_rows, table, jnp.asarray(near), jnp.asarray(count))


def halo(mine, hops, fibre_count):
    if fibre_count % 2:
        columns = [mine]
        for step in range(1, hops + 1):
            pairs = [(i, i - step) for i in range(step, fibre_count)]
            columns.append(lax.ppermute(mine, "fibre", pairs))
        return jnp.concatenate(columns, axis=0)
    strides = min(-(-hops // 2), (fibre_count - 1) // 2)
    own = [mine]
    for step in range(1, strides + 1):
        pairs = [(i, i - 2 * step) for i in range(2 * step, fibre_count)]
        own.append(lax.ppermute(mine, "fibre", pairs))
    swapped = lax.ppermute(jnp.concatenate(own, axis=0), "fibre", [(i, i ^ 1) for i in range(fibre_count)])
    swapped = jnp.split(swapped, strides + 1, axis=0)
    even = [part for pair in zip(own, swapped) for part in pair]
    odd = [part for pair in zip(own, swapped[1:] + [jnp.zeros_like(mine)]) for part in pair]
    odd_side = lax.axis_index("fibre") % 2 == 1
    return jnp.where(odd_side, jnp.concatenate(odd, axis=0), jnp.concatenate(even, axis=0))


def shards(record, offsets, live_mask):
    seg_count = lax.axis_size("seg")
    fibre_count = lax.axis_size("fibre")
    windows_count = offsets.shape[1]
    block = record.shape[1]
    channels = block * fibre_count
    per_owner = BAND // seg_count
    bins_each = NF // seg_count
    live_offsets = min(BAND, channels - 1)
    live_owners = -(-live_offsets // per_owner)
    kept = live_owners * per_owner
    span = block + kept
    hops = min(-(-span // block) - 1, fibre_count - 1)
    me = lax.axis_index("seg")
    rows = seg_count * windows_count
    split = whiten(record[0], offsets[0], live_mask, seg_count, me.astype(jnp.int32))

    gathered = [split[0]]
    for step in range(1, seg_count):
        pairs = [(i, (i + step) % seg_count) for i in range(seg_count)]
        gathered.append(lax.ppermute(split[step], "seg", pairs))
    mine = jnp.concatenate(gathered, axis=1)

    columns = halo(mine, hops, fibre_count)[:span]
    if columns.shape[0] < span:
        columns = jnp.concatenate(
            [columns, jnp.zeros((span - columns.shape[0], columns.shape[1]), columns.dtype)], axis=0
        )
    right = columns.reshape(span, rows, 2, bins_each)
    re_own = right[:block, :, 0]
    im_own = right[:block, :, 1]
    left = jnp.stack([jnp.stack([re_own, im_own], axis=2), jnp.stack([im_own, -re_own], axis=2)])
    cross = jnp.einsum("ocspn,jspn->nocj", left, right, preferred_element_type=jnp.float32)
    band = jnp.stack([cross[:, :, c, c + 1 : c + 1 + kept] for c in range(block)])
    band = band.transpose(3, 0, 2, 1) * (1.0 / math.sqrt(seg_count * windows_count))
    band = band.reshape(kept, block * 2 * bins_each)
    if kept < BAND:
        band = jnp.concatenate([band, jnp.zeros((BAND - kept, band.shape[1]), band.dtype)], axis=0)
    band = band.reshape(seg_count, per_owner, band.shape[1])

    collected = [lax.dynamic_index_in_dim(band, me, 0, keepdims=False)]
    for step in range(1, seg_count):
        sent = lax.dynamic_index_in_dim(band, (me + step) % seg_count, 0, keepdims=False)
        pairs = [(i, (i + step) % seg_count) for i in range(seg_count) if (i + step) % seg_count < live_owners]
        if pairs:
            collected.append(lax.ppermute(sent, "seg", pairs))
        else:
            collected.append(jnp.zeros_like(sent))
    collected = jnp.stack(collected)
    holder = (me - jnp.arange(seg_count, dtype=jnp.int32)) % seg_count
    by_bins = jnp.take(collected, holder, axis=0).reshape(seg_count, per_owner, block, 2, bins_each)
    return by_bins.transpose(1, 2, 3, 0, 4).reshape(per_owner, block, 2 * NF)


def solution(mesh):
    placed = (P("seg", "fibre", None), P("seg", None), P("fibre"))
    return jax.shard_map(
        shards, mesh=mesh, in_specs=placed, out_specs=P("seg", "fibre", None), check_vma=False
    )
```

```python
import math

import jax
import jax.numpy as jnp
import ml_dtypes
import numpy as np
from jax import lax
from jax.experimental import pallas as pl
from jax.experimental.pallas import tpu as pltpu
from jax.sharding import PartitionSpec as P

NF = 64
NT = 3072
BIN0 = 32
BAND = 256
LANES = 128


def spectral_table():
    sample_idx = np.arange(NT, dtype=np.int64)
    bin_idx = BIN0 + np.arange(NF, dtype=np.int64)
    phase_int = sample_idx[:, None] * bin_idx[None, :] % NT
    angle_rad = np.float32(2.0 * math.pi / NT) * phase_int.astype(np.float32)
    angle = angle_rad.astype(np.float64)
    table = np.concatenate([np.cos(angle), -np.sin(angle)], axis=1)
    return table.astype(ml_dtypes.bfloat16)


def whiten_kernel(starts_ref, place_ref, live_ref, record_hbm, table_ref, near_ref, count_ref, *refs):
    *out_refs, chunks, moved_rows, sems = refs
    windows, channels, span = chunks.shape
    blocks = NT // LANES
    last = record_hbm.shape[1] - span
    shifts = []
    for w in range(windows):
        first = starts_ref[w]
        base = pl.multiple_of(jnp.minimum(first - first % LANES, last), LANES)
        pltpu.make_async_copy(record_hbm.at[:, pl.ds(base, span)], chunks.at[w], sems.at[w]).start()
        shifts.append(first - base)
    lane = lax.broadcasted_iota(jnp.int32, (channels, LANES), 1)
    for w in range(windows):
        pltpu.make_async_copy(record_hbm.at[:, pl.ds(0, span)], chunks.at[w], sems.at[w]).wait()
        shift = shifts[w]
        low = lane < LANES - shift
        rolled = [
            pltpu.roll(chunks[w, :, pl.ds(b * LANES, LANES)].astype(jnp.float32), (LANES - shift) % LANES, 1)
            for b in range(blocks + 1)
        ]
        for b in range(blocks):
            moved_rows[pl.ds(w * channels, channels), pl.ds(b * LANES, LANES)] = jnp.where(
                low, rolled[b], rolled[b + 1]
            ).astype(jnp.bfloat16)
    spectra = jnp.dot(moved_rows[...], table_ref[...], preferred_element_type=jnp.float32)
    power = spectra * spectra
    smooth = jnp.dot(
        power, near_ref[...], precision=lax.Precision.HIGHEST, preferred_element_type=jnp.float32
    ) / count_ref[...]
    water_level = jnp.sum(power, axis=-1, keepdims=True) / NF
    rows_of = lax.broadcasted_iota(jnp.int32, spectra.shape, 0) % channels
    live = jnp.zeros(spectra.shape, jnp.float32)
    for c in range(channels):
        live = jnp.where(rows_of == c, live_ref[c].astype(jnp.float32), live)
    gain_of = live / jnp.sqrt(smooth + 0.1 * water_level + 1e-06)
    whitened = spectra * gain_of
    groups = len(out_refs)
    _, lanes_out = out_refs[0].shape
    width = 2 * LANES // (2 * groups)
    per_vreg = LANES // width
    lane = lax.broadcasted_iota(jnp.int32, (channels, LANES), 1)
    for d in range(groups):
        g = (place_ref[0] + d) % groups
        for v in range(lanes_out // LANES):
            gathered = jnp.zeros((channels, LANES), jnp.float32)
            for slot in range(per_vreg):
                w = v * per_vreg + slot
                piece = whitened[w * channels : (w + 1) * channels]
                piece = pltpu.roll(piece, (slot - g) * width % LANES, 1)
                inside = (lane >= slot * width) & (lane < (slot + 1) * width)
                gathered = jnp.where(inside, piece, gathered)
            out_refs[d][:, pl.ds(v * LANES, LANES)] = gathered.astype(out_refs[d].dtype)


def whiten(record_rows, starts, live_mask, groups, place):
    channels, _ = record_rows.shape
    windows = starts.shape[0]
    per_group = NF // groups
    lane_group, lane_part, lane_bin = np.unravel_index(np.arange(2 * NF), (groups, 2, per_group))
    lane_bin = lane_group * per_group + lane_bin
    table = jnp.asarray(spectral_table()[:, lane_part * NF + lane_bin])
    near = (np.abs(lane_bin[:, None] - lane_bin[None, :]) <= 4).astype(np.float32)
    count = (np.abs(np.arange(NF)[:, None] - lane_bin[None, :]) <= 4).sum(axis=0, keepdims=True).astype(np.float32)
    vmem = pl.BlockSpec(memory_space=pltpu.VMEM)
    smem = pl.BlockSpec(memory_space=pltpu.SMEM)
    return pl.pallas_call(
        whiten_kernel,
        out_shape=[jax.ShapeDtypeStruct((channels, windows * 2 * per_group), jnp.bfloat16)] * groups,
        in_specs=[smem, smem, smem, pl.BlockSpec(memory_space=pl.ANY), vmem, vmem, vmem],
        out_specs=[vmem] * groups,
        scratch_shapes=[
            pltpu.VMEM((windows, channels, NT + LANES), jnp.bfloat16),
            pltpu.VMEM((windows * channels, NT), jnp.bfloat16),
            pltpu.SemaphoreType.DMA((windows,)),
        ],
    )(starts, place.reshape(1), live_mask, record_rows, table, jnp.asarray(near), jnp.asarray(count))


def band_kernel(place_ref, own_ref, right_ref, *refs):
    *slot_refs, left, staged = refs
    block, lanes = own_ref.shape
    groups = len(slot_refs)
    per_owner, slot_lanes = slot_refs[0].shape
    width = slot_lanes // block
    bins_each = width // 2
    kept = staged.shape[0]
    scale = 1.0 / math.sqrt(lanes // width)
    lane = lax.broadcasted_iota(jnp.int32, (bins_each, lanes), 1)
    row = lax.broadcasted_iota(jnp.int32, (bins_each, lanes), 0)
    keep = lane % bins_each == row
    own = own_ref[...].astype(jnp.float32)
    turned = jnp.where(
        (lax.broadcasted_iota(jnp.int32, own.shape, 1) // bins_each) % 2 == 0,
        pltpu.roll(own, lanes - bins_each, 1),
        -pltpu.roll(own, bins_each, 1),
    )
    for c in range(block):
        for o, source in enumerate((own, turned)):
            rows = jnp.where(keep, jnp.broadcast_to(source[c : c + 1], (bins_each, lanes)), 0.0)
            left[pl.ds((2 * c + o) * bins_each, bins_each), :] = rows.astype(left.dtype)
    cross = lax.dot_general(
        left[...], right_ref[...], (((1,), (1,)), ((), ())), preferred_element_type=jnp.float32
    )
    span = cross.shape[1]
    per_vreg = LANES // width
    out_lane = lax.broadcasted_iota(jnp.int32, (kept, LANES), 1)
    columns = [jnp.zeros((kept, LANES), jnp.float32) for _ in range(slot_lanes // LANES)]
    for c in range(block):
        part = cross[c * width : (c + 1) * width]
        part = pltpu.roll(part, span - (c + 1), 1)[:, :kept]
        part = jnp.concatenate([part, jnp.zeros((LANES - width, kept), jnp.float32)], axis=0).T
        slot = c % per_vreg
        part = pltpu.roll(part, slot * width, 1)
        inside = (out_lane >= slot * width) & (out_lane < (slot + 1) * width)
        columns[c // per_vreg] = jnp.where(inside, part, columns[c // per_vreg])
    staged[...] = jnp.concatenate(columns, axis=1) * scale
    for d in range(groups):
        owner = (place_ref[0] + d) % groups
        start = pl.multiple_of(jnp.minimum(owner * per_owner, kept - per_owner), per_owner)
        block_rows = staged[pl.ds(start, per_owner), :]
        slot_refs[d][...] = jnp.where(owner * per_owner < kept, block_rows, jnp.zeros_like(block_rows))


def band(place, own, right, groups, per_owner, kept):
    block, lanes = own.shape
    width = 2 * NF // groups
    vmem = pl.BlockSpec(memory_space=pltpu.VMEM)
    return pl.pallas_call(
        band_kernel,
        out_shape=[jax.ShapeDtypeStruct((per_owner, block * width), jnp.float32)] * groups,
        in_specs=[pl.BlockSpec(memory_space=pltpu.SMEM), vmem, vmem],
        out_specs=[vmem] * groups,
        scratch_shapes=[
            pltpu.VMEM((block * width, lanes), jnp.bfloat16),
            pltpu.VMEM((kept, block * width), jnp.float32),
        ],
    )(place.reshape(1), own, right)


def halo(mine, hops, fibre_count):
    if fibre_count % 2:
        columns = [mine]
        for step in range(1, hops + 1):
            pairs = [(i, i - step) for i in range(step, fibre_count)]
            columns.append(lax.ppermute(mine, "fibre", pairs))
        return jnp.concatenate(columns, axis=0)
    strides = min(-(-hops // 2), (fibre_count - 1) // 2)
    own = [mine]
    for step in range(1, strides + 1):
        pairs = [(i, i - 2 * step) for i in range(2 * step, fibre_count)]
        own.append(lax.ppermute(mine, "fibre", pairs))
    swapped = lax.ppermute(jnp.concatenate(own, axis=0), "fibre", [(i, i ^ 1) for i in range(fibre_count)])
    swapped = jnp.split(swapped, strides + 1, axis=0)
    even = [part for pair in zip(own, swapped) for part in pair]
    odd = [part for pair in zip(own, swapped[1:] + [jnp.zeros_like(mine)]) for part in pair]
    odd_side = lax.axis_index("fibre") % 2 == 1
    return jnp.where(odd_side, jnp.concatenate(odd, axis=0), jnp.concatenate(even, axis=0))


def shards(record, offsets, live_mask):
    seg_count = lax.axis_size("seg")
    fibre_count = lax.axis_size("fibre")
    windows_count = offsets.shape[1]
    block = record.shape[1]
    channels = block * fibre_count
    per_owner = BAND // seg_count
    bins_each = NF // seg_count
    live_offsets = min(BAND, channels - 1)
    live_owners = -(-live_offsets // per_owner)
    kept = live_owners * per_owner
    span = block + kept
    hops = min(-(-span // block) - 1, fibre_count - 1)
    me = lax.axis_index("seg")
    rows = seg_count * windows_count
    split = whiten(record[0], offsets[0], live_mask, seg_count, me.astype(jnp.int32))

    gathered = [split[0]]
    for step in range(1, seg_count):
        pairs = [(i, (i + step) % seg_count) for i in range(seg_count)]
        gathered.append(lax.ppermute(split[step], "seg", pairs))
    mine = jnp.concatenate(gathered, axis=1)

    columns = halo(mine, hops, fibre_count)[:span]
    if columns.shape[0] < span:
        columns = jnp.concatenate(
            [columns, jnp.zeros((span - columns.shape[0], columns.shape[1]), columns.dtype)], axis=0
        )
    padded = -(-span // LANES) * LANES
    columns = jnp.concatenate(
        [columns, jnp.zeros((padded - columns.shape[0], columns.shape[1]), columns.dtype)], axis=0
    )
    slots = band(me.astype(jnp.int32), mine, columns, seg_count, per_owner, kept)

    collected = [slots[0]]
    for step in range(1, seg_count):
        pairs = [(i, (i + step) % seg_count) for i in range(seg_count) if (i + step) % seg_count < live_owners]
        if pairs:
            collected.append(lax.ppermute(slots[step], "seg", pairs))
        else:
            collected.append(jnp.zeros_like(slots[step]))
    collected = jnp.stack(collected)
    holder = (me - jnp.arange(seg_count, dtype=jnp.int32)) % seg_count
    by_bins = jnp.take(collected, holder, axis=0).reshape(seg_count, per_owner, block, 2, bins_each)
    return by_bins.transpose(1, 2, 3, 0, 4).reshape(per_owner, block, 2 * NF)


def solution(mesh):
    placed = (P("seg", "fibre", None), P("seg", None), P("fibre"))
    return jax.shard_map(
        shards, mesh=mesh, in_specs=placed, out_specs=P("seg", "fibre", None), check_vma=False
    )
```

```python
import math

import jax
import jax.numpy as jnp
import ml_dtypes
import numpy as np
from jax import lax
from jax.experimental import pallas as pl
from jax.experimental.pallas import tpu as pltpu
from jax.sharding import PartitionSpec as P

NF = 64
NT = 3072
BIN0 = 32
BAND = 256
LANES = 128


def spectral_table():
    sample_idx = np.arange(NT, dtype=np.int64)
    bin_idx = BIN0 + np.arange(NF, dtype=np.int64)
    phase_int = sample_idx[:, None] * bin_idx[None, :] % NT
    angle_rad = np.float32(2.0 * math.pi / NT) * phase_int.astype(np.float32)
    angle = angle_rad.astype(np.float64)
    table = np.concatenate([np.cos(angle), -np.sin(angle)], axis=1)
    return table.astype(ml_dtypes.bfloat16)


def whiten_kernel(starts_ref, place_ref, live_ref, record_hbm, table_ref, count_ref, *refs):
    *out_refs, chunks, moved_rows, sems = refs
    windows, channels, span = chunks.shape
    blocks = NT // LANES
    last = record_hbm.shape[1] - span
    shifts = []
    for w in range(windows):
        first = starts_ref[w]
        base = pl.multiple_of(jnp.minimum(first - first % LANES, last), LANES)
        pltpu.make_async_copy(record_hbm.at[:, pl.ds(base, span)], chunks.at[w], sems.at[w]).start()
        shifts.append(first - base)
    lane = lax.broadcasted_iota(jnp.int32, (channels, LANES), 1)
    for w in range(windows):
        pltpu.make_async_copy(record_hbm.at[:, pl.ds(0, span)], chunks.at[w], sems.at[w]).wait()
        shift = shifts[w]
        low = lane < LANES - shift
        rolled = [
            pltpu.roll(chunks[w, :, pl.ds(b * LANES, LANES)].astype(jnp.float32), (LANES - shift) % LANES, 1)
            for b in range(blocks + 1)
        ]
        for b in range(blocks):
            moved_rows[pl.ds(w * channels, channels), pl.ds(b * LANES, LANES)] = jnp.where(
                low, rolled[b], rolled[b + 1]
            ).astype(jnp.bfloat16)
    spectra = jnp.dot(moved_rows[...], table_ref[...], preferred_element_type=jnp.float32)
    squares = spectra * spectra
    power = squares + pltpu.roll(squares, NF, 1)
    bin_of = lax.broadcasted_iota(jnp.int32, power.shape, 1) % NF
    smooth = power
    for step in range(1, 5):
        above = pltpu.roll(power, 2 * NF - step, 1)
        below = pltpu.roll(power, step, 1)
        smooth = smooth + jnp.where(bin_of + step < NF, above, 0.0) + jnp.where(bin_of >= step, below, 0.0)
    smooth = smooth / count_ref[...]
    water_level = jnp.sum(squares, axis=-1, keepdims=True) / NF
    rows_of = lax.broadcasted_iota(jnp.int32, spectra.shape, 0) % channels
    live = jnp.zeros(spectra.shape, jnp.float32)
    for c in range(channels):
        live = jnp.where(rows_of == c, live_ref[c].astype(jnp.float32), live)
    gain_of = live / jnp.sqrt(smooth + 0.1 * water_level + 1e-06)
    whitened = spectra * gain_of
    groups = len(out_refs)
    _, lanes_out = out_refs[0].shape
    width = 2 * LANES // (2 * groups)
    per_vreg = LANES // width
    lane = lax.broadcasted_iota(jnp.int32, (channels, LANES), 1)
    for d in range(groups):
        g = (place_ref[0] + d) % groups
        for v in range(lanes_out // LANES):
            gathered = jnp.zeros((channels, LANES), jnp.float32)
            for slot in range(per_vreg):
                w = v * per_vreg + slot
                piece = whitened[w * channels : (w + 1) * channels]
                half = width // 2
                for part in range(2):
                    moved = pltpu.roll(piece, (slot * width + part * half - part * NF - g * half) % LANES, 1)
                    inside = (lane >= slot * width + part * half) & (lane < slot * width + (part + 1) * half)
                    gathered = jnp.where(inside, moved, gathered)
            out_refs[d][:, pl.ds(v * LANES, LANES)] = gathered.astype(out_refs[d].dtype)


def whiten(record_rows, starts, live_mask, groups, place):
    channels, _ = record_rows.shape
    windows = starts.shape[0]
    per_group = NF // groups
    table = jnp.asarray(spectral_table())
    lane_bin = np.arange(2 * NF) % NF
    count = (np.abs(np.arange(NF)[:, None] - lane_bin[None, :]) <= 4).sum(axis=0, keepdims=True).astype(np.float32)
    vmem = pl.BlockSpec(memory_space=pltpu.VMEM)
    smem = pl.BlockSpec(memory_space=pltpu.SMEM)
    return pl.pallas_call(
        whiten_kernel,
        out_shape=[jax.ShapeDtypeStruct((channels, windows * 2 * per_group), jnp.bfloat16)] * groups,
        in_specs=[smem, smem, smem, pl.BlockSpec(memory_space=pl.ANY), vmem, vmem],
        out_specs=[vmem] * groups,
        scratch_shapes=[
            pltpu.VMEM((windows, channels, NT + LANES), jnp.bfloat16),
            pltpu.VMEM((windows * channels, NT), jnp.bfloat16),
            pltpu.SemaphoreType.DMA((windows,)),
        ],
    )(starts, place.reshape(1), live_mask, record_rows, table, jnp.asarray(count))


def halo(mine, hops, fibre_count):
    if fibre_count % 2:
        columns = [mine]
        for step in range(1, hops + 1):
            pairs = [(i, i - step) for i in range(step, fibre_count)]
            columns.append(lax.ppermute(mine, "fibre", pairs))
        return jnp.concatenate(columns, axis=0)
    strides = min(-(-hops // 2), (fibre_count - 1) // 2)
    own = [mine]
    for step in range(1, strides + 1):
        pairs = [(i, i - 2 * step) for i in range(2 * step, fibre_count)]
        own.append(lax.ppermute(mine, "fibre", pairs))
    swapped = lax.ppermute(jnp.concatenate(own, axis=0), "fibre", [(i, i ^ 1) for i in range(fibre_count)])
    swapped = jnp.split(swapped, strides + 1, axis=0)
    even = [part for pair in zip(own, swapped) for part in pair]
    odd = [part for pair in zip(own, swapped[1:] + [jnp.zeros_like(mine)]) for part in pair]
    odd_side = lax.axis_index("fibre") % 2 == 1
    return jnp.where(odd_side, jnp.concatenate(odd, axis=0), jnp.concatenate(even, axis=0))


def shards(record, offsets, live_mask):
    seg_count = lax.axis_size("seg")
    fibre_count = lax.axis_size("fibre")
    windows_count = offsets.shape[1]
    block = record.shape[1]
    channels = block * fibre_count
    per_owner = BAND // seg_count
    bins_each = NF // seg_count
    live_offsets = min(BAND, channels - 1)
    live_owners = -(-live_offsets // per_owner)
    kept = live_owners * per_owner
    span = block + kept
    hops = min(-(-span // block) - 1, fibre_count - 1)
    me = lax.axis_index("seg")
    rows = seg_count * windows_count
    split = whiten(record[0], offsets[0], live_mask, seg_count, me.astype(jnp.int32))

    gathered = [split[0]]
    for step in range(1, seg_count):
        pairs = [(i, (i + step) % seg_count) for i in range(seg_count)]
        gathered.append(lax.ppermute(split[step], "seg", pairs))
    mine = jnp.concatenate(gathered, axis=1)

    columns = halo(mine, hops, fibre_count)[:span]
    if columns.shape[0] < span:
        columns = jnp.concatenate(
            [columns, jnp.zeros((span - columns.shape[0], columns.shape[1]), columns.dtype)], axis=0
        )
    right = columns.reshape(span, rows, 2, bins_each)
    re_own = right[:block, :, 0]
    im_own = right[:block, :, 1]
    left = jnp.stack([jnp.stack([re_own, im_own], axis=2), jnp.stack([im_own, -re_own], axis=2)])
    cross = jnp.einsum("ocspn,jspn->nocj", left, right, preferred_element_type=jnp.float32)
    band = jnp.stack([cross[:, :, c, c + 1 : c + 1 + kept] for c in range(block)])
    band = band.transpose(3, 0, 2, 1) * (1.0 / math.sqrt(seg_count * windows_count))
    band = band.reshape(kept, block * 2 * bins_each)
    if kept < BAND:
        band = jnp.concatenate([band, jnp.zeros((BAND - kept, band.shape[1]), band.dtype)], axis=0)
    band = band.reshape(seg_count, per_owner, band.shape[1])

    collected = [lax.dynamic_index_in_dim(band, me, 0, keepdims=False)]
    for step in range(1, seg_count):
        sent = lax.dynamic_index_in_dim(band, (me + step) % seg_count, 0, keepdims=False)
        pairs = [(i, (i + step) % seg_count) for i in range(seg_count) if (i + step) % seg_count < live_owners]
        if pairs:
            collected.append(lax.ppermute(sent, "seg", pairs))
        else:
            collected.append(jnp.zeros_like(sent))
    collected = jnp.stack(collected)
    holder = (me - jnp.arange(seg_count, dtype=jnp.int32)) % seg_count
    by_bins = jnp.take(collected, holder, axis=0).reshape(seg_count, per_owner, block, 2, bins_each)
    return by_bins.transpose(1, 2, 3, 0, 4).reshape(per_owner, block, 2 * NF)


def solution(mesh):
    placed = (P("seg", "fibre", None), P("seg", None), P("fibre"))
    return jax.shard_map(
        shards, mesh=mesh, in_specs=placed, out_specs=P("seg", "fibre", None), check_vma=False
    )
```

```python
import math

import jax
import jax.numpy as jnp
import ml_dtypes
import numpy as np
from jax import lax
from jax.experimental import pallas as pl
from jax.experimental.pallas import tpu as pltpu
from jax.sharding import PartitionSpec as P

NF = 64
NT = 3072
BIN0 = 32
BAND = 256
LANES = 128


def spectral_table():
    sample_idx = np.arange(NT, dtype=np.int64)
    bin_idx = BIN0 + np.arange(NF, dtype=np.int64)
    phase_int = sample_idx[:, None] * bin_idx[None, :] % NT
    angle_rad = np.float32(2.0 * math.pi / NT) * phase_int.astype(np.float32)
    angle = angle_rad.astype(np.float64)
    table = np.concatenate([np.cos(angle), -np.sin(angle)], axis=1)
    return table.astype(ml_dtypes.bfloat16)


def whiten_kernel(starts_ref, place_ref, live_ref, record_hbm, table_ref, near_ref, count_ref, *refs):
    *out_refs, chunks, moved_rows, sems = refs
    windows, channels, span = chunks.shape
    blocks = NT // LANES
    last = record_hbm.shape[1] - span
    shifts = []
    for w in range(windows):
        first = starts_ref[w]
        base = pl.multiple_of(jnp.minimum(first - first % LANES, last), LANES)
        pltpu.make_async_copy(record_hbm.at[:, pl.ds(base, span)], chunks.at[w], sems.at[w]).start()
        shifts.append(first - base)
    lane = lax.broadcasted_iota(jnp.int32, (channels, LANES), 1)
    for w in range(windows):
        pltpu.make_async_copy(record_hbm.at[:, pl.ds(0, span)], chunks.at[w], sems.at[w]).wait()
        shift = shifts[w]
        low = lane < LANES - shift
        rolled = [
            pltpu.roll(chunks[w, :, pl.ds(b * LANES, LANES)], (LANES - shift) % LANES, 1)
            for b in range(blocks + 1)
        ]
        for b in range(blocks):
            moved_rows[pl.ds(w * channels, channels), pl.ds(b * LANES, LANES)] = jnp.where(
                low, rolled[b], rolled[b + 1]
            )
    spectra = jnp.dot(moved_rows[...], table_ref[...], preferred_element_type=jnp.float32)
    power = spectra * spectra
    smooth = jnp.dot(
        power, near_ref[...], precision=lax.Precision.HIGHEST, preferred_element_type=jnp.float32
    ) / count_ref[...]
    water_level = jnp.sum(power, axis=-1, keepdims=True) / NF
    rows_of = lax.broadcasted_iota(jnp.int32, spectra.shape, 0) % channels
    live = jnp.zeros(spectra.shape, jnp.float32)
    for c in range(channels):
        live = jnp.where(rows_of == c, live_ref[c].astype(jnp.float32), live)
    gain_of = live / jnp.sqrt(smooth + 0.1 * water_level + 1e-06)
    whitened = spectra * gain_of
    groups = len(out_refs)
    _, lanes_out = out_refs[0].shape
    width = 2 * LANES // (2 * groups)
    per_vreg = LANES // width
    lane = lax.broadcasted_iota(jnp.int32, (channels, LANES), 1)
    for d in range(groups):
        g = (place_ref[0] + d) % groups
        for v in range(lanes_out // LANES):
            gathered = jnp.zeros((channels, LANES), jnp.float32)
            for slot in range(per_vreg):
                w = v * per_vreg + slot
                piece = whitened[w * channels : (w + 1) * channels]
                piece = pltpu.roll(piece, (slot - g) * width % LANES, 1)
                inside = (lane >= slot * width) & (lane < (slot + 1) * width)
                gathered = jnp.where(inside, piece, gathered)
            out_refs[d][:, pl.ds(v * LANES, LANES)] = gathered.astype(out_refs[d].dtype)


def whiten(record_rows, starts, live_mask, groups, place):
    channels, _ = record_rows.shape
    windows = starts.shape[0]
    per_group = NF // groups
    lane_group, lane_part, lane_bin = np.unravel_index(np.arange(2 * NF), (groups, 2, per_group))
    lane_bin = lane_group * per_group + lane_bin
    table = jnp.asarray(spectral_table()[:, lane_part * NF + lane_bin])
    near = (np.abs(lane_bin[:, None] - lane_bin[None, :]) <= 4).astype(np.float32)
    count = (np.abs(np.arange(NF)[:, None] - lane_bin[None, :]) <= 4).sum(axis=0, keepdims=True).astype(np.float32)
    vmem = pl.BlockSpec(memory_space=pltpu.VMEM)
    smem = pl.BlockSpec(memory_space=pltpu.SMEM)
    return pl.pallas_call(
        whiten_kernel,
        out_shape=[jax.ShapeDtypeStruct((channels, windows * 2 * per_group), jnp.bfloat16)] * groups,
        in_specs=[smem, smem, smem, pl.BlockSpec(memory_space=pl.ANY), vmem, vmem, vmem],
        out_specs=[vmem] * groups,
        scratch_shapes=[
            pltpu.VMEM((windows, channels, NT + LANES), jnp.bfloat16),
            pltpu.VMEM((windows * channels, NT), jnp.bfloat16),
            pltpu.SemaphoreType.DMA((windows,)),
        ],
    )(starts, place.reshape(1), live_mask, record_rows, table, jnp.asarray(near), jnp.asarray(count))


def halo(mine, hops, fibre_count):
    if fibre_count % 2:
        columns = [mine]
        for step in range(1, hops + 1):
            pairs = [(i, i - step) for i in range(step, fibre_count)]
            columns.append(lax.ppermute(mine, "fibre", pairs))
        return jnp.concatenate(columns, axis=0)
    strides = min(-(-hops // 2), (fibre_count - 1) // 2)
    own = [mine]
    for step in range(1, strides + 1):
        pairs = [(i, i - 2 * step) for i in range(2 * step, fibre_count)]
        own.append(lax.ppermute(mine, "fibre", pairs))
    swapped = lax.ppermute(jnp.concatenate(own, axis=0), "fibre", [(i, i ^ 1) for i in range(fibre_count)])
    swapped = jnp.split(swapped, strides + 1, axis=0)
    even = [part for pair in zip(own, swapped) for part in pair]
    odd = [part for pair in zip(own, swapped[1:] + [jnp.zeros_like(mine)]) for part in pair]
    odd_side = lax.axis_index("fibre") % 2 == 1
    return jnp.where(odd_side, jnp.concatenate(odd, axis=0), jnp.concatenate(even, axis=0))


def shards(record, offsets, live_mask):
    seg_count = lax.axis_size("seg")
    fibre_count = lax.axis_size("fibre")
    windows_count = offsets.shape[1]
    block = record.shape[1]
    channels = block * fibre_count
    per_owner = BAND // seg_count
    bins_each = NF // seg_count
    live_offsets = min(BAND, channels - 1)
    live_owners = -(-live_offsets // per_owner)
    kept = live_owners * per_owner
    span = block + kept
    hops = min(-(-span // block) - 1, fibre_count - 1)
    me = lax.axis_index("seg")
    rows = seg_count * windows_count
    split = whiten(record[0], offsets[0], live_mask, seg_count, me.astype(jnp.int32))

    gathered = [split[0]]
    for step in range(1, seg_count):
        pairs = [(i, (i + step) % seg_count) for i in range(seg_count)]
        gathered.append(lax.ppermute(split[step], "seg", pairs))
    mine = jnp.concatenate(gathered, axis=1)

    columns = halo(mine, hops, fibre_count)[:span]
    if columns.shape[0] < span:
        columns = jnp.concatenate(
            [columns, jnp.zeros((span - columns.shape[0], columns.shape[1]), columns.dtype)], axis=0
        )
    right = columns.reshape(span, rows, 2, bins_each)
    re_own = right[:block, :, 0]
    im_own = right[:block, :, 1]
    left = jnp.stack([jnp.stack([re_own, im_own], axis=2), jnp.stack([im_own, -re_own], axis=2)])
    cross = jnp.einsum("ocspn,jspn->nocj", left, right, preferred_element_type=jnp.float32)
    band = jnp.stack([cross[:, :, c, c + 1 : c + 1 + kept] for c in range(block)])
    band = band.transpose(3, 0, 2, 1) * (1.0 / math.sqrt(seg_count * windows_count))
    band = band.reshape(kept, block * 2 * bins_each)
    if kept < BAND:
        band = jnp.concatenate([band, jnp.zeros((BAND - kept, band.shape[1]), band.dtype)], axis=0)
    band = band.reshape(seg_count, per_owner, band.shape[1])

    collected = [lax.dynamic_index_in_dim(band, me, 0, keepdims=False)]
    for step in range(1, seg_count):
        sent = lax.dynamic_index_in_dim(band, (me + step) % seg_count, 0, keepdims=False)
        pairs = [(i, (i + step) % seg_count) for i in range(seg_count) if (i + step) % seg_count < live_owners]
        if pairs:
            collected.append(lax.ppermute(sent, "seg", pairs))
        else:
            collected.append(jnp.zeros_like(sent))
    collected = jnp.stack(collected)
    holder = (me - jnp.arange(seg_count, dtype=jnp.int32)) % seg_count
    by_bins = jnp.take(collected, holder, axis=0).reshape(seg_count, per_owner, block, 2, bins_each)
    return by_bins.transpose(1, 2, 3, 0, 4).reshape(per_owner, block, 2 * NF)


def solution(mesh):
    placed = (P("seg", "fibre", None), P("seg", None), P("fibre"))
    return jax.shard_map(
        shards, mesh=mesh, in_specs=placed, out_specs=P("seg", "fibre", None), check_vma=False
    )
```

```python
import math

import jax
import jax.numpy as jnp
import ml_dtypes
import numpy as np
from jax import lax
from jax.experimental import pallas as pl
from jax.experimental.pallas import tpu as pltpu
from jax.sharding import PartitionSpec as P

NF = 64
NT = 3072
BIN0 = 32
BAND = 256
LANES = 128


def spectral_table():
    sample_idx = np.arange(NT, dtype=np.int64)
    bin_idx = BIN0 + np.arange(NF, dtype=np.int64)
    phase_int = sample_idx[:, None] * bin_idx[None, :] % NT
    angle_rad = np.float32(2.0 * math.pi / NT) * phase_int.astype(np.float32)
    angle = angle_rad.astype(np.float64)
    table = np.concatenate([np.cos(angle), -np.sin(angle)], axis=1)
    return table.astype(ml_dtypes.bfloat16)


def whiten_kernel(starts_ref, place_ref, live_ref, record_hbm, table_ref, near_ref, count_ref, *refs):
    *out_refs, chunks, moved_rows, sems = refs
    windows, channels, span = chunks.shape
    blocks = NT // LANES
    last = record_hbm.shape[1] - span
    shifts = []
    for w in range(windows):
        first = starts_ref[w]
        base = pl.multiple_of(jnp.minimum(first - first % LANES, last), LANES)
        pltpu.make_async_copy(record_hbm.at[:, pl.ds(base, span)], chunks.at[w], sems.at[w]).start()
        shifts.append(first - base)
    lane = lax.broadcasted_iota(jnp.int32, (channels, LANES), 1)
    for w in range(windows):
        pltpu.make_async_copy(record_hbm.at[:, pl.ds(0, span)], chunks.at[w], sems.at[w]).wait()
        shift = shifts[w]
        low = lane < LANES - shift
        rolled = [
            pltpu.roll(chunks[w, :, pl.ds(b * LANES, LANES)].astype(jnp.float32), (LANES - shift) % LANES, 1)
            for b in range(blocks + 1)
        ]
        for b in range(blocks):
            moved_rows[pl.ds(w * channels, channels), pl.ds(b * LANES, LANES)] = jnp.where(
                low, rolled[b], rolled[b + 1]
            ).astype(jnp.bfloat16)
    spectra = jnp.dot(moved_rows[...], table_ref[...], preferred_element_type=jnp.float32)
    power = spectra * spectra
    smooth = jnp.dot(
        power, near_ref[...], precision=lax.Precision.HIGHEST, preferred_element_type=jnp.float32
    ) / count_ref[...]
    water_level = jnp.sum(power, axis=-1, keepdims=True) / NF
    rows_of = lax.broadcasted_iota(jnp.int32, spectra.shape, 0) % channels
    live = jnp.zeros(spectra.shape, jnp.float32)
    for c in range(channels):
        live = jnp.where(rows_of == c, live_ref[c].astype(jnp.float32), live)
    gain_of = live / jnp.sqrt(smooth + 0.1 * water_level + 1e-06)
    whitened = spectra * gain_of
    groups = len(out_refs)
    _, lanes_out = out_refs[0].shape
    width = 2 * LANES // (2 * groups)
    per_vreg = LANES // width
    lane = lax.broadcasted_iota(jnp.int32, (channels, LANES), 1)
    for d in range(groups):
        g = (place_ref[0] + d) % groups
        for v in range(lanes_out // LANES):
            gathered = jnp.zeros((channels, LANES), jnp.float32)
            for slot in range(per_vreg):
                w = v * per_vreg + slot
                piece = whitened[w * channels : (w + 1) * channels]
                piece = pltpu.roll(piece, (slot - g) * width % LANES, 1)
                inside = (lane >= slot * width) & (lane < (slot + 1) * width)
                gathered = jnp.where(inside, piece, gathered)
            out_refs[d][:, pl.ds(v * LANES, LANES)] = gathered.astype(out_refs[d].dtype)


def whiten(record_rows, starts, live_mask, groups, place):
    channels, _ = record_rows.shape
    windows = starts.shape[0]
    per_group = NF // groups
    lane_group, lane_part, lane_bin = np.unravel_index(np.arange(2 * NF), (groups, 2, per_group))
    lane_bin = lane_group * per_group + lane_bin
    table = jnp.asarray(spectral_table()[:, lane_part * NF + lane_bin])
    near = (np.abs(lane_bin[:, None] - lane_bin[None, :]) <= 4).astype(np.float32)
    count = (np.abs(np.arange(NF)[:, None] - lane_bin[None, :]) <= 4).sum(axis=0, keepdims=True).astype(np.float32)
    vmem = pl.BlockSpec(memory_space=pltpu.VMEM)
    smem = pl.BlockSpec(memory_space=pltpu.SMEM)
    return pl.pallas_call(
        whiten_kernel,
        out_shape=[jax.ShapeDtypeStruct((channels, windows * 2 * per_group), jnp.bfloat16)] * groups,
        in_specs=[smem, smem, smem, pl.BlockSpec(memory_space=pl.ANY), vmem, vmem, vmem],
        out_specs=[vmem] * groups,
        scratch_shapes=[
            pltpu.VMEM((windows, channels, NT + LANES), jnp.bfloat16),
            pltpu.VMEM((windows * channels, NT), jnp.bfloat16),
            pltpu.SemaphoreType.DMA((windows,)),
        ],
    )(starts, place.reshape(1), live_mask, record_rows, table, jnp.asarray(near), jnp.asarray(count))


def halo(mine, hops, fibre_count):
    if fibre_count % 2:
        columns = [mine]
        for step in range(1, hops + 1):
            pairs = [(i, i - step) for i in range(step, fibre_count)]
            columns.append(lax.ppermute(mine, "fibre", pairs))
        return jnp.concatenate(columns, axis=0)
    strides = min(-(-hops // 2), (fibre_count - 1) // 2)
    own = [mine]
    for step in range(1, strides + 1):
        pairs = [(i, i - 2 * step) for i in range(2 * step, fibre_count)]
        own.append(lax.ppermute(mine, "fibre", pairs))
    swapped = lax.ppermute(jnp.concatenate(own, axis=0), "fibre", [(i, i ^ 1) for i in range(fibre_count)])
    swapped = jnp.split(swapped, strides + 1, axis=0)
    even = [part for pair in zip(own, swapped) for part in pair]
    odd = [part for pair in zip(own, swapped[1:] + [jnp.zeros_like(mine)]) for part in pair]
    odd_side = lax.axis_index("fibre") % 2 == 1
    return jnp.where(odd_side, jnp.concatenate(odd, axis=0), jnp.concatenate(even, axis=0))


def shards(record, offsets, live_mask):
    seg_count = lax.axis_size("seg")
    fibre_count = lax.axis_size("fibre")
    windows_count = offsets.shape[1]
    block = record.shape[1]
    channels = block * fibre_count
    per_owner = BAND // seg_count
    bins_each = NF // seg_count
    live_offsets = min(BAND, channels - 1)
    live_owners = -(-live_offsets // per_owner)
    kept = live_owners * per_owner
    span = block + kept
    hops = min(-(-span // block) - 1, fibre_count - 1)
    me = lax.axis_index("seg")
    rows = seg_count * windows_count
    split = whiten(record[0], offsets[0], live_mask, seg_count, jnp.zeros((), jnp.int32))

    arrived = lax.all_to_all(jnp.stack(split), "seg", 0, 0, tiled=False)
    mine = arrived.transpose(1, 0, 2).reshape(block, -1)

    columns = halo(mine, hops, fibre_count)[:span]
    if columns.shape[0] < span:
        columns = jnp.concatenate(
            [columns, jnp.zeros((span - columns.shape[0], columns.shape[1]), columns.dtype)], axis=0
        )
    right = columns.reshape(span, rows, 2, bins_each)
    re_own = right[:block, :, 0]
    im_own = right[:block, :, 1]
    left = jnp.stack([jnp.stack([re_own, im_own], axis=2), jnp.stack([im_own, -re_own], axis=2)])
    cross = jnp.einsum("ocspn,jspn->nocj", left, right, preferred_element_type=jnp.float32)
    band = jnp.stack([cross[:, :, c, c + 1 : c + 1 + kept] for c in range(block)])
    band = band.transpose(3, 0, 2, 1) * (1.0 / math.sqrt(seg_count * windows_count))
    band = band.reshape(kept, block * 2 * bins_each)
    if kept < BAND:
        band = jnp.concatenate([band, jnp.zeros((BAND - kept, band.shape[1]), band.dtype)], axis=0)
    band = band.reshape(seg_count, per_owner, band.shape[1])

    collected = [lax.dynamic_index_in_dim(band, me, 0, keepdims=False)]
    for step in range(1, seg_count):
        sent = lax.dynamic_index_in_dim(band, (me + step) % seg_count, 0, keepdims=False)
        pairs = [(i, (i + step) % seg_count) for i in range(seg_count) if (i + step) % seg_count < live_owners]
        if pairs:
            collected.append(lax.ppermute(sent, "seg", pairs))
        else:
            collected.append(jnp.zeros_like(sent))
    collected = jnp.stack(collected)
    holder = (me - jnp.arange(seg_count, dtype=jnp.int32)) % seg_count
    by_bins = jnp.take(collected, holder, axis=0).reshape(seg_count, per_owner, block, 2, bins_each)
    return by_bins.transpose(1, 2, 3, 0, 4).reshape(per_owner, block, 2 * NF)


def solution(mesh):
    placed = (P("seg", "fibre", None), P("seg", None), P("fibre"))
    return jax.shard_map(
        shards, mesh=mesh, in_specs=placed, out_specs=P("seg", "fibre", None), check_vma=False
    )
```

```python
import math

import jax
import jax.numpy as jnp
import ml_dtypes
import numpy as np
from jax import lax
from jax.experimental import pallas as pl
from jax.experimental.pallas import tpu as pltpu
from jax.sharding import PartitionSpec as P

NF = 64
NT = 3072
BIN0 = 32
BAND = 256
LANES = 128


def spectral_table():
    sample_idx = np.arange(NT, dtype=np.int64)
    bin_idx = BIN0 + np.arange(NF, dtype=np.int64)
    phase_int = sample_idx[:, None] * bin_idx[None, :] % NT
    angle_rad = np.float32(2.0 * math.pi / NT) * phase_int.astype(np.float32)
    angle = angle_rad.astype(np.float64)
    table = np.concatenate([np.cos(angle), -np.sin(angle)], axis=1)
    return table.astype(ml_dtypes.bfloat16)


def whiten_kernel(starts_ref, place_ref, live_ref, record_hbm, table_ref, near_ref, count_ref, *refs):
    *out_refs, chunks, moved_rows, sems = refs
    windows, channels, span = chunks.shape
    blocks = NT // LANES
    last = record_hbm.shape[1] - span
    shifts = []
    for w in range(windows):
        first = starts_ref[w]
        base = pl.multiple_of(jnp.minimum(first - first % LANES, last), LANES)
        pltpu.make_async_copy(record_hbm.at[:, pl.ds(base, span)], chunks.at[w], sems.at[w]).start()
        shifts.append(first - base)
    lane = lax.broadcasted_iota(jnp.int32, (channels, LANES), 1)
    for w in range(windows):
        pltpu.make_async_copy(record_hbm.at[:, pl.ds(0, span)], chunks.at[w], sems.at[w]).wait()
        shift = shifts[w]
        low = lane < LANES - shift
        rolled = [
            pltpu.roll(chunks[w, :, pl.ds(b * LANES, LANES)].astype(jnp.float32), (LANES - shift) % LANES, 1)
            for b in range(blocks + 1)
        ]
        for b in range(blocks):
            moved_rows[pl.ds(w * channels, channels), pl.ds(b * LANES, LANES)] = jnp.where(
                low, rolled[b], rolled[b + 1]
            ).astype(jnp.bfloat16)
    spectra = jnp.dot(moved_rows[...], table_ref[...], preferred_element_type=jnp.float32)
    power = spectra * spectra
    smooth = jnp.dot(
        power, near_ref[...], precision=lax.Precision.HIGHEST, preferred_element_type=jnp.float32
    ) / count_ref[...]
    water_level = jnp.sum(power, axis=-1, keepdims=True) / NF
    rows_of = lax.broadcasted_iota(jnp.int32, spectra.shape, 0) % channels
    live = jnp.zeros(spectra.shape, jnp.float32)
    for c in range(channels):
        live = jnp.where(rows_of == c, live_ref[c].astype(jnp.float32), live)
    gain_of = live / jnp.sqrt(smooth + 0.1 * water_level + 1e-06)
    whitened = spectra * gain_of
    groups = len(out_refs)
    _, lanes_out = out_refs[0].shape
    width = 2 * LANES // (2 * groups)
    per_vreg = LANES // width
    lane = lax.broadcasted_iota(jnp.int32, (channels, LANES), 1)
    for d in range(groups):
        g = (place_ref[0] + d) % groups
        for v in range(lanes_out // LANES):
            gathered = jnp.zeros((channels, LANES), jnp.float32)
            for slot in range(per_vreg):
                w = v * per_vreg + slot
                piece = whitened[w * channels : (w + 1) * channels]
                piece = pltpu.roll(piece, (slot - g) * width % LANES, 1)
                inside = (lane >= slot * width) & (lane < (slot + 1) * width)
                gathered = jnp.where(inside, piece, gathered)
            out_refs[d][:, pl.ds(v * LANES, LANES)] = gathered.astype(out_refs[d].dtype)


def whiten(record_rows, starts, live_mask, groups, place):
    channels, _ = record_rows.shape
    windows = starts.shape[0]
    per_group = NF // groups
    lane_group, lane_part, lane_bin = np.unravel_index(np.arange(2 * NF), (groups, 2, per_group))
    lane_bin = lane_group * per_group + lane_bin
    table = jnp.asarray(spectral_table()[:, lane_part * NF + lane_bin])
    near = (np.abs(lane_bin[:, None] - lane_bin[None, :]) <= 4).astype(np.float32)
    count = (np.abs(np.arange(NF)[:, None] - lane_bin[None, :]) <= 4).sum(axis=0, keepdims=True).astype(np.float32)
    vmem = pl.BlockSpec(memory_space=pltpu.VMEM)
    smem = pl.BlockSpec(memory_space=pltpu.SMEM)
    return pl.pallas_call(
        whiten_kernel,
        out_shape=[jax.ShapeDtypeStruct((channels, windows * 2 * per_group), jnp.bfloat16)] * groups,
        in_specs=[smem, smem, smem, pl.BlockSpec(memory_space=pl.ANY), vmem, vmem, vmem],
        out_specs=[vmem] * groups,
        scratch_shapes=[
            pltpu.VMEM((windows, channels, NT + LANES), jnp.bfloat16),
            pltpu.VMEM((windows * channels, NT), jnp.bfloat16),
            pltpu.SemaphoreType.DMA((windows,)),
        ],
    )(starts, place.reshape(1), live_mask, record_rows, table, jnp.asarray(near), jnp.asarray(count))


def halo(mine, hops, fibre_count):
    if fibre_count % 2:
        columns = [mine]
        for step in range(1, hops + 1):
            pairs = [(i, i - step) for i in range(step, fibre_count)]
            columns.append(lax.ppermute(mine, "fibre", pairs))
        return jnp.concatenate(columns, axis=0)
    strides = min(-(-hops // 2), (fibre_count - 1) // 2)
    own = [mine]
    for step in range(1, strides + 1):
        pairs = [(i, i - 2 * step) for i in range(2 * step, fibre_count)]
        own.append(lax.ppermute(mine, "fibre", pairs))
    swapped = lax.ppermute(jnp.concatenate(own, axis=0), "fibre", [(i, i ^ 1) for i in range(fibre_count)])
    swapped = jnp.split(swapped, strides + 1, axis=0)
    even = [part for pair in zip(own, swapped) for part in pair]
    odd = [part for pair in zip(own, swapped[1:] + [jnp.zeros_like(mine)]) for part in pair]
    odd_side = lax.axis_index("fibre") % 2 == 1
    return jnp.where(odd_side, jnp.concatenate(odd, axis=0), jnp.concatenate(even, axis=0))


def shards(record, offsets, live_mask):
    seg_count = lax.axis_size("seg")
    fibre_count = lax.axis_size("fibre")
    windows_count = offsets.shape[1]
    block = record.shape[1]
    channels = block * fibre_count
    per_owner = BAND // seg_count
    bins_each = NF // seg_count
    live_offsets = min(BAND, channels - 1)
    live_owners = -(-live_offsets // per_owner)
    kept = live_owners * per_owner
    span = block + kept
    hops = min(-(-span // block) - 1, fibre_count - 1)
    me = lax.axis_index("seg")
    rows = seg_count * windows_count
    split = whiten(record[0], offsets[0], live_mask, seg_count, me.astype(jnp.int32))

    gathered = [split[0]]
    for step in range(1, seg_count):
        pairs = [(i, (i + step) % seg_count) for i in range(seg_count)]
        gathered.append(lax.ppermute(split[step], "seg", pairs))
    mine = jnp.concatenate(gathered, axis=1)

    columns = halo(mine, hops, fibre_count)[:span]
    if columns.shape[0] < span:
        columns = jnp.concatenate(
            [columns, jnp.zeros((span - columns.shape[0], columns.shape[1]), columns.dtype)], axis=0
        )
    right = columns.reshape(span, rows, 2, bins_each)
    own = mine.reshape(block, rows, 2, bins_each)
    re_own = own[:, :, 0]
    im_own = own[:, :, 1]
    left = jnp.stack([jnp.stack([re_own, im_own], axis=2), jnp.stack([im_own, -re_own], axis=2)])
    cross = jnp.einsum("ocspn,jspn->nocj", left, right, preferred_element_type=jnp.float32)
    band = jnp.stack([cross[:, :, c, c + 1 : c + 1 + kept] for c in range(block)])
    band = band.transpose(3, 0, 2, 1) * (1.0 / math.sqrt(seg_count * windows_count))
    band = band.reshape(kept, block * 2 * bins_each)
    if kept < BAND:
        band = jnp.concatenate([band, jnp.zeros((BAND - kept, band.shape[1]), band.dtype)], axis=0)
    band = band.reshape(seg_count, per_owner, band.shape[1])

    collected = [lax.dynamic_index_in_dim(band, me, 0, keepdims=False)]
    for step in range(1, seg_count):
        sent = lax.dynamic_index_in_dim(band, (me + step) % seg_count, 0, keepdims=False)
        pairs = [(i, (i + step) % seg_count) for i in range(seg_count) if (i + step) % seg_count < live_owners]
        if pairs:
            collected.append(lax.ppermute(sent, "seg", pairs))
        else:
            collected.append(jnp.zeros_like(sent))
    collected = jnp.stack(collected)
    holder = (me - jnp.arange(seg_count, dtype=jnp.int32)) % seg_count
    by_bins = jnp.take(collected, holder, axis=0).reshape(seg_count, per_owner, block, 2, bins_each)
    return by_bins.transpose(1, 2, 3, 0, 4).reshape(per_owner, block, 2 * NF)


def solution(mesh):
    placed = (P("seg", "fibre", None), P("seg", None), P("fibre"))
    return jax.shard_map(
        shards, mesh=mesh, in_specs=placed, out_specs=P("seg", "fibre", None), check_vma=False
    )
```

```python
import math

import jax
import jax.numpy as jnp
import ml_dtypes
import numpy as np
from jax import lax
from jax.experimental import pallas as pl
from jax.experimental.pallas import tpu as pltpu
from jax.sharding import PartitionSpec as P

NF = 64
NT = 3072
BIN0 = 32
BAND = 256
LANES = 128


def spectral_table():
    sample_idx = np.arange(NT, dtype=np.int64)
    bin_idx = BIN0 + np.arange(NF, dtype=np.int64)
    phase_int = sample_idx[:, None] * bin_idx[None, :] % NT
    angle_rad = np.float32(2.0 * math.pi / NT) * phase_int.astype(np.float32)
    angle = angle_rad.astype(np.float64)
    table = np.concatenate([np.cos(angle), -np.sin(angle)], axis=1)
    return table.astype(ml_dtypes.bfloat16)


def whiten_kernel(starts_ref, place_ref, live_ref, record_hbm, table_ref, near_ref, count_ref, *refs):
    *out_refs, chunks, moved_rows, sems = refs
    windows, channels, span = chunks.shape
    blocks = NT // LANES
    last = record_hbm.shape[1] - span
    shifts = []
    for w in range(windows):
        first = starts_ref[w]
        base = pl.multiple_of(jnp.minimum(first - first % LANES, last), LANES)
        pltpu.make_async_copy(record_hbm.at[:, pl.ds(base, span)], chunks.at[w], sems.at[w]).start()
        shifts.append(first - base)
    lane = lax.broadcasted_iota(jnp.int32, (channels, LANES), 1)
    for w in range(windows):
        pltpu.make_async_copy(record_hbm.at[:, pl.ds(0, span)], chunks.at[w], sems.at[w]).wait()
        shift = shifts[w]
        low = lane < LANES - shift
        rolled = [
            pltpu.roll(chunks[w, :, pl.ds(b * LANES, LANES)].astype(jnp.float32), (LANES - shift) % LANES, 1)
            for b in range(blocks + 1)
        ]
        for b in range(blocks):
            moved_rows[pl.ds(w * channels, channels), pl.ds(b * LANES, LANES)] = jnp.where(
                low, rolled[b], rolled[b + 1]
            ).astype(jnp.bfloat16)
    spectra = jnp.dot(moved_rows[...], table_ref[...], preferred_element_type=jnp.float32)
    power = spectra * spectra
    smooth = jnp.dot(
        power, near_ref[...], precision=lax.Precision.HIGHEST, preferred_element_type=jnp.float32
    ) / count_ref[...]
    water_level = jnp.sum(power, axis=-1, keepdims=True) / NF
    rows_of = lax.broadcasted_iota(jnp.int32, spectra.shape, 0) % channels
    live = jnp.zeros(spectra.shape, jnp.float32)
    for c in range(channels):
        live = jnp.where(rows_of == c, live_ref[c].astype(jnp.float32), live)
    gain_of = live / jnp.sqrt(smooth + 0.1 * water_level + 1e-06)
    whitened = spectra * gain_of
    groups = len(out_refs)
    _, lanes_out = out_refs[0].shape
    width = 2 * LANES // (2 * groups)
    per_vreg = LANES // width
    lane = lax.broadcasted_iota(jnp.int32, (channels, LANES), 1)
    for d in range(groups):
        g = (place_ref[0] + d) % groups
        for v in range(lanes_out // LANES):
            gathered = jnp.zeros((channels, LANES), jnp.float32)
            for slot in range(per_vreg):
                w = v * per_vreg + slot
                piece = whitened[w * channels : (w + 1) * channels]
                piece = pltpu.roll(piece, (slot - g) * width % LANES, 1)
                inside = (lane >= slot * width) & (lane < (slot + 1) * width)
                gathered = jnp.where(inside, piece, gathered)
            out_refs[d][:, pl.ds(v * LANES, LANES)] = gathered.astype(out_refs[d].dtype)


def whiten(record_rows, starts, live_mask, groups, place):
    channels, _ = record_rows.shape
    windows = starts.shape[0]
    per_group = NF // groups
    lane_group, lane_part, lane_bin = np.unravel_index(np.arange(2 * NF), (groups, 2, per_group))
    lane_bin = lane_group * per_group + lane_bin
    table = jnp.asarray(spectral_table()[:, lane_part * NF + lane_bin])
    near = (np.abs(lane_bin[:, None] - lane_bin[None, :]) <= 4).astype(np.float32)
    count = (np.abs(np.arange(NF)[:, None] - lane_bin[None, :]) <= 4).sum(axis=0, keepdims=True).astype(np.float32)
    vmem = pl.BlockSpec(memory_space=pltpu.VMEM)
    smem = pl.BlockSpec(memory_space=pltpu.SMEM)
    return pl.pallas_call(
        whiten_kernel,
        out_shape=[jax.ShapeDtypeStruct((channels, windows * 2 * per_group), jnp.bfloat16)] * groups,
        in_specs=[smem, smem, smem, pl.BlockSpec(memory_space=pl.ANY), vmem, vmem, vmem],
        out_specs=[vmem] * groups,
        scratch_shapes=[
            pltpu.VMEM((windows, channels, NT + LANES), jnp.bfloat16),
            pltpu.VMEM((windows * channels, NT), jnp.bfloat16),
            pltpu.SemaphoreType.DMA((windows,)),
        ],
    )(starts, place.reshape(1), live_mask, record_rows, table, jnp.asarray(near), jnp.asarray(count))


def halo(mine, hops, fibre_count):
    if fibre_count % 2:
        columns = [mine]
        for step in range(1, hops + 1):
            pairs = [(i, i - step) for i in range(step, fibre_count)]
            columns.append(lax.ppermute(mine, "fibre", pairs))
        return jnp.concatenate(columns, axis=0)
    strides = min(-(-hops // 2), (fibre_count - 1) // 2)
    own = [mine]
    for step in range(1, strides + 1):
        pairs = [(i, i - 2 * step) for i in range(2 * step, fibre_count)]
        own.append(lax.ppermute(mine, "fibre", pairs))
    swapped = lax.ppermute(jnp.concatenate(own, axis=0), "fibre", [(i, i ^ 1) for i in range(fibre_count)])
    swapped = jnp.split(swapped, strides + 1, axis=0)
    even = [part for pair in zip(own, swapped) for part in pair]
    odd = [part for pair in zip(own, swapped[1:] + [jnp.zeros_like(mine)]) for part in pair]
    odd_side = lax.axis_index("fibre") % 2 == 1
    return jnp.where(odd_side, jnp.concatenate(odd, axis=0), jnp.concatenate(even, axis=0))


def shards(record, offsets, live_mask):
    seg_count = lax.axis_size("seg")
    fibre_count = lax.axis_size("fibre")
    windows_count = offsets.shape[1]
    block = record.shape[1]
    channels = block * fibre_count
    per_owner = BAND // seg_count
    bins_each = NF // seg_count
    live_offsets = min(BAND, channels - 1)
    live_owners = -(-live_offsets // per_owner)
    kept = live_owners * per_owner
    span = block + kept
    hops = min(-(-span // block) - 1, fibre_count - 1)
    me = lax.axis_index("seg")
    rows = seg_count * windows_count
    split = whiten(record[0], offsets[0], live_mask, seg_count, me.astype(jnp.int32))

    gathered = [split[0]]
    for step in range(1, seg_count):
        pairs = [(i, (i + step) % seg_count) for i in range(seg_count)]
        gathered.append(lax.ppermute(split[step], "seg", pairs))
    mine = jnp.concatenate(gathered, axis=1)

    columns = halo(mine, hops, fibre_count)[:span]
    if columns.shape[0] < span:
        columns = jnp.concatenate(
            [columns, jnp.zeros((span - columns.shape[0], columns.shape[1]), columns.dtype)], axis=0
        )
    right = columns.reshape(span, rows, 2, bins_each)
    own = right[:block]
    sign = jnp.asarray([1.0, -1.0], own.dtype)[None, None, :, None]
    turned = jnp.flip(own, axis=2) * sign
    left = jnp.stack([own, turned])
    cross = jnp.einsum("ocspn,jspn->nocj", left, right, preferred_element_type=jnp.float32)
    band = jnp.stack([cross[:, :, c, c + 1 : c + 1 + kept] for c in range(block)])
    band = band.transpose(3, 0, 2, 1) * (1.0 / math.sqrt(seg_count * windows_count))
    band = band.reshape(kept, block * 2 * bins_each)
    if kept < BAND:
        band = jnp.concatenate([band, jnp.zeros((BAND - kept, band.shape[1]), band.dtype)], axis=0)
    band = band.reshape(seg_count, per_owner, band.shape[1])

    collected = [lax.dynamic_index_in_dim(band, me, 0, keepdims=False)]
    for step in range(1, seg_count):
        sent = lax.dynamic_index_in_dim(band, (me + step) % seg_count, 0, keepdims=False)
        pairs = [(i, (i + step) % seg_count) for i in range(seg_count) if (i + step) % seg_count < live_owners]
        if pairs:
            collected.append(lax.ppermute(sent, "seg", pairs))
        else:
            collected.append(jnp.zeros_like(sent))
    collected = jnp.stack(collected)
    holder = (me - jnp.arange(seg_count, dtype=jnp.int32)) % seg_count
    by_bins = jnp.take(collected, holder, axis=0).reshape(seg_count, per_owner, block, 2, bins_each)
    return by_bins.transpose(1, 2, 3, 0, 4).reshape(per_owner, block, 2 * NF)


def solution(mesh):
    placed = (P("seg", "fibre", None), P("seg", None), P("fibre"))
    return jax.shard_map(
        shards, mesh=mesh, in_specs=placed, out_specs=P("seg", "fibre", None), check_vma=False
    )
```

```python
import math

import jax
import jax.numpy as jnp
import ml_dtypes
import numpy as np
from jax import lax
from jax.experimental import pallas as pl
from jax.experimental.pallas import tpu as pltpu
from jax.sharding import PartitionSpec as P

NF = 64
NT = 3072
BIN0 = 32
BAND = 256
LANES = 128


def spectral_table():
    sample_idx = np.arange(NT, dtype=np.int64)
    bin_idx = BIN0 + np.arange(NF, dtype=np.int64)
    phase_int = sample_idx[:, None] * bin_idx[None, :] % NT
    angle_rad = np.float32(2.0 * math.pi / NT) * phase_int.astype(np.float32)
    angle = angle_rad.astype(np.float64)
    table = np.concatenate([np.cos(angle), -np.sin(angle)], axis=1)
    return table.astype(ml_dtypes.bfloat16)


def whiten_kernel(starts_ref, place_ref, live_ref, record_hbm, table_ref, near_ref, count_ref, *refs):
    *out_refs, chunks, moved_rows, sems = refs
    windows, channels, span = chunks.shape
    blocks = NT // LANES
    last = record_hbm.shape[1] - span
    shifts = []
    for w in range(windows):
        first = starts_ref[w]
        base = pl.multiple_of(jnp.minimum(first - first % LANES, last), LANES)
        pltpu.make_async_copy(record_hbm.at[:, pl.ds(base, span)], chunks.at[w], sems.at[w]).start()
        shifts.append(first - base)
    lane = lax.broadcasted_iota(jnp.int32, (channels, LANES), 1)
    for w in range(windows):
        pltpu.make_async_copy(record_hbm.at[:, pl.ds(0, span)], chunks.at[w], sems.at[w]).wait()
        shift = shifts[w]
        low = lane < LANES - shift
        rolled = [
            pltpu.roll(chunks[w, :, pl.ds(b * LANES, LANES)].astype(jnp.float32), (LANES - shift) % LANES, 1)
            for b in range(blocks + 1)
        ]
        for b in range(blocks):
            moved_rows[pl.ds(w * channels, channels), pl.ds(b * LANES, LANES)] = jnp.where(
                low, rolled[b], rolled[b + 1]
            ).astype(jnp.bfloat16)
    spectra = jnp.dot(moved_rows[...], table_ref[...], preferred_element_type=jnp.float32)
    power = spectra * spectra
    smooth = jnp.dot(
        power, near_ref[...], precision=lax.Precision.HIGHEST, preferred_element_type=jnp.float32
    ) / count_ref[...]
    water_level = jnp.sum(power, axis=-1, keepdims=True) / NF
    rows_of = lax.broadcasted_iota(jnp.int32, spectra.shape, 0) % channels
    live = jnp.zeros(spectra.shape, jnp.float32)
    for c in range(channels):
        live = jnp.where(rows_of == c, live_ref[c].astype(jnp.float32), live)
    gain_of = live / jnp.sqrt(smooth + 0.1 * water_level + 1e-06)
    whitened = spectra * gain_of
    groups = len(out_refs)
    _, lanes_out = out_refs[0].shape
    width = 2 * LANES // (2 * groups)
    per_vreg = LANES // width
    lane = lax.broadcasted_iota(jnp.int32, (channels, LANES), 1)
    for d in range(groups):
        g = (place_ref[0] + d) % groups
        for v in range(lanes_out // LANES):
            gathered = jnp.zeros((channels, LANES), jnp.float32)
            for slot in range(per_vreg):
                w = v * per_vreg + slot
                piece = whitened[w * channels : (w + 1) * channels]
                piece = pltpu.roll(piece, (slot - g) * width % LANES, 1)
                inside = (lane >= slot * width) & (lane < (slot + 1) * width)
                gathered = jnp.where(inside, piece, gathered)
            out_refs[d][:, pl.ds(v * LANES, LANES)] = gathered.astype(out_refs[d].dtype)


def whiten(record_rows, starts, live_mask, groups, place):
    channels, _ = record_rows.shape
    windows = starts.shape[0]
    per_group = NF // groups
    lane_group, lane_part, lane_bin = np.unravel_index(np.arange(2 * NF), (groups, 2, per_group))
    lane_bin = lane_group * per_group + lane_bin
    table = jnp.asarray(spectral_table()[:, lane_part * NF + lane_bin])
    near = (np.abs(lane_bin[:, None] - lane_bin[None, :]) <= 4).astype(np.float32)
    count = (np.abs(np.arange(NF)[:, None] - lane_bin[None, :]) <= 4).sum(axis=0, keepdims=True).astype(np.float32)
    vmem = pl.BlockSpec(memory_space=pltpu.VMEM)
    smem = pl.BlockSpec(memory_space=pltpu.SMEM)
    return pl.pallas_call(
        whiten_kernel,
        out_shape=[jax.ShapeDtypeStruct((channels, windows * 2 * per_group), jnp.bfloat16)] * groups,
        in_specs=[smem, smem, smem, pl.BlockSpec(memory_space=pl.ANY), vmem, vmem, vmem],
        out_specs=[vmem] * groups,
        scratch_shapes=[
            pltpu.VMEM((windows, channels, NT + LANES), jnp.bfloat16),
            pltpu.VMEM((windows * channels, NT), jnp.bfloat16),
            pltpu.SemaphoreType.DMA((windows,)),
        ],
    )(starts, place.reshape(1), live_mask, record_rows, table, jnp.asarray(near), jnp.asarray(count))


def halo(mine, hops, fibre_count):
    if fibre_count % 2:
        columns = [mine]
        for step in range(1, hops + 1):
            pairs = [(i, i - step) for i in range(step, fibre_count)]
            columns.append(lax.ppermute(mine, "fibre", pairs))
        return jnp.concatenate(columns, axis=0)
    strides = min(-(-hops // 2), (fibre_count - 1) // 2)
    own = [mine]
    for step in range(1, strides + 1):
        pairs = [(i, i - 2 * step) for i in range(2 * step, fibre_count)]
        own.append(lax.ppermute(mine, "fibre", pairs))
    swapped = lax.ppermute(jnp.concatenate(own, axis=0), "fibre", [(i, i ^ 1) for i in range(fibre_count)])
    swapped = jnp.split(swapped, strides + 1, axis=0)
    even = [part for pair in zip(own, swapped) for part in pair]
    odd = [part for pair in zip(own, swapped[1:] + [jnp.zeros_like(mine)]) for part in pair]
    odd_side = lax.axis_index("fibre") % 2 == 1
    return jnp.where(odd_side, jnp.concatenate(odd, axis=0), jnp.concatenate(even, axis=0))


def shards(record, offsets, live_mask):
    seg_count = lax.axis_size("seg")
    fibre_count = lax.axis_size("fibre")
    windows_count = offsets.shape[1]
    block = record.shape[1]
    channels = block * fibre_count
    per_owner = BAND // seg_count
    bins_each = NF // seg_count
    live_offsets = min(BAND, channels - 1)
    live_owners = -(-live_offsets // per_owner)
    kept = live_owners * per_owner
    span = block + kept
    hops = min(-(-span // block) - 1, fibre_count - 1)
    me = lax.axis_index("seg")
    rows = seg_count * windows_count
    split = whiten(record[0], offsets[0], live_mask, seg_count, me.astype(jnp.int32))

    gathered = [split[0]]
    for step in range(1, seg_count):
        pairs = [(i, (i + step) % seg_count) for i in range(seg_count)]
        gathered.append(lax.ppermute(split[step], "seg", pairs))
    mine = jnp.concatenate(gathered, axis=1)

    columns = halo(mine, hops, fibre_count)[:span]
    if columns.shape[0] < span:
        columns = jnp.concatenate(
            [columns, jnp.zeros((span - columns.shape[0], columns.shape[1]), columns.dtype)], axis=0
        )
    right = columns.reshape(span, rows, 2, bins_each)
    own = right[:block]
    sign = jnp.asarray([1.0, -1.0], own.dtype)[None, None, :, None]
    turned = jnp.flip(own, axis=2) * sign
    left = jnp.stack([own, turned])
    cross = jnp.einsum("ocspn,jspn->nocj", left, right, preferred_element_type=jnp.float32)
    band = jnp.stack([cross[:, :, c, c + 1 : c + 1 + kept] for c in range(block)])
    band = band.transpose(3, 0, 2, 1) * (1.0 / math.sqrt(seg_count * windows_count))
    band = band.reshape(kept, block * 2 * bins_each)
    if kept < BAND:
        band = jnp.concatenate([band, jnp.zeros((BAND - kept, band.shape[1]), band.dtype)], axis=0)
    band = band.reshape(seg_count, per_owner, band.shape[1])

    collected = [lax.dynamic_index_in_dim(band, me, 0, keepdims=False)]
    for step in range(1, seg_count):
        sent = lax.dynamic_index_in_dim(band, (me + step) % seg_count, 0, keepdims=False)
        pairs = [(i, (i + step) % seg_count) for i in range(seg_count) if (i + step) % seg_count < live_owners]
        if pairs:
            collected.append(lax.ppermute(sent, "seg", pairs))
        else:
            collected.append(jnp.zeros_like(sent))
    collected = jnp.stack(collected)
    turned_rows = jnp.concatenate([collected[:1], collected[1:][::-1]], axis=0)
    doubled = jnp.concatenate([turned_rows, turned_rows], axis=0)
    by_bins = lax.dynamic_slice_in_dim(doubled, (seg_count - me) % seg_count, seg_count, 0)
    by_bins = by_bins.reshape(seg_count, per_owner, block, 2, bins_each)
    return by_bins.transpose(1, 2, 3, 0, 4).reshape(per_owner, block, 2 * NF)


def solution(mesh):
    placed = (P("seg", "fibre", None), P("seg", None), P("fibre"))
    return jax.shard_map(
        shards, mesh=mesh, in_specs=placed, out_specs=P("seg", "fibre", None), check_vma=False
    )
```

```python
import math

import jax
import jax.numpy as jnp
import ml_dtypes
import numpy as np
from jax import lax
from jax.experimental import pallas as pl
from jax.experimental.pallas import tpu as pltpu
from jax.sharding import PartitionSpec as P

NF = 64
NT = 3072
BIN0 = 32
BAND = 256
LANES = 128


def spectral_table():
    sample_idx = np.arange(NT, dtype=np.int64)
    bin_idx = BIN0 + np.arange(NF, dtype=np.int64)
    phase_int = sample_idx[:, None] * bin_idx[None, :] % NT
    angle_rad = np.float32(2.0 * math.pi / NT) * phase_int.astype(np.float32)
    angle = angle_rad.astype(np.float64)
    table = np.concatenate([np.cos(angle), -np.sin(angle)], axis=1)
    return table.astype(ml_dtypes.bfloat16)


def whiten_kernel(starts_ref, place_ref, live_ref, record_hbm, table_ref, near_ref, count_ref, *refs):
    *out_refs, chunks, moved_rows, sems = refs
    windows, channels, span = chunks.shape
    blocks = NT // LANES
    last = record_hbm.shape[1] - span
    shifts = []
    for w in range(windows):
        first = starts_ref[w]
        base = pl.multiple_of(jnp.minimum(first - first % LANES, last), LANES)
        pltpu.make_async_copy(record_hbm.at[:, pl.ds(base, span)], chunks.at[w], sems.at[w]).start()
        shifts.append(first - base)
    lane = lax.broadcasted_iota(jnp.int32, (channels, LANES), 1)
    for w in range(windows):
        pltpu.make_async_copy(record_hbm.at[:, pl.ds(0, span)], chunks.at[w], sems.at[w]).wait()
        shift = shifts[w]
        low = lane < LANES - shift
        rolled = [
            pltpu.roll(chunks[w, :, pl.ds(b * LANES, LANES)].astype(jnp.float32), (LANES - shift) % LANES, 1)
            for b in range(blocks + 1)
        ]
        for b in range(blocks):
            moved_rows[pl.ds(w * channels, channels), pl.ds(b * LANES, LANES)] = jnp.where(
                low, rolled[b], rolled[b + 1]
            ).astype(jnp.bfloat16)
    spectra = jnp.dot(moved_rows[...], table_ref[...], preferred_element_type=jnp.float32)
    power = spectra * spectra
    smooth = jnp.dot(
        power, near_ref[...], precision=lax.Precision.HIGHEST, preferred_element_type=jnp.float32
    ) / count_ref[...]
    water_level = jnp.sum(power, axis=-1, keepdims=True) / NF
    rows_of = lax.broadcasted_iota(jnp.int32, spectra.shape, 0) % channels
    live = jnp.zeros(spectra.shape, jnp.float32)
    for c in range(channels):
        live = jnp.where(rows_of == c, live_ref[c].astype(jnp.float32), live)
    gain_of = live / jnp.sqrt(smooth + 0.1 * water_level + 1e-06)
    whitened = spectra * gain_of
    groups = len(out_refs)
    _, lanes_out = out_refs[0].shape
    width = 2 * LANES // (2 * groups)
    per_vreg = LANES // width
    lane = lax.broadcasted_iota(jnp.int32, (channels, LANES), 1)
    for d in range(groups):
        g = (place_ref[0] + d) % groups
        for v in range(lanes_out // LANES):
            gathered = jnp.zeros((channels, LANES), jnp.float32)
            for slot in range(per_vreg):
                w = v * per_vreg + slot
                piece = whitened[w * channels : (w + 1) * channels]
                piece = pltpu.roll(piece, (slot - g) * width % LANES, 1)
                inside = (lane >= slot * width) & (lane < (slot + 1) * width)
                gathered = jnp.where(inside, piece, gathered)
            out_refs[d][:, pl.ds(v * LANES, LANES)] = gathered.astype(out_refs[d].dtype)


def whiten(record_rows, starts, live_mask, groups, place):
    channels, _ = record_rows.shape
    windows = starts.shape[0]
    per_group = NF // groups
    lane_group, lane_part, lane_bin = np.unravel_index(np.arange(2 * NF), (groups, 2, per_group))
    lane_bin = lane_group * per_group + lane_bin
    table = jnp.asarray(spectral_table()[:, lane_part * NF + lane_bin])
    near = (np.abs(lane_bin[:, None] - lane_bin[None, :]) <= 4).astype(np.float32)
    count = (np.abs(np.arange(NF)[:, None] - lane_bin[None, :]) <= 4).sum(axis=0, keepdims=True).astype(np.float32)
    vmem = pl.BlockSpec(memory_space=pltpu.VMEM)
    smem = pl.BlockSpec(memory_space=pltpu.SMEM)
    return pl.pallas_call(
        whiten_kernel,
        out_shape=[jax.ShapeDtypeStruct((channels, windows * 2 * per_group), jnp.bfloat16)] * groups,
        in_specs=[smem, smem, smem, pl.BlockSpec(memory_space=pl.ANY), vmem, vmem, vmem],
        out_specs=[vmem] * groups,
        scratch_shapes=[
            pltpu.VMEM((windows, channels, NT + LANES), jnp.bfloat16),
            pltpu.VMEM((windows * channels, NT), jnp.bfloat16),
            pltpu.SemaphoreType.DMA((windows,)),
        ],
    )(starts, place.reshape(1), live_mask, record_rows, table, jnp.asarray(near), jnp.asarray(count))


def halo(mine, hops, fibre_count):
    if fibre_count % 2:
        columns = [mine]
        for step in range(1, hops + 1):
            pairs = [(i, i - step) for i in range(step, fibre_count)]
            columns.append(lax.ppermute(mine, "fibre", pairs))
        return jnp.concatenate(columns, axis=0)
    strides = min(-(-hops // 2), (fibre_count - 1) // 2)
    own = [mine]
    for step in range(1, strides + 1):
        pairs = [(i, i - 2 * step) for i in range(2 * step, fibre_count)]
        own.append(lax.ppermute(mine, "fibre", pairs))
    swapped = lax.ppermute(jnp.concatenate(own, axis=0), "fibre", [(i, i ^ 1) for i in range(fibre_count)])
    swapped = jnp.split(swapped, strides + 1, axis=0)
    even = [part for pair in zip(own, swapped) for part in pair]
    odd = [part for pair in zip(own, swapped[1:] + [jnp.zeros_like(mine)]) for part in pair]
    odd_side = lax.axis_index("fibre") % 2 == 1
    return jnp.where(odd_side, jnp.concatenate(odd, axis=0), jnp.concatenate(even, axis=0))


def shards(record, offsets, live_mask):
    seg_count = lax.axis_size("seg")
    fibre_count = lax.axis_size("fibre")
    windows_count = offsets.shape[1]
    block = record.shape[1]
    channels = block * fibre_count
    per_owner = BAND // seg_count
    bins_each = NF // seg_count
    live_offsets = min(BAND, channels - 1)
    live_owners = -(-live_offsets // per_owner)
    kept = live_owners * per_owner
    span = block + kept
    hops = min(-(-span // block) - 1, fibre_count - 1)
    me = lax.axis_index("seg")
    rows = seg_count * windows_count
    split = whiten(record[0], offsets[0], live_mask, seg_count, me.astype(jnp.int32))

    gathered = [split[0]]
    for step in range(1, seg_count):
        pairs = [(i, (i + step) % seg_count) for i in range(seg_count)]
        gathered.append(lax.ppermute(split[step], "seg", pairs))
    mine = jnp.concatenate(gathered, axis=1)

    columns = halo(mine, hops, fibre_count)[:span]
    if columns.shape[0] < span:
        columns = jnp.concatenate(
            [columns, jnp.zeros((span - columns.shape[0], columns.shape[1]), columns.dtype)], axis=0
        )
    right = columns.reshape(span, rows, 2, bins_each)
    own = right[:block]
    sign = jnp.asarray([1.0, -1.0], own.dtype)[None, None, :, None]
    turned = jnp.flip(own, axis=2) * sign
    left = jnp.stack([own, turned])
    cross = jnp.einsum("ocspn,jspn->nocj", left, right, preferred_element_type=jnp.float32)
    band = jnp.stack([cross[:, :, c, c + 1 : c + 1 + kept] for c in range(block)])
    band = band.transpose(3, 0, 2, 1) * (1.0 / math.sqrt(seg_count * windows_count))
    band = band.reshape(kept, block * 2 * bins_each)
    if kept < BAND:
        band = jnp.concatenate([band, jnp.zeros((BAND - kept, band.shape[1]), band.dtype)], axis=0)
    band = band.reshape(seg_count, per_owner, band.shape[1])

    collected = [lax.dynamic_index_in_dim(band, me, 0, keepdims=False)]
    for step in range(1, seg_count):
        sent = lax.dynamic_index_in_dim(band, (me + step) % seg_count, 0, keepdims=False)
        pairs = [(i, (i + step) % seg_count) for i in range(seg_count) if (i + step) % seg_count < live_owners]
        if pairs:
            collected.append(lax.ppermute(sent, "seg", pairs))
        else:
            collected.append(jnp.zeros_like(sent))
    collected = jnp.stack(collected)
    turned_rows = jnp.concatenate([collected[:1], collected[1:][::-1]], axis=0)
    doubled = jnp.concatenate([turned_rows, turned_rows], axis=0)
    doubled = doubled.reshape(2 * seg_count, per_owner, block, 2, bins_each)
    start = (seg_count - me) % seg_count
    by_bins = [lax.dynamic_index_in_dim(doubled, start + b, 0, keepdims=False) for b in range(seg_count)]
    return jnp.stack(by_bins, axis=3).reshape(per_owner, block, 2 * NF)


def solution(mesh):
    placed = (P("seg", "fibre", None), P("seg", None), P("fibre"))
    return jax.shard_map(
        shards, mesh=mesh, in_specs=placed, out_specs=P("seg", "fibre", None), check_vma=False
    )
```

```python
import math

import jax
import jax.numpy as jnp
import ml_dtypes
import numpy as np
from jax import lax
from jax.experimental import pallas as pl
from jax.experimental.pallas import tpu as pltpu
from jax.sharding import PartitionSpec as P

NF = 64
NT = 3072
BIN0 = 32
BAND = 256
LANES = 128


def spectral_table():
    sample_idx = np.arange(NT, dtype=np.int64)
    bin_idx = BIN0 + np.arange(NF, dtype=np.int64)
    phase_int = sample_idx[:, None] * bin_idx[None, :] % NT
    angle_rad = np.float32(2.0 * math.pi / NT) * phase_int.astype(np.float32)
    angle = angle_rad.astype(np.float64)
    table = np.concatenate([np.cos(angle), -np.sin(angle)], axis=1)
    return table.astype(ml_dtypes.bfloat16)


def whiten_kernel(starts_ref, place_ref, live_ref, record_hbm, table_ref, near_ref, count_ref, *refs):
    *out_refs, chunks, moved_rows, sems = refs
    windows, channels, span = chunks.shape
    blocks = NT // LANES
    last = record_hbm.shape[1] - span
    shifts = []
    for w in range(windows):
        first = starts_ref[w]
        base = pl.multiple_of(jnp.minimum(first - first % LANES, last), LANES)
        pltpu.make_async_copy(record_hbm.at[:, pl.ds(base, span)], chunks.at[w], sems.at[w]).start()
        shifts.append(first - base)
    lane = lax.broadcasted_iota(jnp.int32, (channels, LANES), 1)
    for w in range(windows):
        pltpu.make_async_copy(record_hbm.at[:, pl.ds(0, span)], chunks.at[w], sems.at[w]).wait()
        shift = shifts[w]
        low = lane < LANES - shift
        rolled = [
            pltpu.roll(chunks[w, :, pl.ds(b * LANES, LANES)].astype(jnp.float32), (LANES - shift) % LANES, 1)
            for b in range(blocks + 1)
        ]
        for b in range(blocks):
            moved_rows[pl.ds(w * channels, channels), pl.ds(b * LANES, LANES)] = jnp.where(
                low, rolled[b], rolled[b + 1]
            ).astype(jnp.bfloat16)
    spectra = jnp.dot(moved_rows[...], table_ref[...], preferred_element_type=jnp.float32)
    power = spectra * spectra
    smooth = jnp.dot(
        power, near_ref[...], precision=lax.Precision.HIGHEST, preferred_element_type=jnp.float32
    ) / count_ref[...]
    water_level = jnp.sum(power, axis=-1, keepdims=True) / NF
    rows_of = lax.broadcasted_iota(jnp.int32, spectra.shape, 0) % channels
    live = jnp.zeros(spectra.shape, jnp.float32)
    for c in range(channels):
        live = jnp.where(rows_of == c, live_ref[c].astype(jnp.float32), live)
    gain_of = live / jnp.sqrt(smooth + 0.1 * water_level + 1e-06)
    whitened = spectra * gain_of
    groups = len(out_refs)
    _, lanes_out = out_refs[0].shape
    width = 2 * LANES // (2 * groups)
    per_vreg = LANES // width
    lane = lax.broadcasted_iota(jnp.int32, (channels, LANES), 1)
    for d in range(groups):
        g = (place_ref[0] + d) % groups
        for v in range(lanes_out // LANES):
            gathered = jnp.zeros((channels, LANES), jnp.float32)
            for slot in range(per_vreg):
                w = v * per_vreg + slot
                piece = whitened[w * channels : (w + 1) * channels]
                piece = pltpu.roll(piece, (slot - g) * width % LANES, 1)
                inside = (lane >= slot * width) & (lane < (slot + 1) * width)
                gathered = jnp.where(inside, piece, gathered)
            out_refs[d][:, pl.ds(v * LANES, LANES)] = gathered.astype(out_refs[d].dtype)


def whiten(record_rows, starts, live_mask, groups, place):
    channels, _ = record_rows.shape
    windows = starts.shape[0]
    per_group = NF // groups
    lane_group, lane_part, lane_bin = np.unravel_index(np.arange(2 * NF), (groups, 2, per_group))
    lane_bin = lane_group * per_group + lane_bin
    table = jnp.asarray(spectral_table()[:, lane_part * NF + lane_bin])
    near = (np.abs(lane_bin[:, None] - lane_bin[None, :]) <= 4).astype(np.float32)
    count = (np.abs(np.arange(NF)[:, None] - lane_bin[None, :]) <= 4).sum(axis=0, keepdims=True).astype(np.float32)
    vmem = pl.BlockSpec(memory_space=pltpu.VMEM)
    smem = pl.BlockSpec(memory_space=pltpu.SMEM)
    return pl.pallas_call(
        whiten_kernel,
        out_shape=[jax.ShapeDtypeStruct((channels, windows * 2 * per_group), jnp.bfloat16)] * groups,
        in_specs=[smem, smem, smem, pl.BlockSpec(memory_space=pl.ANY), vmem, vmem, vmem],
        out_specs=[vmem] * groups,
        scratch_shapes=[
            pltpu.VMEM((windows, channels, NT + LANES), jnp.bfloat16),
            pltpu.VMEM((windows * channels, NT), jnp.bfloat16),
            pltpu.SemaphoreType.DMA((windows,)),
        ],
    )(starts, place.reshape(1), live_mask, record_rows, table, jnp.asarray(near), jnp.asarray(count))


def halo(mine, hops, fibre_count):
    if fibre_count % 2:
        columns = [mine]
        for step in range(1, hops + 1):
            pairs = [(i, i - step) for i in range(step, fibre_count)]
            columns.append(lax.ppermute(mine, "fibre", pairs))
        return jnp.concatenate(columns, axis=0)
    strides = min(-(-hops // 2), (fibre_count - 1) // 2)
    own = [mine]
    for step in range(1, strides + 1):
        pairs = [(i, i - 2 * step) for i in range(2 * step, fibre_count)]
        own.append(lax.ppermute(mine, "fibre", pairs))
    swapped = lax.ppermute(jnp.concatenate(own, axis=0), "fibre", [(i, i ^ 1) for i in range(fibre_count)])
    swapped = jnp.split(swapped, strides + 1, axis=0)
    even = [part for pair in zip(own, swapped) for part in pair]
    odd = [part for pair in zip(own, swapped[1:] + [jnp.zeros_like(mine)]) for part in pair]
    odd_side = lax.axis_index("fibre") % 2 == 1
    return jnp.where(odd_side, jnp.concatenate(odd, axis=0), jnp.concatenate(even, axis=0))


def shards(record, offsets, live_mask):
    seg_count = lax.axis_size("seg")
    fibre_count = lax.axis_size("fibre")
    windows_count = offsets.shape[1]
    block = record.shape[1]
    channels = block * fibre_count
    per_owner = BAND // seg_count
    bins_each = NF // seg_count
    live_offsets = min(BAND, channels - 1)
    live_owners = -(-live_offsets // per_owner)
    kept = live_owners * per_owner
    span = block + kept
    hops = min(-(-span // block) - 1, fibre_count - 1)
    me = lax.axis_index("seg")
    rows = seg_count * windows_count
    split = whiten(record[0], offsets[0], live_mask, seg_count, me.astype(jnp.int32))

    gathered = [split[0]]
    for step in range(1, seg_count):
        pairs = [(i, (i + step) % seg_count) for i in range(seg_count)]
        gathered.append(lax.ppermute(split[step], "seg", pairs))
    mine = jnp.concatenate(gathered, axis=1)

    columns = halo(mine, hops, fibre_count)[:span]
    if columns.shape[0] < span:
        columns = jnp.concatenate(
            [columns, jnp.zeros((span - columns.shape[0], columns.shape[1]), columns.dtype)], axis=0
        )
    right = columns.reshape(span, rows, 2, bins_each)
    own = right[:block]
    sign = jnp.asarray([1.0, -1.0], own.dtype)[None, None, :, None]
    turned = jnp.flip(own, axis=2) * sign
    cross = jnp.stack(
        [jnp.einsum("cspn,jspn->ncj", part, right, preferred_element_type=jnp.float32) for part in (own, turned)],
        axis=1,
    )
    band = jnp.stack([cross[:, :, c, c + 1 : c + 1 + kept] for c in range(block)])
    band = band.transpose(3, 0, 2, 1) * (1.0 / math.sqrt(seg_count * windows_count))
    band = band.reshape(kept, block * 2 * bins_each)
    if kept < BAND:
        band = jnp.concatenate([band, jnp.zeros((BAND - kept, band.shape[1]), band.dtype)], axis=0)
    band = band.reshape(seg_count, per_owner, band.shape[1])

    collected = [lax.dynamic_index_in_dim(band, me, 0, keepdims=False)]
    for step in range(1, seg_count):
        sent = lax.dynamic_index_in_dim(band, (me + step) % seg_count, 0, keepdims=False)
        pairs = [(i, (i + step) % seg_count) for i in range(seg_count) if (i + step) % seg_count < live_owners]
        if pairs:
            collected.append(lax.ppermute(sent, "seg", pairs))
        else:
            collected.append(jnp.zeros_like(sent))
    collected = jnp.stack(collected)
    turned_rows = jnp.concatenate([collected[:1], collected[1:][::-1]], axis=0)
    doubled = jnp.concatenate([turned_rows, turned_rows], axis=0)
    doubled = doubled.reshape(2 * seg_count, per_owner, block, 2, bins_each)
    start = (seg_count - me) % seg_count
    by_bins = [lax.dynamic_index_in_dim(doubled, start + b, 0, keepdims=False) for b in range(seg_count)]
    return jnp.stack(by_bins, axis=3).reshape(per_owner, block, 2 * NF)


def solution(mesh):
    placed = (P("seg", "fibre", None), P("seg", None), P("fibre"))
    return jax.shard_map(
        shards, mesh=mesh, in_specs=placed, out_specs=P("seg", "fibre", None), check_vma=False
    )
```

```python
import math

import jax
import jax.numpy as jnp
import ml_dtypes
import numpy as np
from jax import lax
from jax.experimental import pallas as pl
from jax.experimental.pallas import tpu as pltpu
from jax.sharding import PartitionSpec as P

NF = 64
NT = 3072
BIN0 = 32
BAND = 256
LANES = 128


def spectral_table():
    sample_idx = np.arange(NT, dtype=np.int64)
    bin_idx = BIN0 + np.arange(NF, dtype=np.int64)
    phase_int = sample_idx[:, None] * bin_idx[None, :] % NT
    angle_rad = np.float32(2.0 * math.pi / NT) * phase_int.astype(np.float32)
    angle = angle_rad.astype(np.float64)
    table = np.concatenate([np.cos(angle), -np.sin(angle)], axis=1)
    return table.astype(ml_dtypes.bfloat16)


def whiten_kernel(starts_ref, place_ref, live_ref, record_hbm, table_ref, near_ref, count_ref, *refs):
    *out_refs, chunks, moved_rows, sems = refs
    windows, channels, span = chunks.shape
    blocks = NT // LANES
    last = record_hbm.shape[1] - span
    shifts = []
    for w in range(windows):
        first = starts_ref[w]
        base = pl.multiple_of(jnp.minimum(first - first % LANES, last), LANES)
        pltpu.make_async_copy(record_hbm.at[:, pl.ds(base, span)], chunks.at[w], sems.at[w]).start()
        shifts.append(first - base)
    lane = lax.broadcasted_iota(jnp.int32, (channels, LANES), 1)
    for w in range(windows):
        pltpu.make_async_copy(record_hbm.at[:, pl.ds(0, span)], chunks.at[w], sems.at[w]).wait()
        shift = shifts[w]
        low = lane < LANES - shift
        rolled = [
            pltpu.roll(chunks[w, :, pl.ds(b * LANES, LANES)].astype(jnp.float32), (LANES - shift) % LANES, 1)
            for b in range(blocks + 1)
        ]
        for b in range(blocks):
            moved_rows[pl.ds(w * channels, channels), pl.ds(b * LANES, LANES)] = jnp.where(
                low, rolled[b], rolled[b + 1]
            ).astype(jnp.bfloat16)
    spectra = jnp.dot(moved_rows[...], table_ref[...], preferred_element_type=jnp.float32)
    power = spectra * spectra
    smooth = jnp.dot(
        power, near_ref[...], precision=lax.Precision.HIGHEST, preferred_element_type=jnp.float32
    ) / count_ref[...]
    water_level = jnp.sum(power, axis=-1, keepdims=True) / NF
    rows_of = lax.broadcasted_iota(jnp.int32, spectra.shape, 0) % channels
    live = jnp.zeros(spectra.shape, jnp.float32)
    for c in range(channels):
        live = jnp.where(rows_of == c, live_ref[c].astype(jnp.float32), live)
    gain_of = live / jnp.sqrt(smooth + 0.1 * water_level + 1e-06)
    whitened = spectra * gain_of
    groups = len(out_refs)
    _, lanes_out = out_refs[0].shape
    width = 2 * LANES // (2 * groups)
    per_vreg = LANES // width
    lane = lax.broadcasted_iota(jnp.int32, (channels, LANES), 1)
    for d in range(groups):
        g = (place_ref[0] + d) % groups
        for v in range(lanes_out // LANES):
            gathered = jnp.zeros((channels, LANES), jnp.float32)
            for slot in range(per_vreg):
                w = v * per_vreg + slot
                piece = whitened[w * channels : (w + 1) * channels]
                piece = pltpu.roll(piece, (slot - g) * width % LANES, 1)
                inside = (lane >= slot * width) & (lane < (slot + 1) * width)
                gathered = jnp.where(inside, piece, gathered)
            out_refs[d][:, pl.ds(v * LANES, LANES)] = gathered.astype(out_refs[d].dtype)


def whiten(record_rows, starts, live_mask, groups, place):
    channels, _ = record_rows.shape
    windows = starts.shape[0]
    per_group = NF // groups
    lane_group, lane_part, lane_bin = np.unravel_index(np.arange(2 * NF), (groups, 2, per_group))
    lane_bin = lane_group * per_group + lane_bin
    table = jnp.asarray(spectral_table()[:, lane_part * NF + lane_bin])
    near = (np.abs(lane_bin[:, None] - lane_bin[None, :]) <= 4).astype(np.float32)
    count = (np.abs(np.arange(NF)[:, None] - lane_bin[None, :]) <= 4).sum(axis=0, keepdims=True).astype(np.float32)
    vmem = pl.BlockSpec(memory_space=pltpu.VMEM)
    smem = pl.BlockSpec(memory_space=pltpu.SMEM)
    return pl.pallas_call(
        whiten_kernel,
        out_shape=[jax.ShapeDtypeStruct((channels, windows * 2 * per_group), jnp.bfloat16)] * groups,
        in_specs=[smem, smem, smem, pl.BlockSpec(memory_space=pl.ANY), vmem, vmem, vmem],
        out_specs=[vmem] * groups,
        scratch_shapes=[
            pltpu.VMEM((windows, channels, NT + LANES), jnp.bfloat16),
            pltpu.VMEM((windows * channels, NT), jnp.bfloat16),
            pltpu.SemaphoreType.DMA((windows,)),
        ],
    )(starts, place.reshape(1), live_mask, record_rows, table, jnp.asarray(near), jnp.asarray(count))


def halo(mine, hops, fibre_count):
    if fibre_count % 2:
        columns = [mine]
        for step in range(1, hops + 1):
            pairs = [(i, i - step) for i in range(step, fibre_count)]
            columns.append(lax.ppermute(mine, "fibre", pairs))
        return jnp.concatenate(columns, axis=0)
    strides = min(-(-hops // 2), (fibre_count - 1) // 2)
    own = [mine]
    for step in range(1, strides + 1):
        pairs = [(i, i - 2 * step) for i in range(2 * step, fibre_count)]
        own.append(lax.ppermute(mine, "fibre", pairs))
    swapped = lax.ppermute(jnp.concatenate(own, axis=0), "fibre", [(i, i ^ 1) for i in range(fibre_count)])
    swapped = jnp.split(swapped, strides + 1, axis=0)
    even = [part for pair in zip(own, swapped) for part in pair]
    odd = [part for pair in zip(own, swapped[1:] + [jnp.zeros_like(mine)]) for part in pair]
    odd_side = lax.axis_index("fibre") % 2 == 1
    return jnp.where(odd_side, jnp.concatenate(odd, axis=0), jnp.concatenate(even, axis=0))


def shards(record, offsets, live_mask):
    seg_count = lax.axis_size("seg")
    fibre_count = lax.axis_size("fibre")
    windows_count = offsets.shape[1]
    block = record.shape[1]
    channels = block * fibre_count
    per_owner = BAND // seg_count
    bins_each = NF // seg_count
    live_offsets = min(BAND, channels - 1)
    live_owners = -(-live_offsets // per_owner)
    kept = live_owners * per_owner
    span = block + kept
    hops = min(-(-span // block) - 1, fibre_count - 1)
    me = lax.axis_index("seg")
    rows = seg_count * windows_count
    split = whiten(record[0], offsets[0], live_mask, seg_count, me.astype(jnp.int32))

    gathered = [split[0]]
    for step in range(1, seg_count):
        pairs = [(i, (i + step) % seg_count) for i in range(seg_count)]
        gathered.append(lax.ppermute(split[step], "seg", pairs))
    mine = jnp.concatenate(gathered, axis=1)

    columns = halo(mine, hops, fibre_count)[:span]
    if columns.shape[0] < span:
        columns = jnp.concatenate(
            [columns, jnp.zeros((span - columns.shape[0], columns.shape[1]), columns.dtype)], axis=0
        )
    right = columns.reshape(span, rows, 2, bins_each)
    own = right[:block]
    sign = jnp.asarray([1.0, -1.0], own.dtype)[None, None, :, None]
    turned = jnp.flip(own, axis=2) * sign
    left = jnp.stack([own, turned])
    cross = jnp.einsum("ocspn,jspn->nocj", left, right, preferred_element_type=jnp.float32)
    band = jnp.stack([cross[:, :, c, c + 1 : c + 1 + kept] for c in range(block)])
    band = band.transpose(3, 0, 2, 1) * (1.0 / math.sqrt(seg_count * windows_count))
    band = band.reshape(kept, block * 2 * bins_each)
    if kept < BAND:
        band = jnp.concatenate([band, jnp.zeros((BAND - kept, band.shape[1]), band.dtype)], axis=0)
    band = band.reshape(seg_count, per_owner, band.shape[1])

    collected = [lax.dynamic_index_in_dim(band, me, 0, keepdims=False)]
    for step in range(1, seg_count):
        sent = lax.dynamic_index_in_dim(band, (me + step) % seg_count, 0, keepdims=False)
        pairs = [(i, (i + step) % seg_count) for i in range(seg_count) if (i + step) % seg_count < live_owners]
        if pairs:
            collected.append(lax.ppermute(sent, "seg", pairs))
        else:
            collected.append(jnp.zeros_like(sent))
    collected = jnp.stack(collected)
    turned_rows = jnp.concatenate([collected[:1], collected[1:][::-1]], axis=0)
    doubled = jnp.concatenate([turned_rows, turned_rows], axis=0)
    doubled = doubled.reshape(2 * seg_count, per_owner, block, 2, bins_each)
    start = (seg_count - me) % seg_count
    by_bins = [lax.dynamic_index_in_dim(doubled, start + b, 0, keepdims=False) for b in range(seg_count)]
    return jnp.concatenate([part[:, :, o] for o in range(2) for part in by_bins], axis=-1)


def solution(mesh):
    placed = (P("seg", "fibre", None), P("seg", None), P("fibre"))
    return jax.shard_map(
        shards, mesh=mesh, in_specs=placed, out_specs=P("seg", "fibre", None), check_vma=False
    )
```

```python
import math

import jax
import jax.numpy as jnp
import ml_dtypes
import numpy as np
from jax import lax
from jax.experimental import pallas as pl
from jax.experimental.pallas import tpu as pltpu
from jax.sharding import PartitionSpec as P

NF = 64
NT = 3072
BIN0 = 32
BAND = 256
LANES = 128


def spectral_table():
    sample_idx = np.arange(NT, dtype=np.int64)
    bin_idx = BIN0 + np.arange(NF, dtype=np.int64)
    phase_int = sample_idx[:, None] * bin_idx[None, :] % NT
    angle_rad = np.float32(2.0 * math.pi / NT) * phase_int.astype(np.float32)
    angle = angle_rad.astype(np.float64)
    table = np.concatenate([np.cos(angle), -np.sin(angle)], axis=1)
    return table.astype(ml_dtypes.bfloat16)


def whiten_kernel(starts_ref, place_ref, live_ref, record_hbm, table_ref, near_ref, count_ref, *refs):
    *out_refs, chunks, moved_rows, sems = refs
    windows, channels, span = chunks.shape
    blocks = NT // LANES
    last = record_hbm.shape[1] - span
    shifts = []
    for w in range(windows):
        first = starts_ref[w]
        base = pl.multiple_of(jnp.minimum(first - first % LANES, last), LANES)
        pltpu.make_async_copy(record_hbm.at[:, pl.ds(base, span)], chunks.at[w], sems.at[w]).start()
        shifts.append(first - base)
    lane = lax.broadcasted_iota(jnp.int32, (channels, LANES), 1)
    for w in range(windows):
        pltpu.make_async_copy(record_hbm.at[:, pl.ds(0, span)], chunks.at[w], sems.at[w]).wait()
        shift = shifts[w]
        low = lane < LANES - shift
        rolled = [
            pltpu.roll(chunks[w, :, pl.ds(b * LANES, LANES)].astype(jnp.float32), (LANES - shift) % LANES, 1)
            for b in range(blocks + 1)
        ]
        for b in range(blocks):
            moved_rows[pl.ds(w * channels, channels), pl.ds(b * LANES, LANES)] = jnp.where(
                low, rolled[b], rolled[b + 1]
            ).astype(jnp.bfloat16)
    spectra = jnp.dot(moved_rows[...], table_ref[...], preferred_element_type=jnp.float32)
    power = spectra * spectra
    smooth = jnp.dot(
        power, near_ref[...], precision=lax.Precision.HIGHEST, preferred_element_type=jnp.float32
    ) / count_ref[...]
    water_level = jnp.sum(power, axis=-1, keepdims=True) / NF
    rows_of = lax.broadcasted_iota(jnp.int32, spectra.shape, 0) % channels
    live = jnp.zeros(spectra.shape, jnp.float32)
    for c in range(channels):
        live = jnp.where(rows_of == c, live_ref[c].astype(jnp.float32), live)
    gain_of = live / jnp.sqrt(smooth + 0.1 * water_level + 1e-06)
    whitened = spectra * gain_of
    groups = len(out_refs)
    _, lanes_out = out_refs[0].shape
    width = 2 * LANES // (2 * groups)
    per_vreg = LANES // width
    lane = lax.broadcasted_iota(jnp.int32, (channels, LANES), 1)
    for d in range(groups):
        g = (place_ref[0] + d) % groups
        for v in range(lanes_out // LANES):
            gathered = jnp.zeros((channels, LANES), jnp.float32)
            for slot in range(per_vreg):
                w = v * per_vreg + slot
                piece = whitened[w * channels : (w + 1) * channels]
                piece = pltpu.roll(piece, (slot - g) * width % LANES, 1)
                inside = (lane >= slot * width) & (lane < (slot + 1) * width)
                gathered = jnp.where(inside, piece, gathered)
            out_refs[d][:, pl.ds(v * LANES, LANES)] = gathered.astype(out_refs[d].dtype)


def whiten(record_rows, starts, live_mask, groups, place):
    channels, _ = record_rows.shape
    windows = starts.shape[0]
    per_group = NF // groups
    lane_group, lane_part, lane_bin = np.unravel_index(np.arange(2 * NF), (groups, 2, per_group))
    lane_bin = lane_group * per_group + lane_bin
    table = jnp.asarray(spectral_table()[:, lane_part * NF + lane_bin])
    near = (np.abs(lane_bin[:, None] - lane_bin[None, :]) <= 4).astype(np.float32)
    count = (np.abs(np.arange(NF)[:, None] - lane_bin[None, :]) <= 4).sum(axis=0, keepdims=True).astype(np.float32)
    vmem = pl.BlockSpec(memory_space=pltpu.VMEM)
    smem = pl.BlockSpec(memory_space=pltpu.SMEM)
    return pl.pallas_call(
        whiten_kernel,
        out_shape=[jax.ShapeDtypeStruct((channels, windows * 2 * per_group), jnp.bfloat16)] * groups,
        in_specs=[smem, smem, smem, pl.BlockSpec(memory_space=pl.ANY), vmem, vmem, vmem],
        out_specs=[vmem] * groups,
        scratch_shapes=[
            pltpu.VMEM((windows, channels, NT + LANES), jnp.bfloat16),
            pltpu.VMEM((windows * channels, NT), jnp.bfloat16),
            pltpu.SemaphoreType.DMA((windows,)),
        ],
    )(starts, place.reshape(1), live_mask, record_rows, table, jnp.asarray(near), jnp.asarray(count))


def halo(mine, hops, fibre_count):
    if fibre_count % 2:
        columns = [mine]
        for step in range(1, hops + 1):
            pairs = [(i, i - step) for i in range(step, fibre_count)]
            columns.append(lax.ppermute(mine, "fibre", pairs))
        return jnp.concatenate(columns, axis=0)
    strides = min(-(-hops // 2), (fibre_count - 1) // 2)
    own = [mine]
    for step in range(1, strides + 1):
        pairs = [(i, i - 2 * step) for i in range(2 * step, fibre_count)]
        own.append(lax.ppermute(mine, "fibre", pairs))
    swapped = lax.ppermute(jnp.concatenate(own, axis=0), "fibre", [(i, i ^ 1) for i in range(fibre_count)])
    swapped = jnp.split(swapped, strides + 1, axis=0)
    even = [part for pair in zip(own, swapped) for part in pair]
    odd = [part for pair in zip(own, swapped[1:] + [jnp.zeros_like(mine)]) for part in pair]
    odd_side = lax.axis_index("fibre") % 2 == 1
    return jnp.where(odd_side, jnp.concatenate(odd, axis=0), jnp.concatenate(even, axis=0))


def shards(record, offsets, live_mask):
    seg_count = lax.axis_size("seg")
    fibre_count = lax.axis_size("fibre")
    windows_count = offsets.shape[1]
    block = record.shape[1]
    channels = block * fibre_count
    per_owner = BAND // seg_count
    bins_each = NF // seg_count
    live_offsets = min(BAND, channels - 1)
    live_owners = -(-live_offsets // per_owner)
    kept = live_owners * per_owner
    span = block + kept
    hops = min(-(-span // block) - 1, fibre_count - 1)
    me = lax.axis_index("seg")
    rows = seg_count * windows_count
    split = whiten(record[0], offsets[0], live_mask, seg_count, me.astype(jnp.int32))

    gathered = [split[0]]
    for step in range(1, seg_count):
        pairs = [(i, (i + step) % seg_count) for i in range(seg_count)]
        gathered.append(lax.ppermute(split[step], "seg", pairs))
    mine = jnp.concatenate(gathered, axis=1)

    columns = halo(mine, hops, fibre_count)[:span]
    if columns.shape[0] < span:
        columns = jnp.concatenate(
            [columns, jnp.zeros((span - columns.shape[0], columns.shape[1]), columns.dtype)], axis=0
        )
    right = columns.reshape(span, rows, 2, bins_each)
    own = right[:block]
    sign = jnp.asarray([1.0, -1.0], own.dtype)[None, None, :, None]
    turned = jnp.flip(own, axis=2) * sign
    left = jnp.stack([own, turned])
    cross = jnp.einsum("ocspn,jspn->nocj", left, right, preferred_element_type=jnp.float32)
    band = jnp.stack([cross[:, :, c, c + 1 : c + 1 + kept] for c in range(block)])
    band = band.transpose(3, 0, 2, 1) * (1.0 / math.sqrt(seg_count * windows_count))
    band = band.reshape(kept, block * 2 * bins_each)
    if kept < BAND:
        band = jnp.concatenate([band, jnp.zeros((BAND - kept, band.shape[1]), band.dtype)], axis=0)
    band = band.reshape(seg_count, per_owner, band.shape[1])

    collected = [lax.dynamic_index_in_dim(band, me, 0, keepdims=False)]
    for step in range(1, seg_count):
        sent = lax.dynamic_index_in_dim(band, (me + step) % seg_count, 0, keepdims=False)
        pairs = [(i, (i + step) % seg_count) for i in range(seg_count) if (i + step) % seg_count < live_owners]
        if pairs:
            collected.append(lax.ppermute(sent, "seg", pairs))
        else:
            collected.append(jnp.zeros_like(sent))
    collected = jnp.stack(collected)
    collected = collected.reshape(seg_count, per_owner, block, 2, bins_each)
    by_bins = [lax.dynamic_index_in_dim(collected, (me - b) % seg_count, 0, keepdims=False) for b in range(seg_count)]
    return jnp.stack(by_bins, axis=3).reshape(per_owner, block, 2 * NF)


def solution(mesh):
    placed = (P("seg", "fibre", None), P("seg", None), P("fibre"))
    return jax.shard_map(
        shards, mesh=mesh, in_specs=placed, out_specs=P("seg", "fibre", None), check_vma=False
    )
```

```python
import math

import jax
import jax.numpy as jnp
import ml_dtypes
import numpy as np
from jax import lax
from jax.experimental import pallas as pl
from jax.experimental.pallas import tpu as pltpu
from jax.sharding import PartitionSpec as P

NF = 64
NT = 3072
BIN0 = 32
BAND = 256
LANES = 128


def spectral_table():
    sample_idx = np.arange(NT, dtype=np.int64)
    bin_idx = BIN0 + np.arange(NF, dtype=np.int64)
    phase_int = sample_idx[:, None] * bin_idx[None, :] % NT
    angle_rad = np.float32(2.0 * math.pi / NT) * phase_int.astype(np.float32)
    angle = angle_rad.astype(np.float64)
    table = np.concatenate([np.cos(angle), -np.sin(angle)], axis=1)
    return table.astype(ml_dtypes.bfloat16)


def whiten_kernel(starts_ref, place_ref, live_ref, record_hbm, table_ref, near_ref, count_ref, *refs):
    *out_refs, chunks, moved_rows, sems = refs
    windows, channels, span = chunks.shape
    blocks = NT // LANES
    last = record_hbm.shape[1] - span
    shifts = []
    for w in range(windows):
        first = starts_ref[w]
        base = pl.multiple_of(jnp.minimum(first - first % LANES, last), LANES)
        pltpu.make_async_copy(record_hbm.at[:, pl.ds(base, span)], chunks.at[w], sems.at[w]).start()
        shifts.append(first - base)
    lane = lax.broadcasted_iota(jnp.int32, (channels, LANES), 1)
    for w in range(windows):
        pltpu.make_async_copy(record_hbm.at[:, pl.ds(0, span)], chunks.at[w], sems.at[w]).wait()
        shift = shifts[w]
        low = lane < LANES - shift
        rolled = [
            pltpu.roll(chunks[w, :, pl.ds(b * LANES, LANES)].astype(jnp.float32), (LANES - shift) % LANES, 1)
            for b in range(blocks + 1)
        ]
        for b in range(blocks):
            moved_rows[pl.ds(w * channels, channels), pl.ds(b * LANES, LANES)] = jnp.where(
                low, rolled[b], rolled[b + 1]
            ).astype(jnp.bfloat16)
    spectra = jnp.dot(moved_rows[...], table_ref[...], preferred_element_type=jnp.float32)
    power = spectra * spectra
    smooth = jnp.dot(
        power, near_ref[...], precision=lax.Precision.HIGHEST, preferred_element_type=jnp.float32
    ) / count_ref[...]
    water_level = jnp.sum(power, axis=-1, keepdims=True) / NF
    rows_of = lax.broadcasted_iota(jnp.int32, spectra.shape, 0) % channels
    live = jnp.zeros(spectra.shape, jnp.float32)
    for c in range(channels):
        live = jnp.where(rows_of == c, live_ref[c].astype(jnp.float32), live)
    gain_of = live / jnp.sqrt(smooth + 0.1 * water_level + 1e-06)
    whitened = spectra * gain_of
    groups = len(out_refs)
    _, lanes_out = out_refs[0].shape
    width = 2 * LANES // (2 * groups)
    per_vreg = LANES // width
    lane = lax.broadcasted_iota(jnp.int32, (channels, LANES), 1)
    for d in range(groups):
        g = (place_ref[0] + d) % groups
        for v in range(lanes_out // LANES):
            gathered = jnp.zeros((channels, LANES), jnp.float32)
            for slot in range(per_vreg):
                w = v * per_vreg + slot
                piece = whitened[w * channels : (w + 1) * channels]
                piece = pltpu.roll(piece, (slot - g) * width % LANES, 1)
                inside = (lane >= slot * width) & (lane < (slot + 1) * width)
                gathered = jnp.where(inside, piece, gathered)
            out_refs[d][:, pl.ds(v * LANES, LANES)] = gathered.astype(out_refs[d].dtype)


def whiten(record_rows, starts, live_mask, groups, place):
    channels, _ = record_rows.shape
    windows = starts.shape[0]
    per_group = NF // groups
    lane_group, lane_part, lane_bin = np.unravel_index(np.arange(2 * NF), (groups, 2, per_group))
    lane_bin = lane_group * per_group + lane_bin
    table = jnp.asarray(spectral_table()[:, lane_part * NF + lane_bin])
    near = (np.abs(lane_bin[:, None] - lane_bin[None, :]) <= 4).astype(np.float32)
    count = (np.abs(np.arange(NF)[:, None] - lane_bin[None, :]) <= 4).sum(axis=0, keepdims=True).astype(np.float32)
    vmem = pl.BlockSpec(memory_space=pltpu.VMEM)
    smem = pl.BlockSpec(memory_space=pltpu.SMEM)
    return pl.pallas_call(
        whiten_kernel,
        out_shape=[jax.ShapeDtypeStruct((channels, windows * 2 * per_group), jnp.bfloat16)] * groups,
        in_specs=[smem, smem, smem, pl.BlockSpec(memory_space=pl.ANY), vmem, vmem, vmem],
        out_specs=[vmem] * groups,
        scratch_shapes=[
            pltpu.VMEM((windows, channels, NT + LANES), jnp.bfloat16),
            pltpu.VMEM((windows * channels, NT), jnp.bfloat16),
            pltpu.SemaphoreType.DMA((windows,)),
        ],
    )(starts, place.reshape(1), live_mask, record_rows, table, jnp.asarray(near), jnp.asarray(count))


def halo(mine, hops, fibre_count):
    if fibre_count % 2:
        columns = [mine]
        for step in range(1, hops + 1):
            pairs = [(i, i - step) for i in range(step, fibre_count)]
            columns.append(lax.ppermute(mine, "fibre", pairs))
        return jnp.concatenate(columns, axis=0)
    strides = min(-(-hops // 2), (fibre_count - 1) // 2)
    own = [mine]
    for step in range(1, strides + 1):
        pairs = [(i, i - 2 * step) for i in range(2 * step, fibre_count)]
        own.append(lax.ppermute(mine, "fibre", pairs))
    even_side = lax.axis_index("fibre") % 2 == 0
    sent = jnp.where(
        even_side,
        jnp.concatenate(own[1:] + [jnp.zeros_like(mine)], axis=0),
        jnp.concatenate(own, axis=0),
    )
    swapped = lax.ppermute(sent, "fibre", [(i, i ^ 1) for i in range(fibre_count)])
    swapped = jnp.split(swapped, strides + 1, axis=0)
    return jnp.concatenate([part for pair in zip(own, swapped) for part in pair], axis=0)


def shards(record, offsets, live_mask):
    seg_count = lax.axis_size("seg")
    fibre_count = lax.axis_size("fibre")
    windows_count = offsets.shape[1]
    block = record.shape[1]
    channels = block * fibre_count
    per_owner = BAND // seg_count
    bins_each = NF // seg_count
    live_offsets = min(BAND, channels - 1)
    live_owners = -(-live_offsets // per_owner)
    kept = live_owners * per_owner
    span = block + kept
    hops = min(-(-span // block) - 1, fibre_count - 1)
    me = lax.axis_index("seg")
    rows = seg_count * windows_count
    split = whiten(record[0], offsets[0], live_mask, seg_count, me.astype(jnp.int32))

    gathered = [split[0]]
    for step in range(1, seg_count):
        pairs = [(i, (i + step) % seg_count) for i in range(seg_count)]
        gathered.append(lax.ppermute(split[step], "seg", pairs))
    mine = jnp.concatenate(gathered, axis=1)

    columns = halo(mine, hops, fibre_count)[:span]
    if columns.shape[0] < span:
        columns = jnp.concatenate(
            [columns, jnp.zeros((span - columns.shape[0], columns.shape[1]), columns.dtype)], axis=0
        )
    right = columns.reshape(span, rows, 2, bins_each)
    own = right[:block]
    sign = jnp.asarray([1.0, -1.0], own.dtype)[None, None, :, None]
    turned = jnp.flip(own, axis=2) * sign
    left = jnp.stack([own, turned])
    cross = jnp.einsum("ocspn,jspn->nocj", left, right, preferred_element_type=jnp.float32)
    band = jnp.stack([cross[:, :, c, c + 1 : c + 1 + kept] for c in range(block)])
    band = band.transpose(3, 0, 2, 1) * (1.0 / math.sqrt(seg_count * windows_count))
    band = band.reshape(kept, block * 2 * bins_each)
    if kept < BAND:
        band = jnp.concatenate([band, jnp.zeros((BAND - kept, band.shape[1]), band.dtype)], axis=0)
    band = band.reshape(seg_count, per_owner, band.shape[1])

    collected = [lax.dynamic_index_in_dim(band, me, 0, keepdims=False)]
    for step in range(1, seg_count):
        sent = lax.dynamic_index_in_dim(band, (me + step) % seg_count, 0, keepdims=False)
        pairs = [(i, (i + step) % seg_count) for i in range(seg_count) if (i + step) % seg_count < live_owners]
        if pairs:
            collected.append(lax.ppermute(sent, "seg", pairs))
        else:
            collected.append(jnp.zeros_like(sent))
    collected = jnp.stack(collected)
    turned_rows = jnp.concatenate([collected[:1], collected[1:][::-1]], axis=0)
    doubled = jnp.concatenate([turned_rows, turned_rows], axis=0)
    doubled = doubled.reshape(2 * seg_count, per_owner, block, 2, bins_each)
    start = (seg_count - me) % seg_count
    by_bins = [lax.dynamic_index_in_dim(doubled, start + b, 0, keepdims=False) for b in range(seg_count)]
    return jnp.stack(by_bins, axis=3).reshape(per_owner, block, 2 * NF)


def solution(mesh):
    placed = (P("seg", "fibre", None), P("seg", None), P("fibre"))
    return jax.shard_map(
        shards, mesh=mesh, in_specs=placed, out_specs=P("seg", "fibre", None), check_vma=False
    )
```

```python
import math

import jax
import jax.numpy as jnp
import ml_dtypes
import numpy as np
from jax import lax
from jax.experimental import pallas as pl
from jax.experimental.pallas import tpu as pltpu
from jax.sharding import PartitionSpec as P

NF = 64
NT = 3072
BIN0 = 32
BAND = 256
LANES = 128


def spectral_table():
    sample_idx = np.arange(NT, dtype=np.int64)
    bin_idx = BIN0 + np.arange(NF, dtype=np.int64)
    phase_int = sample_idx[:, None] * bin_idx[None, :] % NT
    angle_rad = np.float32(2.0 * math.pi / NT) * phase_int.astype(np.float32)
    angle = angle_rad.astype(np.float64)
    table = np.concatenate([np.cos(angle), -np.sin(angle)], axis=1)
    return table.astype(ml_dtypes.bfloat16)


def whiten_kernel(starts_ref, place_ref, live_ref, record_hbm, table_ref, near_ref, count_ref, *refs):
    *out_refs, chunks, moved_rows, sems = refs
    windows, channels, span = chunks.shape
    blocks = NT // LANES
    last = record_hbm.shape[1] - span
    shifts = []
    for w in range(windows):
        first = starts_ref[w]
        base = pl.multiple_of(jnp.minimum(first - first % LANES, last), LANES)
        pltpu.make_async_copy(record_hbm.at[:, pl.ds(base, span)], chunks.at[w], sems.at[w]).start()
        shifts.append(first - base)
    lane = lax.broadcasted_iota(jnp.int32, (channels, LANES), 1)
    for w in range(windows):
        pltpu.make_async_copy(record_hbm.at[:, pl.ds(0, span)], chunks.at[w], sems.at[w]).wait()
        shift = shifts[w]
        low = lane < LANES - shift
        rolled = [
            pltpu.roll(chunks[w, :, pl.ds(b * LANES, LANES)].astype(jnp.float32), (LANES - shift) % LANES, 1)
            for b in range(blocks + 1)
        ]
        for b in range(blocks):
            moved_rows[pl.ds(w * channels, channels), pl.ds(b * LANES, LANES)] = jnp.where(
                low, rolled[b], rolled[b + 1]
            ).astype(jnp.bfloat16)
    spectra = jnp.dot(moved_rows[...], table_ref[...], preferred_element_type=jnp.float32)
    power = spectra * spectra
    smooth = jnp.dot(
        power, near_ref[...], precision=lax.Precision.HIGHEST, preferred_element_type=jnp.float32
    ) / count_ref[...]
    water_level = jnp.sum(power, axis=-1, keepdims=True) / NF
    rows_of = lax.broadcasted_iota(jnp.int32, spectra.shape, 0) % channels
    live = jnp.zeros(spectra.shape, jnp.float32)
    for c in range(channels):
        live = jnp.where(rows_of == c, live_ref[c].astype(jnp.float32), live)
    gain_of = live / jnp.sqrt(smooth + 0.1 * water_level + 1e-06)
    whitened = spectra * gain_of
    groups = len(out_refs)
    _, lanes_out = out_refs[0].shape
    width = 2 * LANES // (2 * groups)
    per_vreg = LANES // width
    lane = lax.broadcasted_iota(jnp.int32, (channels, LANES), 1)
    for d in range(groups):
        g = place_ref[0] ^ d if groups & (groups - 1) == 0 else (place_ref[0] + d) % groups
        for v in range(lanes_out // LANES):
            gathered = jnp.zeros((channels, LANES), jnp.float32)
            for slot in range(per_vreg):
                w = v * per_vreg + slot
                piece = whitened[w * channels : (w + 1) * channels]
                piece = pltpu.roll(piece, (slot - g) * width % LANES, 1)
                inside = (lane >= slot * width) & (lane < (slot + 1) * width)
                gathered = jnp.where(inside, piece, gathered)
            out_refs[d][:, pl.ds(v * LANES, LANES)] = gathered.astype(out_refs[d].dtype)


def whiten(record_rows, starts, live_mask, groups, place):
    channels, _ = record_rows.shape
    windows = starts.shape[0]
    per_group = NF // groups
    lane_group, lane_part, lane_bin = np.unravel_index(np.arange(2 * NF), (groups, 2, per_group))
    lane_bin = lane_group * per_group + lane_bin
    table = jnp.asarray(spectral_table()[:, lane_part * NF + lane_bin])
    near = (np.abs(lane_bin[:, None] - lane_bin[None, :]) <= 4).astype(np.float32)
    count = (np.abs(np.arange(NF)[:, None] - lane_bin[None, :]) <= 4).sum(axis=0, keepdims=True).astype(np.float32)
    vmem = pl.BlockSpec(memory_space=pltpu.VMEM)
    smem = pl.BlockSpec(memory_space=pltpu.SMEM)
    return pl.pallas_call(
        whiten_kernel,
        out_shape=[jax.ShapeDtypeStruct((channels, windows * 2 * per_group), jnp.bfloat16)] * groups,
        in_specs=[smem, smem, smem, pl.BlockSpec(memory_space=pl.ANY), vmem, vmem, vmem],
        out_specs=[vmem] * groups,
        scratch_shapes=[
            pltpu.VMEM((windows, channels, NT + LANES), jnp.bfloat16),
            pltpu.VMEM((windows * channels, NT), jnp.bfloat16),
            pltpu.SemaphoreType.DMA((windows,)),
        ],
    )(starts, place.reshape(1), live_mask, record_rows, table, jnp.asarray(near), jnp.asarray(count))


def halo(mine, hops, fibre_count):
    if fibre_count % 2:
        columns = [mine]
        for step in range(1, hops + 1):
            pairs = [(i, i - step) for i in range(step, fibre_count)]
            columns.append(lax.ppermute(mine, "fibre", pairs))
        return jnp.concatenate(columns, axis=0)
    strides = min(-(-hops // 2), (fibre_count - 1) // 2)
    own = [mine]
    for step in range(1, strides + 1):
        pairs = [(i, i - 2 * step) for i in range(2 * step, fibre_count)]
        own.append(lax.ppermute(mine, "fibre", pairs))
    even_side = lax.axis_index("fibre") % 2 == 0
    sent = jnp.where(
        even_side,
        jnp.concatenate(own[1:] + [jnp.zeros_like(mine)], axis=0),
        jnp.concatenate(own, axis=0),
    )
    swapped = lax.ppermute(sent, "fibre", [(i, i ^ 1) for i in range(fibre_count)])
    swapped = jnp.split(swapped, strides + 1, axis=0)
    return jnp.concatenate([part for pair in zip(own, swapped) for part in pair], axis=0)


def shards(record, offsets, live_mask):
    seg_count = lax.axis_size("seg")
    fibre_count = lax.axis_size("fibre")
    windows_count = offsets.shape[1]
    block = record.shape[1]
    channels = block * fibre_count
    per_owner = BAND // seg_count
    bins_each = NF // seg_count
    live_offsets = min(BAND, channels - 1)
    live_owners = -(-live_offsets // per_owner)
    kept = live_owners * per_owner
    span = block + kept
    hops = min(-(-span // block) - 1, fibre_count - 1)
    me = lax.axis_index("seg")
    rows = seg_count * windows_count
    split = whiten(record[0], offsets[0], live_mask, seg_count, me.astype(jnp.int32))

    gathered = [split[0]]
    for step in range(1, seg_count):
        if seg_count & (seg_count - 1) == 0:
            pairs = [(i, i ^ step) for i in range(seg_count)]
        else:
            pairs = [(i, (i + step) % seg_count) for i in range(seg_count)]
        gathered.append(lax.ppermute(split[step], "seg", pairs))
    mine = jnp.concatenate(gathered, axis=1)

    columns = halo(mine, hops, fibre_count)[:span]
    if columns.shape[0] < span:
        columns = jnp.concatenate(
            [columns, jnp.zeros((span - columns.shape[0], columns.shape[1]), columns.dtype)], axis=0
        )
    right = columns.reshape(span, rows, 2, bins_each)
    own = right[:block]
    sign = jnp.asarray([1.0, -1.0], own.dtype)[None, None, :, None]
    turned = jnp.flip(own, axis=2) * sign
    left = jnp.stack([own, turned])
    cross = jnp.einsum("ocspn,jspn->nocj", left, right, preferred_element_type=jnp.float32)
    band = jnp.stack([cross[:, :, c, c + 1 : c + 1 + kept] for c in range(block)])
    band = band.transpose(3, 0, 2, 1) * (1.0 / math.sqrt(seg_count * windows_count))
    band = band.reshape(kept, block * 2 * bins_each)
    if kept < BAND:
        band = jnp.concatenate([band, jnp.zeros((BAND - kept, band.shape[1]), band.dtype)], axis=0)
    band = band.reshape(seg_count, per_owner, band.shape[1])

    collected = [lax.dynamic_index_in_dim(band, me, 0, keepdims=False)]
    for step in range(1, seg_count):
        sent = lax.dynamic_index_in_dim(band, (me + step) % seg_count, 0, keepdims=False)
        pairs = [(i, (i + step) % seg_count) for i in range(seg_count) if (i + step) % seg_count < live_owners]
        if pairs:
            collected.append(lax.ppermute(sent, "seg", pairs))
        else:
            collected.append(jnp.zeros_like(sent))
    collected = jnp.stack(collected)
    turned_rows = jnp.concatenate([collected[:1], collected[1:][::-1]], axis=0)
    doubled = jnp.concatenate([turned_rows, turned_rows], axis=0)
    doubled = doubled.reshape(2 * seg_count, per_owner, block, 2, bins_each)
    start = (seg_count - me) % seg_count
    by_bins = [lax.dynamic_index_in_dim(doubled, start + b, 0, keepdims=False) for b in range(seg_count)]
    return jnp.stack(by_bins, axis=3).reshape(per_owner, block, 2 * NF)


def solution(mesh):
    placed = (P("seg", "fibre", None), P("seg", None), P("fibre"))
    return jax.shard_map(
        shards, mesh=mesh, in_specs=placed, out_specs=P("seg", "fibre", None), check_vma=False
    )
```
